32 devices in a mesh: seq: 8 (over z, x), ch: 4 (over y, core).
Axes of the slice: x: 2, y: 2, z: 4, core: 2. Of those that a mesh axis runs over, the one named last changes fastest.
Arguments:
- xin: bfloat16 [8192, 16384], P('seq', 'ch'), may hold values from -6 to 6
- gate_in: bfloat16 [8192, 16384], P('seq', 'ch'), may hold values from -6 to 6
- bc_proj: bfloat16 [8192, 256], P('seq', 'ch'), may hold values from -6 to 6
- dt_raw: float32 [8192, 128], P('seq', 'ch'), may hold values from -6 to 6
- dt_bias: float32 [128], P('ch'), may hold values from -1 to 1
- rate: float32 [128], P('ch'), may hold values from 6.1035156e-05 to 0.1
- skip_gain: float32 [128], P('ch'), may hold values from 0.5 to 2
- conv_x: bfloat16 [4, 16384], P(None, 'ch'), may hold values from -3 to 3
- conv_bc: bfloat16 [4, 256], P(None, 'ch'), may hold values from -3 to 3
- norm_gain: float32 [16384], P('ch'), may hold values from 0.5 to 1.5
- valid_blocks: int32 [8], P('seq'), may hold values from 1 to 8, 48 in all
Outputs:
- mixed: bfloat16 [8192, 16384], P('seq', 'ch')
The draws below stay inside these ranges and needn't reach their ends.
Inputs may be any that keep to these rules, and one draw needn't show every extreme that they name: valid_blocks sums to 48; some entry equals 8.
All inputs are finite; a program needn't handle non-finite values.
Results may differ from the reference program's by a relative error of at most 0.0034.
Values may be sent and summed in bfloat16 or wider, within the bound.
No kernel may reach another device: no remote copies, remote signals or barrier semaphores. Data moves between devices by JAX's collectives and lax.ppermute only.
A program may use at most 256 MiB of HBM per device.

```python
import math
import jax
import jax.numpy as jnp
import numpy as np
from jax import lax

HEADS = 128
HEAD_DIM = 128
STATE = 128
KW = 4
SEGMENT_LENGTH = 256
BLOCK = 128
BLOCKS_DEV = 8
INNER = 16384
PROMPT_CAPACITY = 8192
SHARDS = 8
N_SEQ = 8


def draw_dt_raw(key, part):
    sampler_seeds = jax.random.split(key, 5)
    group_rows = PROMPT_CAPACITY // SHARDS
    starting_shift = jnp.clip(jax.random.normal(sampler_seeds[0], (PROMPT_CAPACITY, HEADS), jnp.float32), -3.0, 3.0)
    faint_magnitude = -5.0 + jnp.clip(0.4 * jax.random.normal(sampler_seeds[1], (PROMPT_CAPACITY, HEADS), jnp.float32), -0.9, 0.9)
    first_quiet = jax.random.randint(sampler_seeds[2], (), 1, SHARDS - 5)
    group_ids = jnp.arange(SHARDS)
    random_quiet = jax.random.bernoulli(sampler_seeds[3], 0.3, (SHARDS,))
    forced = (group_ids >= first_quiet) & (group_ids < first_quiet + 5)
    quiet = jnp.where(group_ids == first_quiet - 1, False, forced | random_quiet)
    prompt_lines = jnp.arange(PROMPT_CAPACITY)
    line_faint_amplitude = quiet[prompt_lines // group_rows]
    spike_amplitude = jax.random.bernoulli(sampler_seeds[4], 0.15, (PROMPT_CAPACITY // SEGMENT_LENGTH,))
    line_spike_amplitude = spike_amplitude[prompt_lines // SEGMENT_LENGTH]
    strong_amplitude = jnp.clip(starting_shift + 3.0, -6.0, 6.0)
    payload_lines = jnp.where(line_faint_amplitude[:, None], faint_magnitude, jnp.where(line_spike_amplitude[:, None], strong_amplitude, starting_shift))
    return payload_lines.astype(jnp.float32)


def level_of(rng, extent, pieces, low, largest):
    loudness, own = 1.0, jax.random.fold_in(rng, 6)
    for axis_at, parts in pieces:
        steps = jnp.exp(jax.random.uniform(jax.random.fold_in(own, axis_at), (parts,), jnp.float32, low / len(pieces), largest / len(pieces)))
        loudness = loudness * jnp.repeat(steps, extent[axis_at] // parts).reshape([-1 if axis == axis_at else 1 for axis in range(len(extent))])
    return loudness


def length_profile(number_of, total, limit, skew):
    weights = [(1 << 20) // math.isqrt(standing ** skew) + 1 for standing in range(2, number_of + 1)]
    surplus, counts = total - limit - (number_of - 1), [1] * (number_of - 1)
    while surplus > 0:
        candidates = [i for i in range(number_of - 1) if counts[i] < limit]
        mass, left = sum([weights[i] for i in candidates]), surplus
        for i in candidates:
            more = min(limit - counts[i], max(1, left * weights[i] // mass), surplus)
            counts[i] = counts[i] + more
            surplus = surplus - more
    return np.array([limit] + counts)


def ragged_sizes(rng, number_of, total, bound, slope):
    if number_of == 2:
        one = jax.random.randint(rng, (), max(1, total - bound), min(bound, total - 1) + 1)
        return jnp.stack([one, total - one])
    tallies = jnp.asarray(length_profile(number_of, total, bound, slope), jnp.int32)
    pairs = (number_of - 1) // 2
    giver, receiver = tallies[1:1 + 2 * pairs:2], tallies[2:2 + 2 * pairs:2]
    slack = jnp.minimum(giver - 1, bound - receiver)
    passed = jax.random.randint(jax.random.fold_in(rng, 1), (pairs,), 0, 1 << 20) % (slack + 1)
    tallies = tallies.at[1:1 + 2 * pairs:2].set(giver - passed).at[2:2 + 2 * pairs:2].set(receiver + passed)
    return tallies[jax.random.permutation(jax.random.fold_in(rng, 2), number_of)]


def gaussian(key, shape, scale, limit, pieces=(), kind=jnp.bfloat16):
    result = jax.random.normal(key, shape, jnp.float32) * scale
    if len(pieces) > 0:
        result = level_of(key, shape, pieces, -0.22, 0.18) * result
    return jnp.clip(result, min=-limit, max=limit).astype(kind)


def setup_inputs(seed: int = 0) -> dict:
    key_of = jax.random.split(jax.random.key(seed), 12)
    return {
        "xin": gaussian(key_of[0], (PROMPT_CAPACITY, INNER), 1.0, 6.0, ((0, 8), (1, 4))),
        "gate_in": gaussian(key_of[1], (PROMPT_CAPACITY, INNER), 1.0, 6.0, ((0, 8), (1, 4))),
        "bc_proj": gaussian(key_of[2], (PROMPT_CAPACITY, 2 * STATE), 1.0, 6.0, ((0, 8), (1, 4))),
        "dt_raw": draw_dt_raw(jax.random.fold_in(key_of[11], 71), 0),
        "dt_bias": jnp.clip(jax.random.uniform(key_of[4], (HEADS,), jnp.float32, -1.0, 1.0) * level_of(key_of[4], (HEADS,), ((0, 4),), -0.4, 0.0), -1.0, 1.0),
        "rate": jnp.clip(jnp.exp(math.log(0.1) - 7.4014754 * jax.random.uniform(key_of[5], (HEADS,), jnp.float32) ** level_of(key_of[5], (HEADS,), ((0, 4),), -0.2, 0.2)), 6.103515625e-05, 0.1),
        "skip_gain": jnp.clip(0.5 + 1.5 * jax.random.uniform(key_of[6], (HEADS,), jnp.float32) ** level_of(key_of[6], (HEADS,), ((0, 4),), -0.2, 0.2), 0.5, 2.0),
        "conv_x": gaussian(key_of[7], (KW, INNER), KW ** -0.5, 3.0, ((1, 4),)),
        "conv_bc": gaussian(key_of[8], (KW, 2 * STATE), KW ** -0.5, 3.0, ((1, 4),)),
        "norm_gain": jnp.clip(1.0 + 0.1 * jax.random.normal(key_of[9], (INNER,), jnp.float32), 0.5, 1.5),
        "valid_blocks": ragged_sizes(key_of[10], SHARDS, (3 * BLOCKS_DEV // 4) * N_SEQ, BLOCKS_DEV, 2).astype(jnp.int32),
    }


def conv_silu(signal, tail_rows, weights):
    stacked = jnp.concatenate([tail_rows, signal], axis=0)
    kernel_taps = weights.shape[0]
    length = signal.shape[0]
    accum = jnp.zeros(signal.shape, jnp.float32)
    for offset in range(kernel_taps):
        accum = accum + weights[offset].astype(jnp.float32) * stacked[offset:offset + length].astype(jnp.float32)
    return jax.nn.silu(accum).astype(jnp.bfloat16)

def widen(value):
    return lax.optimization_barrier(value).astype(jnp.float32)

def reference(xin, gate_in, bc_proj, dt_raw, dt_bias, rate, skip_gain, conv_x, conv_bc, norm_gain, valid_blocks):
    row_count = BLOCK * BLOCKS_DEV
    span_count = row_count // SEGMENT_LENGTH
    x_blocks = xin.reshape(N_SEQ, row_count, INNER)
    z_blocks = gate_in.reshape(N_SEQ, row_count, INNER)
    bc_blocks = bc_proj.reshape(N_SEQ, row_count, 2 * STATE)
    dt_blocks = dt_raw.reshape(N_SEQ, row_count, HEADS)

    def per_group(running, inputs):
        state_in, tail_x, tail_bc = running
        x_grp, z_grp, bc_grp, dt_grp, count = inputs
        live_rows = count * BLOCK
        row_valid = (jnp.arange(row_count) < live_rows).astype(jnp.float32)
        xconv = conv_silu(x_grp, tail_x, conv_x)
        bconv = conv_silu(bc_grp, tail_bc, conv_bc)
        new_tail_x = lax.dynamic_slice_in_dim(x_grp, live_rows - (KW - 1), KW - 1, 0)
        new_tail_bc = lax.dynamic_slice_in_dim(bc_grp, live_rows - (KW - 1), KW - 1, 0)
        step_size = jax.nn.softplus(dt_grp + dt_bias[None, :]) * row_valid[:, None]
        xfour = widen(xconv).reshape(span_count, SEGMENT_LENGTH, HEADS, HEAD_DIM)
        bfull = widen(bconv)
        b_three = bfull[:, :STATE].reshape(span_count, SEGMENT_LENGTH, STATE)
        c_three = bfull[:, STATE:].reshape(span_count, SEGMENT_LENGTH, STATE)
        step_three = step_size.reshape(span_count, SEGMENT_LENGTH, HEADS)
        cumul = jnp.cumsum(-rate[None, None, :] * step_three, axis=1)
        scores = jnp.einsum('cqn,csn->cqs', c_three, b_three)
        cum_heads = jnp.transpose(cumul, (0, 2, 1))
        diff = cum_heads[:, :, :, None] - cum_heads[:, :, None, :]
        causal = jnp.arange(SEGMENT_LENGTH)[:, None] >= jnp.arange(SEGMENT_LENGTH)[None, :]
        decay = jnp.where(causal, jnp.exp(jnp.where(causal, diff, 0.0)), 0.0)
        weights = (scores[:, None] * decay * jnp.transpose(step_three, (0, 2, 1))[:, :, None, :]).astype(jnp.bfloat16)
        intra = jnp.einsum('chqs,cshp->cqhp', widen(weights), xfour)
        last_cum = cum_heads[:, :, -1]
        to_end = jnp.exp(last_cum[:, None, :] - cumul) * step_three
        x_weighted = (xfour * to_end[..., None]).astype(jnp.bfloat16)
        block_state = jnp.einsum('csn,cshp->chnp', b_three, widen(x_weighted))
        block_decay = jnp.exp(last_cum)
        state_list = []
        current = state_in
        for index in range(span_count):
            state_list.append(current)
            current = block_decay[index][:, None, None] * current + block_state[index]
        state_enter = jnp.stack(state_list, axis=0)
        inter = jnp.einsum('cqn,chnp->cqhp', c_three, state_enter, precision=lax.Precision.HIGHEST)
        inter = inter * jnp.exp(cumul)[..., None]
        y_full = intra + inter + skip_gain[None, None, :, None] * xfour
        y_full = y_full.reshape(row_count, INNER)
        gated = y_full * jax.nn.silu(z_grp.astype(jnp.float32))
        mean_sq = lax.optimization_barrier(jnp.sum(gated * gated, axis=1)) / INNER
        normed = gated * lax.rsqrt(mean_sq + 1e-05)[:, None] * norm_gain[None, :] * row_valid[:, None]
        return ((current, new_tail_x, new_tail_bc), normed.astype(jnp.bfloat16))
    start = (jnp.zeros((HEADS, STATE, HEAD_DIM), jnp.float32), jnp.zeros((KW - 1, INNER), jnp.bfloat16), jnp.zeros((KW - 1, 2 * STATE), jnp.bfloat16))
    unused, outputs = lax.scan(per_group, start, (x_blocks, z_blocks, bc_blocks, dt_blocks, valid_blocks))
    return outputs.reshape(PROMPT_CAPACITY, INNER)
```

```python
import jax
import jax.numpy as jnp
from jax import lax
from jax.sharding import PartitionSpec as P

SEGMENT_LENGTH = 256
BLOCK = 128
INNER = 16384


def passed_along(block, axis, distance):
    devices = range(lax.axis_size(axis))
    route = [(i - distance, i) for i in devices if i - distance in devices]
    return lax.ppermute(block, axis, route)


def prefix(part, axis, combine, identity):
    place = lax.axis_index(axis)
    gathered = jax.tree.map(lambda a: lax.all_gather(a, axis), part)
    state = jax.tree.map(lambda a, e: jnp.zeros_like(a) + jnp.asarray(e, a.dtype), part, identity)

    def one(turn, state):
        return combine(
            state, jax.tree.map(lambda a: lax.dynamic_index_in_dim(a, turn, 0, False), gathered)
        )

    return lax.fori_loop(0, place, one, state)


def scan_states(factor, state, axis):
    count = lax.axis_size(axis)
    heads, size, width = state.shape
    piece = size // count
    parts = state.reshape(heads, count, piece, width).transpose(1, 0, 2, 3)
    got = lax.all_to_all(parts, axis, 0, 0, tiled=True)
    decays = lax.all_gather(factor, axis)
    running = jnp.zeros((heads, piece, width), jnp.float32)
    entries = []
    for index in range(count):
        entries.append(running)
        running = decays[index][:, None, None] * running + got[index]
    back = lax.all_to_all(jnp.stack(entries, axis=0), axis, 0, 0, tiled=True)
    return back.transpose(1, 0, 2, 3).reshape(heads, size, width)


def conv_silu(signal, tail_rows, weights):
    stacked = jnp.concatenate([tail_rows, signal], axis=0)
    kernel_taps = weights.shape[0]
    length = signal.shape[0]
    accum = jnp.zeros(signal.shape, jnp.float32)
    for offset in range(kernel_taps):
        accum = accum + weights[offset].astype(jnp.float32) * stacked[
            offset : offset + length
        ].astype(jnp.float32)
    return jax.nn.silu(accum).astype(jnp.bfloat16)


def combine_states(earlier, latter):
    return (earlier[0] * latter[0], latter[0][:, None, None] * earlier[1] + latter[1])


def local(
    xin,
    gate_in,
    bc_proj,
    dt_raw,
    dt_bias,
    rate,
    skip_gain,
    conv_x,
    conv_bc,
    norm_gain,
    valid_blocks,
):
    row_count, channels = xin.shape
    head_count = dt_raw.shape[1]
    head_size = channels // head_count
    span_count = row_count // SEGMENT_LENGTH
    kernel_taps = conv_x.shape[0]
    live_rows = valid_blocks[0] * BLOCK
    tail_x = lax.dynamic_slice_in_dim(xin, live_rows - (kernel_taps - 1), kernel_taps - 1, 0)
    tail_bc = lax.dynamic_slice_in_dim(bc_proj, live_rows - (kernel_taps - 1), kernel_taps - 1, 0)
    prev_x, prev_bc = passed_along((tail_x, tail_bc), "seq", 1)
    xconv = conv_silu(xin, prev_x, conv_x)
    bc_local = conv_silu(bc_proj, prev_bc, conv_bc)
    bc_full = lax.all_gather(bc_local, "ch", axis=1, tiled=True)
    state_size = bc_full.shape[1] // 2
    row_valid = (jnp.arange(row_count) < live_rows).astype(jnp.float32)
    step_size = jax.nn.softplus(dt_raw + dt_bias[None, :]) * row_valid[:, None]
    xfour = xconv.reshape(span_count, SEGMENT_LENGTH, head_count, head_size)
    b_three = bc_full[:, :state_size].reshape(span_count, SEGMENT_LENGTH, state_size)
    c_three = bc_full[:, state_size:].reshape(span_count, SEGMENT_LENGTH, state_size)
    step_three = step_size.reshape(span_count, SEGMENT_LENGTH, head_count)
    cumul = jnp.cumsum(-rate[None, None, :] * step_three, axis=1)
    scores = jnp.einsum("cqn,csn->cqs", c_three, b_three, preferred_element_type=jnp.float32)
    cum_heads = jnp.transpose(cumul, (0, 2, 1))
    diff = cum_heads[:, :, :, None] - cum_heads[:, :, None, :]
    causal = jnp.arange(SEGMENT_LENGTH)[:, None] >= jnp.arange(SEGMENT_LENGTH)[None, :]
    decay = jnp.where(causal, jnp.exp(jnp.where(causal, diff, 0.0)), 0.0)
    weights = (
        scores[:, None] * decay * jnp.transpose(step_three, (0, 2, 1))[:, :, None, :]
    ).astype(jnp.bfloat16)
    intra = jnp.einsum("chqs,cshp->cqhp", weights, xfour, preferred_element_type=jnp.float32)
    last_cum = cum_heads[:, :, -1]
    to_end = jnp.exp(last_cum[:, None, :] - cumul) * step_three
    x_weighted = (xfour.astype(jnp.float32) * to_end[..., None]).astype(jnp.bfloat16)
    block_state = jnp.einsum(
        "csn,cshp->chnp", b_three, x_weighted, preferred_element_type=jnp.float32
    )
    block_decay = jnp.exp(last_cum)
    current = jnp.zeros((head_count, state_size, head_size), jnp.float32)
    factor = jnp.ones((head_count,), jnp.float32)
    local_enter = []
    factor_list = []
    for index in range(span_count):
        local_enter.append(current)
        factor_list.append(factor)
        current = block_decay[index][:, None, None] * current + block_state[index]
        factor = factor * block_decay[index]
    group_state = scan_states(factor, current, "seq")
    state_enter = jnp.stack(
        [
            local_enter[index] + factor_list[index][:, None, None] * group_state
            for index in range(span_count)
        ],
        axis=0,
    )
    inter = jnp.einsum(
        "cqn,chnp->cqhp", c_three.astype(jnp.float32), state_enter, precision=lax.Precision.HIGHEST
    )
    inter = inter * jnp.exp(cumul)[..., None]
    y_full = intra + inter + skip_gain[None, None, :, None] * xfour.astype(jnp.float32)
    y_full = y_full.reshape(row_count, channels)
    gated = y_full * jax.nn.silu(gate_in.astype(jnp.float32))
    square_sum = lax.psum(jnp.sum(gated * gated, axis=1), "ch")
    mean_sq = square_sum / INNER
    normed = gated * lax.rsqrt(mean_sq + 1e-05)[:, None] * norm_gain[None, :] * row_valid[:, None]
    return normed.astype(jnp.bfloat16)


def solution(mesh):
    placed = (
        P("seq", "ch"),
        P("seq", "ch"),
        P("seq", "ch"),
        P("seq", "ch"),
        P("ch"),
        P("ch"),
        P("ch"),
        P(None, "ch"),
        P(None, "ch"),
        P("ch"),
        P("seq"),
    )
    return jax.shard_map(
        local, mesh=mesh, in_specs=placed, out_specs=P("seq", "ch"), check_vma=False
    )
```

```python
import functools

import jax
import jax.numpy as jnp
from jax import lax
from jax.experimental import pallas as pl
from jax.experimental.pallas import tpu as pltpu
from jax.sharding import PartitionSpec as P

SEGMENT_LENGTH = 256
BLOCK = 128
INNER = 16384


def passed_along(block, axis, distance):
    devices = range(lax.axis_size(axis))
    route = [(i - distance, i) for i in devices if i - distance in devices]
    return lax.ppermute(block, axis, route)


def scan_states(factor, state, axis):
    count = lax.axis_size(axis)
    heads, size, width = state.shape
    piece = size // count
    parts = state.reshape(heads, count, piece, width).transpose(1, 0, 2, 3)
    got = lax.all_to_all(parts, axis, 0, 0, tiled=True)
    decays = lax.all_gather(factor, axis)
    running = jnp.zeros((heads, piece, width), jnp.float32)
    entries = []
    for index in range(count):
        entries.append(running)
        running = decays[index][:, None, None] * running + got[index]
    back = lax.all_to_all(jnp.stack(entries, axis=0), axis, 0, 0, tiled=True)
    return back.transpose(1, 0, 2, 3).reshape(heads, size, width)


def conv_silu(signal, tail_rows, weights):
    stacked = jnp.concatenate([tail_rows, signal], axis=0)
    kernel_taps = weights.shape[0]
    length = signal.shape[0]
    accum = jnp.zeros(signal.shape, jnp.float32)
    for offset in range(kernel_taps):
        accum = accum + weights[offset].astype(jnp.float32) * stacked[
            offset : offset + length
        ].astype(jnp.float32)
    return jax.nn.silu(accum).astype(jnp.bfloat16)


def state_kernel(x_ref, bt_ref, toend_ref, out_ref):
    xw = (x_ref[...].astype(jnp.float32) * toend_ref[0, 0]).astype(jnp.bfloat16)
    out_ref[0, 0] = jnp.dot(bt_ref[0], xw, preferred_element_type=jnp.float32)


def intra_kernel(skip_ref, c_ref, b_ref, x_ref, cumc_ref, cumr_ref, stepr_ref, out_ref, scores):
    head = pl.program_id(1)

    @pl.when(head == 0)
    def _():
        scores[...] = lax.dot_general(
            c_ref[...], b_ref[...], (((1,), (1,)), ((), ())), preferred_element_type=jnp.float32
        )

    length = scores.shape[0]
    rows = lax.broadcasted_iota(jnp.int32, (length, length), 0)
    cols = lax.broadcasted_iota(jnp.int32, (length, length), 1)
    causal = rows >= cols
    diff = cumc_ref[0, 0] - cumr_ref[0, 0]
    decay = jnp.where(causal, jnp.exp(jnp.where(causal, diff, 0.0)), 0.0)
    weights = (scores[...] * decay * stepr_ref[0, 0]).astype(jnp.bfloat16)
    x = x_ref[...]
    intra = jnp.dot(weights, x, preferred_element_type=jnp.float32)
    out_ref[...] = intra + skip_ref[head] * x.astype(jnp.float32)


def gate_kernel(part_ref, c_ref, state_ref, ecum_ref, z_ref, out_ref, sq_ref):
    head = pl.program_id(1)
    state = state_ref[0, 0]
    high = state.astype(jnp.bfloat16)
    rest = state - high.astype(jnp.float32)
    mid = rest.astype(jnp.bfloat16)
    low = (rest - mid.astype(jnp.float32)).astype(jnp.bfloat16)
    c = c_ref[...]
    inter = (
        jnp.dot(c, high, preferred_element_type=jnp.float32)
        + jnp.dot(c, mid, preferred_element_type=jnp.float32)
        + jnp.dot(c, low, preferred_element_type=jnp.float32)
    )
    y = part_ref[...] + inter * ecum_ref[0, 0]
    z = z_ref[...].astype(jnp.float32)
    gated = y * (z / (1.0 + jnp.exp(-z)))
    out_ref[...] = gated
    total = jnp.sum(gated * gated, axis=1, keepdims=True)

    @pl.when(head == 0)
    def _():
        sq_ref[...] = total

    @pl.when(head > 0)
    def _():
        sq_ref[...] = sq_ref[...] + total


def block_states(xconv, b_t, to_end_col, spans, heads, width):
    rows = xconv.shape[0]
    size = b_t.shape[1]
    return pl.pallas_call(
        state_kernel,
        grid=(spans, heads),
        in_specs=[
            pl.BlockSpec((SEGMENT_LENGTH, width), lambda c, h: (c, h)),
            pl.BlockSpec((1, size, SEGMENT_LENGTH), lambda c, h: (c, 0, 0)),
            pl.BlockSpec((1, 1, SEGMENT_LENGTH, 1), lambda c, h: (c, h, 0, 0)),
        ],
        out_specs=pl.BlockSpec((1, 1, size, width), lambda c, h: (c, h, 0, 0)),
        out_shape=jax.ShapeDtypeStruct((spans, heads, size, width), jnp.float32),
        cost_estimate=pl.CostEstimate(
            flops=2 * rows * heads * width * size,
            bytes_accessed=rows * heads * width * 2 + spans * heads * size * width * 4,
            transcendentals=0,
        ),
    )(xconv, b_t, to_end_col)


def intra_terms(skip_gain, c_part, b_part, xconv, cum_col, cum_row, step_row, spans, heads, width):
    rows = xconv.shape[0]
    size = c_part.shape[1]
    return pl.pallas_call(
        intra_kernel,
        grid=(spans, heads),
        in_specs=[
            pl.BlockSpec(memory_space=pltpu.SMEM),
            pl.BlockSpec((SEGMENT_LENGTH, size), lambda c, h: (c, 0)),
            pl.BlockSpec((SEGMENT_LENGTH, size), lambda c, h: (c, 0)),
            pl.BlockSpec((SEGMENT_LENGTH, width), lambda c, h: (c, h)),
            pl.BlockSpec((1, 1, SEGMENT_LENGTH, 1), lambda c, h: (c, h, 0, 0)),
            pl.BlockSpec((1, 1, 1, SEGMENT_LENGTH), lambda c, h: (c, h, 0, 0)),
            pl.BlockSpec((1, 1, 1, SEGMENT_LENGTH), lambda c, h: (c, h, 0, 0)),
        ],
        out_specs=pl.BlockSpec((SEGMENT_LENGTH, width), lambda c, h: (c, h)),
        out_shape=jax.ShapeDtypeStruct((rows, heads * width), jnp.float32),
        scratch_shapes=[pltpu.VMEM((SEGMENT_LENGTH, SEGMENT_LENGTH), jnp.float32)],
        cost_estimate=pl.CostEstimate(
            flops=2 * rows * SEGMENT_LENGTH * (heads * width + size),
            bytes_accessed=rows * heads * width * 6,
            transcendentals=rows * SEGMENT_LENGTH * heads,
        ),
    )(skip_gain, c_part, b_part, xconv, cum_col, cum_row, step_row)


def gate_terms(partial, c_part, state_enter, ecum_col, gate_in, spans, heads, width):
    rows = partial.shape[0]
    size = c_part.shape[1]
    return pl.pallas_call(
        gate_kernel,
        grid=(spans, heads),
        in_specs=[
            pl.BlockSpec((SEGMENT_LENGTH, width), lambda c, h: (c, h)),
            pl.BlockSpec((SEGMENT_LENGTH, size), lambda c, h: (c, 0)),
            pl.BlockSpec((1, 1, size, width), lambda c, h: (c, h, 0, 0)),
            pl.BlockSpec((1, 1, SEGMENT_LENGTH, 1), lambda c, h: (c, h, 0, 0)),
            pl.BlockSpec((SEGMENT_LENGTH, width), lambda c, h: (c, h)),
        ],
        out_specs=[
            pl.BlockSpec((SEGMENT_LENGTH, width), lambda c, h: (c, h)),
            pl.BlockSpec((SEGMENT_LENGTH, 1), lambda c, h: (c, 0)),
        ],
        out_shape=[
            jax.ShapeDtypeStruct((rows, heads * width), jnp.float32),
            jax.ShapeDtypeStruct((rows, 1), jnp.float32),
        ],
        cost_estimate=pl.CostEstimate(
            flops=6 * rows * size * heads * width,
            bytes_accessed=rows * heads * width * 10,
            transcendentals=rows * heads * width,
        ),
    )(partial, c_part, state_enter, ecum_col, gate_in)


def local(
    xin,
    gate_in,
    bc_proj,
    dt_raw,
    dt_bias,
    rate,
    skip_gain,
    conv_x,
    conv_bc,
    norm_gain,
    valid_blocks,
):
    row_count, channels = xin.shape
    head_count = dt_raw.shape[1]
    head_size = channels // head_count
    span_count = row_count // SEGMENT_LENGTH
    kernel_taps = conv_x.shape[0]
    live_rows = valid_blocks[0] * BLOCK
    tail_x = lax.dynamic_slice_in_dim(xin, live_rows - (kernel_taps - 1), kernel_taps - 1, 0)
    tail_bc = lax.dynamic_slice_in_dim(bc_proj, live_rows - (kernel_taps - 1), kernel_taps - 1, 0)
    prev_x, prev_bc = passed_along((tail_x, tail_bc), "seq", 1)
    xconv = conv_silu(xin, prev_x, conv_x)
    bc_local = conv_silu(bc_proj, prev_bc, conv_bc)
    bc_full = lax.all_gather(bc_local, "ch", axis=1, tiled=True)
    state_size = bc_full.shape[1] // 2
    b_part = bc_full[:, :state_size]
    c_part = bc_full[:, state_size:]
    b_t = b_part.reshape(span_count, SEGMENT_LENGTH, state_size).transpose(0, 2, 1)
    row_valid = (jnp.arange(row_count) < live_rows).astype(jnp.float32)
    step_size = jax.nn.softplus(dt_raw + dt_bias[None, :]) * row_valid[:, None]
    step_three = step_size.reshape(span_count, SEGMENT_LENGTH, head_count)
    cumul = jnp.cumsum(-rate[None, None, :] * step_three, axis=1)
    cum_heads = jnp.transpose(cumul, (0, 2, 1))
    step_heads = jnp.transpose(step_three, (0, 2, 1))
    last_cum = cum_heads[:, :, -1]
    to_end = jnp.exp(last_cum[:, :, None] - cum_heads) * step_heads
    block_state = block_states(
        xconv, b_t, to_end[..., None], span_count, head_count, head_size
    )
    partial = intra_terms(
        skip_gain,
        c_part,
        b_part,
        xconv,
        cum_heads[..., None],
        cum_heads[:, :, None, :],
        step_heads[:, :, None, :],
        span_count,
        head_count,
        head_size,
    )
    block_decay = jnp.exp(last_cum)
    current = jnp.zeros((head_count, state_size, head_size), jnp.float32)
    factor = jnp.ones((head_count,), jnp.float32)
    local_enter = []
    factor_list = []
    for index in range(span_count):
        local_enter.append(current)
        factor_list.append(factor)
        current = block_decay[index][:, None, None] * current + block_state[index]
        factor = factor * block_decay[index]
    group_state = scan_states(factor, current, "seq")
    state_enter = jnp.stack(
        [
            local_enter[index] + factor_list[index][:, None, None] * group_state
            for index in range(span_count)
        ],
        axis=0,
    )
    gated, square_part = gate_terms(
        partial,
        c_part,
        state_enter,
        jnp.exp(cum_heads)[..., None],
        gate_in,
        span_count,
        head_count,
        head_size,
    )
    square_sum = lax.psum(square_part[:, 0], "ch")
    mean_sq = square_sum / INNER
    normed = gated * lax.rsqrt(mean_sq + 1e-05)[:, None] * norm_gain[None, :] * row_valid[:, None]
    return normed.astype(jnp.bfloat16)


def solution(mesh):
    placed = (
        P("seq", "ch"),
        P("seq", "ch"),
        P("seq", "ch"),
        P("seq", "ch"),
        P("ch"),
        P("ch"),
        P("ch"),
        P(None, "ch"),
        P(None, "ch"),
        P("ch"),
        P("seq"),
    )
    return jax.shard_map(
        local, mesh=mesh, in_specs=placed, out_specs=P("seq", "ch"), check_vma=False
    )
```

```python
import functools

import jax
import jax.numpy as jnp
from jax import lax
from jax.experimental import pallas as pl
from jax.experimental.pallas import tpu as pltpu
from jax.sharding import PartitionSpec as P

SEGMENT_LENGTH = 256
BLOCK = 128
INNER = 16384


def passed_along(block, axis, distance):
    devices = range(lax.axis_size(axis))
    route = [(i - distance, i) for i in devices if i - distance in devices]
    return lax.ppermute(block, axis, route)


def scan_states(factor, state, axis):
    count = lax.axis_size(axis)
    heads, size, width = state.shape
    piece = size // count
    parts = state.reshape(heads, count, piece, width).transpose(1, 0, 2, 3)
    got = lax.all_to_all(parts, axis, 0, 0, tiled=True)
    decays = lax.all_gather(factor, axis)
    running = jnp.zeros((heads, piece, width), jnp.float32)
    entries = []
    for index in range(count):
        entries.append(running)
        running = decays[index][:, None, None] * running + got[index]
    back = lax.all_to_all(jnp.stack(entries, axis=0), axis, 0, 0, tiled=True)
    return back.transpose(1, 0, 2, 3).reshape(heads, size, width)


def conv_silu(signal, tail_rows, weights):
    stacked = jnp.concatenate([tail_rows, signal], axis=0)
    kernel_taps = weights.shape[0]
    length = signal.shape[0]
    accum = jnp.zeros(signal.shape, jnp.float32)
    for offset in range(kernel_taps):
        accum = accum + weights[offset].astype(jnp.float32) * stacked[
            offset : offset + length
        ].astype(jnp.float32)
    return jax.nn.silu(accum).astype(jnp.bfloat16)


HEAD_GROUP = 8


def state_kernel(x_ref, bt_ref, toend_ref, out_ref):
    width = out_ref.shape[-1]
    bt = bt_ref[0]
    for j in range(out_ref.shape[1]):
        x = x_ref[:, j * width : (j + 1) * width].astype(jnp.float32)
        xw = (x * toend_ref[0, 0, :, j : j + 1]).astype(jnp.bfloat16)
        out_ref[0, j] = jnp.dot(bt, xw, preferred_element_type=jnp.float32)


def intra_kernel(skip_ref, c_ref, b_ref, x_ref, cumc_ref, cumr_ref, stepr_ref, out_ref):
    group = pl.program_id(1)
    heads = cumc_ref.shape[-1]
    width = out_ref.shape[-1] // heads
    scores = lax.dot_general(
        c_ref[...], b_ref[...], (((1,), (1,)), ((), ())), preferred_element_type=jnp.float32
    )
    length = scores.shape[0]
    rows = lax.broadcasted_iota(jnp.int32, (length, length), 0)
    cols = lax.broadcasted_iota(jnp.int32, (length, length), 1)
    causal = rows >= cols
    for j in range(heads):
        diff = cumc_ref[0, 0, :, j : j + 1] - cumr_ref[0, 0, j : j + 1, :]
        decay = jnp.where(causal, jnp.exp(jnp.where(causal, diff, 0.0)), 0.0)
        weights = (scores * decay * stepr_ref[0, 0, j : j + 1, :]).astype(jnp.bfloat16)
        x = x_ref[:, j * width : (j + 1) * width]
        intra = jnp.dot(weights, x, preferred_element_type=jnp.float32)
        out_ref[:, j * width : (j + 1) * width] = (
            intra + skip_ref[group * heads + j] * x.astype(jnp.float32)
        )


def gate_kernel(part_ref, c_ref, state_ref, ecum_ref, z_ref, out_ref, sq_ref):
    group = pl.program_id(1)
    heads = ecum_ref.shape[-1]
    width = out_ref.shape[-1] // heads
    c = c_ref[...]
    total = jnp.zeros((c.shape[0], 1), jnp.float32)
    for j in range(heads):
        state = state_ref[0, j]
        high = state.astype(jnp.bfloat16)
        rest = state - high.astype(jnp.float32)
        mid = rest.astype(jnp.bfloat16)
        low = (rest - mid.astype(jnp.float32)).astype(jnp.bfloat16)
        inter = (
            jnp.dot(c, high, preferred_element_type=jnp.float32)
            + jnp.dot(c, mid, preferred_element_type=jnp.float32)
            + jnp.dot(c, low, preferred_element_type=jnp.float32)
        )
        columns = slice(j * width, (j + 1) * width)
        y = part_ref[:, columns] + inter * ecum_ref[0, 0, :, j : j + 1]
        z = z_ref[:, columns].astype(jnp.float32)
        gated = y * (z / (1.0 + jnp.exp(-z)))
        out_ref[:, columns] = gated
        total = total + jnp.sum(gated * gated, axis=1, keepdims=True)

    @pl.when(group == 0)
    def _():
        sq_ref[...] = total

    @pl.when(group > 0)
    def _():
        sq_ref[...] = sq_ref[...] + total


def by_group(values, spans, heads):
    return values.reshape(spans, heads // HEAD_GROUP, HEAD_GROUP, -1)


def columns_by_group(values, spans, heads):
    return by_group(values, spans, heads).transpose(0, 1, 3, 2)


def block_states(xconv, b_t, to_end, spans, heads, width):
    rows = xconv.shape[0]
    size = b_t.shape[1]
    group = HEAD_GROUP
    return pl.pallas_call(
        state_kernel,
        grid=(spans, heads // group),
        in_specs=[
            pl.BlockSpec((SEGMENT_LENGTH, group * width), lambda c, g: (c, g)),
            pl.BlockSpec((1, size, SEGMENT_LENGTH), lambda c, g: (c, 0, 0)),
            pl.BlockSpec((1, 1, SEGMENT_LENGTH, group), lambda c, g: (c, g, 0, 0)),
        ],
        out_specs=pl.BlockSpec((1, group, size, width), lambda c, g: (c, g, 0, 0)),
        out_shape=jax.ShapeDtypeStruct((spans, heads, size, width), jnp.float32),
        cost_estimate=pl.CostEstimate(
            flops=2 * rows * heads * width * size,
            bytes_accessed=rows * heads * width * 2 + spans * heads * size * width * 4,
            transcendentals=0,
        ),
    )(xconv, b_t, columns_by_group(to_end, spans, heads))


def intra_terms(skip_gain, c_part, b_part, xconv, cum_heads, step_heads, spans, heads, width):
    rows = xconv.shape[0]
    size = c_part.shape[1]
    group = HEAD_GROUP
    return pl.pallas_call(
        intra_kernel,
        grid=(spans, heads // group),
        in_specs=[
            pl.BlockSpec(memory_space=pltpu.SMEM),
            pl.BlockSpec((SEGMENT_LENGTH, size), lambda c, g: (c, 0)),
            pl.BlockSpec((SEGMENT_LENGTH, size), lambda c, g: (c, 0)),
            pl.BlockSpec((SEGMENT_LENGTH, group * width), lambda c, g: (c, g)),
            pl.BlockSpec((1, 1, SEGMENT_LENGTH, group), lambda c, g: (c, g, 0, 0)),
            pl.BlockSpec((1, 1, group, SEGMENT_LENGTH), lambda c, g: (c, g, 0, 0)),
            pl.BlockSpec((1, 1, group, SEGMENT_LENGTH), lambda c, g: (c, g, 0, 0)),
        ],
        out_specs=pl.BlockSpec((SEGMENT_LENGTH, group * width), lambda c, g: (c, g)),
        out_shape=jax.ShapeDtypeStruct((rows, heads * width), jnp.float32),
        cost_estimate=pl.CostEstimate(
            flops=2 * rows * SEGMENT_LENGTH * (heads * width + size),
            bytes_accessed=rows * heads * width * 6,
            transcendentals=rows * SEGMENT_LENGTH * heads,
        ),
    )(
        skip_gain,
        c_part,
        b_part,
        xconv,
        columns_by_group(cum_heads, spans, heads),
        by_group(cum_heads, spans, heads),
        by_group(step_heads, spans, heads),
    )


def gate_terms(partial, c_part, state_enter, ecum, gate_in, spans, heads, width):
    rows = partial.shape[0]
    size = c_part.shape[1]
    group = HEAD_GROUP
    return pl.pallas_call(
        gate_kernel,
        grid=(spans, heads // group),
        in_specs=[
            pl.BlockSpec((SEGMENT_LENGTH, group * width), lambda c, g: (c, g)),
            pl.BlockSpec((SEGMENT_LENGTH, size), lambda c, g: (c, 0)),
            pl.BlockSpec((1, group, size, width), lambda c, g: (c, g, 0, 0)),
            pl.BlockSpec((1, 1, SEGMENT_LENGTH, group), lambda c, g: (c, g, 0, 0)),
            pl.BlockSpec((SEGMENT_LENGTH, group * width), lambda c, g: (c, g)),
        ],
        out_specs=[
            pl.BlockSpec((SEGMENT_LENGTH, group * width), lambda c, g: (c, g)),
            pl.BlockSpec((SEGMENT_LENGTH, 1), lambda c, g: (c, 0)),
        ],
        out_shape=[
            jax.ShapeDtypeStruct((rows, heads * width), jnp.float32),
            jax.ShapeDtypeStruct((rows, 1), jnp.float32),
        ],
        cost_estimate=pl.CostEstimate(
            flops=6 * rows * size * heads * width,
            bytes_accessed=rows * heads * width * 10,
            transcendentals=rows * heads * width,
        ),
    )(partial, c_part, state_enter, columns_by_group(ecum, spans, heads), gate_in)


def local(
    xin,
    gate_in,
    bc_proj,
    dt_raw,
    dt_bias,
    rate,
    skip_gain,
    conv_x,
    conv_bc,
    norm_gain,
    valid_blocks,
):
    row_count, channels = xin.shape
    head_count = dt_raw.shape[1]
    head_size = channels // head_count
    span_count = row_count // SEGMENT_LENGTH
    kernel_taps = conv_x.shape[0]
    live_rows = valid_blocks[0] * BLOCK
    tail_x = lax.dynamic_slice_in_dim(xin, live_rows - (kernel_taps - 1), kernel_taps - 1, 0)
    tail_bc = lax.dynamic_slice_in_dim(bc_proj, live_rows - (kernel_taps - 1), kernel_taps - 1, 0)
    prev_x, prev_bc = passed_along((tail_x, tail_bc), "seq", 1)
    xconv = conv_silu(xin, prev_x, conv_x)
    bc_local = conv_silu(bc_proj, prev_bc, conv_bc)
    bc_full = lax.all_gather(bc_local, "ch", axis=1, tiled=True)
    state_size = bc_full.shape[1] // 2
    b_part = bc_full[:, :state_size]
    c_part = bc_full[:, state_size:]
    b_t = b_part.reshape(span_count, SEGMENT_LENGTH, state_size).transpose(0, 2, 1)
    row_valid = (jnp.arange(row_count) < live_rows).astype(jnp.float32)
    step_size = jax.nn.softplus(dt_raw + dt_bias[None, :]) * row_valid[:, None]
    step_three = step_size.reshape(span_count, SEGMENT_LENGTH, head_count)
    cumul = jnp.cumsum(-rate[None, None, :] * step_three, axis=1)
    cum_heads = jnp.transpose(cumul, (0, 2, 1))
    step_heads = jnp.transpose(step_three, (0, 2, 1))
    last_cum = cum_heads[:, :, -1]
    to_end = jnp.exp(last_cum[:, :, None] - cum_heads) * step_heads
    block_state = block_states(xconv, b_t, to_end, span_count, head_count, head_size)
    partial = intra_terms(
        skip_gain,
        c_part,
        b_part,
        xconv,
        cum_heads,
        step_heads,
        span_count,
        head_count,
        head_size,
    )
    block_decay = jnp.exp(last_cum)
    current = jnp.zeros((head_count, state_size, head_size), jnp.float32)
    factor = jnp.ones((head_count,), jnp.float32)
    local_enter = []
    factor_list = []
    for index in range(span_count):
        local_enter.append(current)
        factor_list.append(factor)
        current = block_decay[index][:, None, None] * current + block_state[index]
        factor = factor * block_decay[index]
    group_state = scan_states(factor, current, "seq")
    state_enter = jnp.stack(
        [
            local_enter[index] + factor_list[index][:, None, None] * group_state
            for index in range(span_count)
        ],
        axis=0,
    )
    gated, square_part = gate_terms(
        partial,
        c_part,
        state_enter,
        jnp.exp(cum_heads),
        gate_in,
        span_count,
        head_count,
        head_size,
    )
    square_sum = lax.psum(square_part[:, 0], "ch")
    mean_sq = square_sum / INNER
    normed = gated * lax.rsqrt(mean_sq + 1e-05)[:, None] * norm_gain[None, :] * row_valid[:, None]
    return normed.astype(jnp.bfloat16)


def solution(mesh):
    placed = (
        P("seq", "ch"),
        P("seq", "ch"),
        P("seq", "ch"),
        P("seq", "ch"),
        P("ch"),
        P("ch"),
        P("ch"),
        P(None, "ch"),
        P(None, "ch"),
        P("ch"),
        P("seq"),
    )
    return jax.shard_map(
        local, mesh=mesh, in_specs=placed, out_specs=P("seq", "ch"), check_vma=False
    )
```

```python
import functools

import jax
import jax.numpy as jnp
from jax import lax
from jax.experimental import pallas as pl
from jax.experimental.pallas import tpu as pltpu
from jax.sharding import PartitionSpec as P

SEGMENT_LENGTH = 256
BLOCK = 128
INNER = 16384


def passed_along(block, axis, distance):
    devices = range(lax.axis_size(axis))
    route = [(i - distance, i) for i in devices if i - distance in devices]
    return lax.ppermute(block, axis, route)


def scan_states(factor, state, axis):
    count = lax.axis_size(axis)
    heads, size, width = state.shape
    piece = size // count
    parts = state.reshape(heads, count, piece, width).transpose(1, 0, 2, 3)
    got = lax.all_to_all(parts, axis, 0, 0, tiled=True)
    decays = lax.all_gather(factor, axis)
    running = jnp.zeros((heads, piece, width), jnp.float32)
    entries = []
    for index in range(count):
        entries.append(running)
        running = decays[index][:, None, None] * running + got[index]
    back = lax.all_to_all(jnp.stack(entries, axis=0), axis, 0, 0, tiled=True)
    return back.transpose(1, 0, 2, 3).reshape(heads, size, width)


def conv_silu(signal, tail_rows, weights):
    stacked = jnp.concatenate([tail_rows, signal], axis=0)
    kernel_taps = weights.shape[0]
    length = signal.shape[0]
    accum = jnp.zeros(signal.shape, jnp.float32)
    for offset in range(kernel_taps):
        accum = accum + weights[offset].astype(jnp.float32) * stacked[
            offset : offset + length
        ].astype(jnp.float32)
    return jax.nn.silu(accum).astype(jnp.bfloat16)


HEAD_GROUP = 8


def state_kernel(x_ref, halo_ref, taps_ref, bt_ref, toend_ref, out_ref, conv_ref):
    width = out_ref.shape[-1]
    taps = taps_ref[...].astype(jnp.float32)
    kernel_taps = taps.shape[0]
    signal = x_ref[...].astype(jnp.float32)
    edge = halo_ref[0].astype(jnp.float32)
    lead = edge.shape[0]
    stacked = jnp.concatenate([edge, signal[:lead]], axis=0)
    accum = jnp.zeros(signal.shape, jnp.float32)
    head = jnp.zeros((lead, signal.shape[1]), jnp.float32)
    for offset in range(kernel_taps):
        shift = kernel_taps - 1 - offset
        moved = signal if shift == 0 else pltpu.roll(signal, shift, 0)
        accum = accum + taps[offset : offset + 1] * moved
        head = head + taps[offset : offset + 1] * stacked[lead - shift : 2 * lead - shift]
    conv_ref[...] = (accum / (1.0 + jnp.exp(-accum))).astype(jnp.bfloat16)
    conv_ref[:lead, :] = (head / (1.0 + jnp.exp(-head))).astype(jnp.bfloat16)
    bt = bt_ref[0]
    for j in range(out_ref.shape[1]):
        x = conv_ref[:, j * width : (j + 1) * width].astype(jnp.float32)
        xw = (x * toend_ref[0, 0, :, j : j + 1]).astype(jnp.bfloat16)
        out_ref[0, j] = jnp.dot(bt, xw, preferred_element_type=jnp.float32)


def intra_kernel(skip_ref, c_ref, b_ref, x_ref, cumc_ref, cumr_ref, stepr_ref, out_ref):
    group = pl.program_id(1)
    heads = cumc_ref.shape[-1]
    width = out_ref.shape[-1] // heads
    scores = lax.dot_general(
        c_ref[...], b_ref[...], (((1,), (1,)), ((), ())), preferred_element_type=jnp.float32
    )
    length = scores.shape[0]
    rows = lax.broadcasted_iota(jnp.int32, (length, length), 0)
    cols = lax.broadcasted_iota(jnp.int32, (length, length), 1)
    causal = rows >= cols
    for j in range(heads):
        diff = cumc_ref[0, 0, :, j : j + 1] - cumr_ref[0, 0, j : j + 1, :]
        decay = jnp.where(causal, jnp.exp(jnp.where(causal, diff, 0.0)), 0.0)
        weights = (scores * decay * stepr_ref[0, 0, j : j + 1, :]).astype(jnp.bfloat16)
        x = x_ref[:, j * width : (j + 1) * width]
        intra = jnp.dot(weights, x, preferred_element_type=jnp.float32)
        out_ref[:, j * width : (j + 1) * width] = (
            intra + skip_ref[group * heads + j] * x.astype(jnp.float32)
        )


def gate_kernel(part_ref, c_ref, state_ref, ecum_ref, z_ref, out_ref, sq_ref):
    group = pl.program_id(1)
    heads = ecum_ref.shape[-1]
    width = out_ref.shape[-1] // heads
    c = c_ref[...]
    total = jnp.zeros((c.shape[0], 1), jnp.float32)
    for j in range(heads):
        state = state_ref[0, j]
        high = state.astype(jnp.bfloat16)
        rest = state - high.astype(jnp.float32)
        mid = rest.astype(jnp.bfloat16)
        low = (rest - mid.astype(jnp.float32)).astype(jnp.bfloat16)
        inter = (
            jnp.dot(c, high, preferred_element_type=jnp.float32)
            + jnp.dot(c, mid, preferred_element_type=jnp.float32)
            + jnp.dot(c, low, preferred_element_type=jnp.float32)
        )
        columns = slice(j * width, (j + 1) * width)
        y = part_ref[:, columns] + inter * ecum_ref[0, 0, :, j : j + 1]
        z = z_ref[:, columns].astype(jnp.float32)
        gated = y * (z / (1.0 + jnp.exp(-z)))
        out_ref[:, columns] = gated
        total = total + jnp.sum(gated * gated, axis=1, keepdims=True)

    @pl.when(group == 0)
    def _():
        sq_ref[...] = total

    @pl.when(group > 0)
    def _():
        sq_ref[...] = sq_ref[...] + total


def by_group(values, spans, heads):
    return values.reshape(spans, heads // HEAD_GROUP, HEAD_GROUP, -1)


def columns_by_group(values, spans, heads):
    return by_group(values, spans, heads).transpose(0, 1, 3, 2)


def block_states(xin, halo, conv_x, b_t, to_end, spans, heads, width):
    rows = xin.shape[0]
    size = b_t.shape[1]
    group = HEAD_GROUP
    lead = halo.shape[1]
    kernel_taps = conv_x.shape[0]
    return pl.pallas_call(
        state_kernel,
        grid=(spans, heads // group),
        in_specs=[
            pl.BlockSpec((SEGMENT_LENGTH, group * width), lambda c, g: (c, g)),
            pl.BlockSpec((1, lead, group * width), lambda c, g: (c, 0, g)),
            pl.BlockSpec((kernel_taps, group * width), lambda c, g: (0, g)),
            pl.BlockSpec((1, size, SEGMENT_LENGTH), lambda c, g: (c, 0, 0)),
            pl.BlockSpec((1, 1, SEGMENT_LENGTH, group), lambda c, g: (c, g, 0, 0)),
        ],
        out_specs=[
            pl.BlockSpec((1, group, size, width), lambda c, g: (c, g, 0, 0)),
            pl.BlockSpec((SEGMENT_LENGTH, group * width), lambda c, g: (c, g)),
        ],
        out_shape=[
            jax.ShapeDtypeStruct((spans, heads, size, width), jnp.float32),
            jax.ShapeDtypeStruct((rows, heads * width), jnp.bfloat16),
        ],
        cost_estimate=pl.CostEstimate(
            flops=2 * rows * heads * width * size,
            bytes_accessed=rows * heads * width * 4 + spans * heads * size * width * 4,
            transcendentals=rows * heads * width,
        ),
    )(xin, halo, conv_x, b_t, columns_by_group(to_end, spans, heads))


def intra_terms(skip_gain, c_part, b_part, xconv, cum_heads, step_heads, spans, heads, width):
    rows = xconv.shape[0]
    size = c_part.shape[1]
    group = HEAD_GROUP
    return pl.pallas_call(
        intra_kernel,
        grid=(spans, heads // group),
        in_specs=[
            pl.BlockSpec(memory_space=pltpu.SMEM),
            pl.BlockSpec((SEGMENT_LENGTH, size), lambda c, g: (c, 0)),
            pl.BlockSpec((SEGMENT_LENGTH, size), lambda c, g: (c, 0)),
            pl.BlockSpec((SEGMENT_LENGTH, group * width), lambda c, g: (c, g)),
            pl.BlockSpec((1, 1, SEGMENT_LENGTH, group), lambda c, g: (c, g, 0, 0)),
            pl.BlockSpec((1, 1, group, SEGMENT_LENGTH), lambda c, g: (c, g, 0, 0)),
            pl.BlockSpec((1, 1, group, SEGMENT_LENGTH), lambda c, g: (c, g, 0, 0)),
        ],
        out_specs=pl.BlockSpec((SEGMENT_LENGTH, group * width), lambda c, g: (c, g)),
        out_shape=jax.ShapeDtypeStruct((rows, heads * width), jnp.float32),
        cost_estimate=pl.CostEstimate(
            flops=2 * rows * SEGMENT_LENGTH * (heads * width + size),
            bytes_accessed=rows * heads * width * 6,
            transcendentals=rows * SEGMENT_LENGTH * heads,
        ),
    )(
        skip_gain,
        c_part,
        b_part,
        xconv,
        columns_by_group(cum_heads, spans, heads),
        by_group(cum_heads, spans, heads),
        by_group(step_heads, spans, heads),
    )


def gate_terms(partial, c_part, state_enter, ecum, gate_in, spans, heads, width):
    rows = partial.shape[0]
    size = c_part.shape[1]
    group = HEAD_GROUP
    return pl.pallas_call(
        gate_kernel,
        grid=(spans, heads // group),
        in_specs=[
            pl.BlockSpec((SEGMENT_LENGTH, group * width), lambda c, g: (c, g)),
            pl.BlockSpec((SEGMENT_LENGTH, size), lambda c, g: (c, 0)),
            pl.BlockSpec((1, group, size, width), lambda c, g: (c, g, 0, 0)),
            pl.BlockSpec((1, 1, SEGMENT_LENGTH, group), lambda c, g: (c, g, 0, 0)),
            pl.BlockSpec((SEGMENT_LENGTH, group * width), lambda c, g: (c, g)),
        ],
        out_specs=[
            pl.BlockSpec((SEGMENT_LENGTH, group * width), lambda c, g: (c, g)),
            pl.BlockSpec((SEGMENT_LENGTH, 1), lambda c, g: (c, 0)),
        ],
        out_shape=[
            jax.ShapeDtypeStruct((rows, heads * width), jnp.float32),
            jax.ShapeDtypeStruct((rows, 1), jnp.float32),
        ],
        cost_estimate=pl.CostEstimate(
            flops=6 * rows * size * heads * width,
            bytes_accessed=rows * heads * width * 10,
            transcendentals=rows * heads * width,
        ),
    )(partial, c_part, state_enter, columns_by_group(ecum, spans, heads), gate_in)


def local(
    xin,
    gate_in,
    bc_proj,
    dt_raw,
    dt_bias,
    rate,
    skip_gain,
    conv_x,
    conv_bc,
    norm_gain,
    valid_blocks,
):
    row_count, channels = xin.shape
    head_count = dt_raw.shape[1]
    head_size = channels // head_count
    span_count = row_count // SEGMENT_LENGTH
    kernel_taps = conv_x.shape[0]
    live_rows = valid_blocks[0] * BLOCK
    tail_x = lax.dynamic_slice_in_dim(xin, live_rows - (kernel_taps - 1), kernel_taps - 1, 0)
    tail_bc = lax.dynamic_slice_in_dim(bc_proj, live_rows - (kernel_taps - 1), kernel_taps - 1, 0)
    prev_x, prev_bc = passed_along((tail_x, tail_bc), "seq", 1)
    lead = 8
    edges = jnp.concatenate(
        [prev_x[None], xin.reshape(span_count, SEGMENT_LENGTH, channels)[:-1, -(kernel_taps - 1) :]],
        axis=0,
    )
    halo = jnp.pad(edges, ((0, 0), (lead - (kernel_taps - 1), 0), (0, 0)))
    bc_local = conv_silu(bc_proj, prev_bc, conv_bc)
    bc_full = lax.all_gather(bc_local, "ch", axis=1, tiled=True)
    state_size = bc_full.shape[1] // 2
    b_part = bc_full[:, :state_size]
    c_part = bc_full[:, state_size:]
    b_t = b_part.reshape(span_count, SEGMENT_LENGTH, state_size).transpose(0, 2, 1)
    row_valid = (jnp.arange(row_count) < live_rows).astype(jnp.float32)
    step_size = jax.nn.softplus(dt_raw + dt_bias[None, :]) * row_valid[:, None]
    step_three = step_size.reshape(span_count, SEGMENT_LENGTH, head_count)
    cumul = jnp.cumsum(-rate[None, None, :] * step_three, axis=1)
    cum_heads = jnp.transpose(cumul, (0, 2, 1))
    step_heads = jnp.transpose(step_three, (0, 2, 1))
    last_cum = cum_heads[:, :, -1]
    to_end = jnp.exp(last_cum[:, :, None] - cum_heads) * step_heads
    block_state, xconv = block_states(
        xin, halo, conv_x, b_t, to_end, span_count, head_count, head_size
    )
    partial = intra_terms(
        skip_gain,
        c_part,
        b_part,
        xconv,
        cum_heads,
        step_heads,
        span_count,
        head_count,
        head_size,
    )
    block_decay = jnp.exp(last_cum)
    current = jnp.zeros((head_count, state_size, head_size), jnp.float32)
    factor = jnp.ones((head_count,), jnp.float32)
    local_enter = []
    factor_list = []
    for index in range(span_count):
        local_enter.append(current)
        factor_list.append(factor)
        current = block_decay[index][:, None, None] * current + block_state[index]
        factor = factor * block_decay[index]
    group_state = scan_states(factor, current, "seq")
    state_enter = jnp.stack(
        [
            local_enter[index] + factor_list[index][:, None, None] * group_state
            for index in range(span_count)
        ],
        axis=0,
    )
    gated, square_part = gate_terms(
        partial,
        c_part,
        state_enter,
        jnp.exp(cum_heads),
        gate_in,
        span_count,
        head_count,
        head_size,
    )
    square_sum = lax.psum(square_part[:, 0], "ch")
    mean_sq = square_sum / INNER
    normed = gated * lax.rsqrt(mean_sq + 1e-05)[:, None] * norm_gain[None, :] * row_valid[:, None]
    return normed.astype(jnp.bfloat16)


def solution(mesh):
    placed = (
        P("seq", "ch"),
        P("seq", "ch"),
        P("seq", "ch"),
        P("seq", "ch"),
        P("ch"),
        P("ch"),
        P("ch"),
        P(None, "ch"),
        P(None, "ch"),
        P("ch"),
        P("seq"),
    )
    return jax.shard_map(
        local, mesh=mesh, in_specs=placed, out_specs=P("seq", "ch"), check_vma=False
    )
```

```python
import functools

import jax
import jax.numpy as jnp
from jax import lax
from jax.experimental import pallas as pl
from jax.experimental.pallas import tpu as pltpu
from jax.sharding import PartitionSpec as P

SEGMENT_LENGTH = 256
BLOCK = 128
INNER = 16384


def passed_along(block, axis, distance):
    devices = range(lax.axis_size(axis))
    route = [(i - distance, i) for i in devices if i - distance in devices]
    return lax.ppermute(block, axis, route)


def scan_states(factor, state, axis):
    count = lax.axis_size(axis)
    heads, size, width = state.shape
    piece = size // count
    parts = state.reshape(heads, count, piece, width).transpose(1, 0, 2, 3)
    slot = jnp.zeros((piece, width), jnp.float32).at[0, :heads].set(factor)
    payload = jnp.concatenate(
        [parts, jnp.broadcast_to(slot, (count, 1, piece, width))], axis=1
    )
    got = lax.all_to_all(payload, axis, 0, 0, tiled=True)
    decays = got[:, heads, 0, :heads]
    running = jnp.zeros((heads, piece, width), jnp.float32)
    entries = []
    for index in range(count):
        entries.append(running)
        running = decays[index][:, None, None] * running + got[index, :heads]
    back = lax.all_to_all(jnp.stack(entries, axis=0), axis, 0, 0, tiled=True)
    return back.transpose(1, 0, 2, 3).reshape(heads, size, width)


def conv_silu(signal, tail_rows, weights):
    stacked = jnp.concatenate([tail_rows, signal], axis=0)
    kernel_taps = weights.shape[0]
    length = signal.shape[0]
    accum = jnp.zeros(signal.shape, jnp.float32)
    for offset in range(kernel_taps):
        accum = accum + weights[offset].astype(jnp.float32) * stacked[
            offset : offset + length
        ].astype(jnp.float32)
    return jax.nn.silu(accum).astype(jnp.bfloat16)


HEAD_GROUP = 8


def state_kernel(x_ref, halo_ref, taps_ref, bt_ref, toend_ref, out_ref, conv_ref):
    width = out_ref.shape[-1]
    taps = taps_ref[...].astype(jnp.float32)
    kernel_taps = taps.shape[0]
    signal = x_ref[...].astype(jnp.float32)
    edge = halo_ref[0].astype(jnp.float32)
    lead = edge.shape[0]
    stacked = jnp.concatenate([edge, signal[:lead]], axis=0)
    accum = jnp.zeros(signal.shape, jnp.float32)
    head = jnp.zeros((lead, signal.shape[1]), jnp.float32)
    for offset in range(kernel_taps):
        shift = kernel_taps - 1 - offset
        moved = signal if shift == 0 else pltpu.roll(signal, shift, 0)
        accum = accum + taps[offset : offset + 1] * moved
        head = head + taps[offset : offset + 1] * stacked[lead - shift : 2 * lead - shift]
    conv_ref[...] = (accum / (1.0 + jnp.exp(-accum))).astype(jnp.bfloat16)
    conv_ref[:lead, :] = (head / (1.0 + jnp.exp(-head))).astype(jnp.bfloat16)
    bt = bt_ref[0]
    for j in range(out_ref.shape[1]):
        x = conv_ref[:, j * width : (j + 1) * width].astype(jnp.float32)
        xw = (x * toend_ref[0, 0, :, j : j + 1]).astype(jnp.bfloat16)
        out_ref[0, j] = jnp.dot(bt, xw, preferred_element_type=jnp.float32)


def intra_kernel(skip_ref, c_ref, b_ref, x_ref, cumc_ref, cumr_ref, stepr_ref, out_ref):
    group = pl.program_id(1)
    heads = cumc_ref.shape[-1]
    width = out_ref.shape[-1] // heads
    scores = lax.dot_general(
        c_ref[...], b_ref[...], (((1,), (1,)), ((), ())), preferred_element_type=jnp.float32
    )
    length = scores.shape[0]
    rows = lax.broadcasted_iota(jnp.int32, (length, length), 0)
    cols = lax.broadcasted_iota(jnp.int32, (length, length), 1)
    causal = rows >= cols
    for j in range(heads):
        diff = cumc_ref[0, 0, :, j : j + 1] - cumr_ref[0, 0, j : j + 1, :]
        decay = jnp.where(causal, jnp.exp(jnp.where(causal, diff, 0.0)), 0.0)
        weights = (scores * decay * stepr_ref[0, 0, j : j + 1, :]).astype(jnp.bfloat16)
        x = x_ref[:, j * width : (j + 1) * width]
        intra = jnp.dot(weights, x, preferred_element_type=jnp.float32)
        out_ref[:, j * width : (j + 1) * width] = (
            intra + skip_ref[group * heads + j] * x.astype(jnp.float32)
        )


def gate_kernel(part_ref, c_ref, state_ref, ecum_ref, z_ref, out_ref, sq_ref):
    group = pl.program_id(1)
    heads = ecum_ref.shape[-1]
    width = out_ref.shape[-1] // heads
    c = c_ref[...]
    total = jnp.zeros((c.shape[0], 1), jnp.float32)
    for j in range(heads):
        state = state_ref[0, j]
        high = state.astype(jnp.bfloat16)
        rest = state - high.astype(jnp.float32)
        mid = rest.astype(jnp.bfloat16)
        low = (rest - mid.astype(jnp.float32)).astype(jnp.bfloat16)
        inter = (
            jnp.dot(c, high, preferred_element_type=jnp.float32)
            + jnp.dot(c, mid, preferred_element_type=jnp.float32)
            + jnp.dot(c, low, preferred_element_type=jnp.float32)
        )
        columns = slice(j * width, (j + 1) * width)
        y = part_ref[:, columns] + inter * ecum_ref[0, 0, :, j : j + 1]
        z = z_ref[:, columns].astype(jnp.float32)
        gated = y * (z / (1.0 + jnp.exp(-z)))
        out_ref[:, columns] = gated
        total = total + jnp.sum(gated * gated, axis=1, keepdims=True)

    @pl.when(group == 0)
    def _():
        sq_ref[...] = total

    @pl.when(group > 0)
    def _():
        sq_ref[...] = sq_ref[...] + total


def by_group(values, spans, heads):
    return values.reshape(spans, heads // HEAD_GROUP, HEAD_GROUP, -1)


def columns_by_group(values, spans, heads):
    return by_group(values, spans, heads).transpose(0, 1, 3, 2)


def block_states(xin, halo, conv_x, b_t, to_end, spans, heads, width, offset):
    rows = xin.shape[0]
    size = b_t.shape[1]
    group = HEAD_GROUP
    lead = halo.shape[1]
    kernel_taps = conv_x.shape[0]
    return pl.pallas_call(
        state_kernel,
        grid=(spans, heads // group),
        in_specs=[
            pl.BlockSpec((SEGMENT_LENGTH, group * width), lambda c, g: (c, g + offset)),
            pl.BlockSpec((1, lead, group * width), lambda c, g: (c, 0, g + offset)),
            pl.BlockSpec((kernel_taps, group * width), lambda c, g: (0, g + offset)),
            pl.BlockSpec((1, size, SEGMENT_LENGTH), lambda c, g: (c, 0, 0)),
            pl.BlockSpec((1, 1, SEGMENT_LENGTH, group), lambda c, g: (c, g, 0, 0)),
        ],
        out_specs=[
            pl.BlockSpec((1, group, size, width), lambda c, g: (c, g, 0, 0)),
            pl.BlockSpec((SEGMENT_LENGTH, group * width), lambda c, g: (c, g)),
        ],
        out_shape=[
            jax.ShapeDtypeStruct((spans, heads, size, width), jnp.float32),
            jax.ShapeDtypeStruct((rows, heads * width), jnp.bfloat16),
        ],
        cost_estimate=pl.CostEstimate(
            flops=2 * rows * heads * width * size,
            bytes_accessed=rows * heads * width * 4 + spans * heads * size * width * 4,
            transcendentals=rows * heads * width,
        ),
    )(xin, halo, conv_x, b_t, columns_by_group(to_end, spans, heads))


def intra_terms(skip_gain, c_part, b_part, xconv, cum_heads, step_heads, spans, heads, width):
    rows = xconv.shape[0]
    size = c_part.shape[1]
    group = HEAD_GROUP
    return pl.pallas_call(
        intra_kernel,
        grid=(spans, heads // group),
        in_specs=[
            pl.BlockSpec(memory_space=pltpu.SMEM),
            pl.BlockSpec((SEGMENT_LENGTH, size), lambda c, g: (c, 0)),
            pl.BlockSpec((SEGMENT_LENGTH, size), lambda c, g: (c, 0)),
            pl.BlockSpec((SEGMENT_LENGTH, group * width), lambda c, g: (c, g)),
            pl.BlockSpec((1, 1, SEGMENT_LENGTH, group), lambda c, g: (c, g, 0, 0)),
            pl.BlockSpec((1, 1, group, SEGMENT_LENGTH), lambda c, g: (c, g, 0, 0)),
            pl.BlockSpec((1, 1, group, SEGMENT_LENGTH), lambda c, g: (c, g, 0, 0)),
        ],
        out_specs=pl.BlockSpec((SEGMENT_LENGTH, group * width), lambda c, g: (c, g)),
        out_shape=jax.ShapeDtypeStruct((rows, heads * width), jnp.float32),
        cost_estimate=pl.CostEstimate(
            flops=2 * rows * SEGMENT_LENGTH * (heads * width + size),
            bytes_accessed=rows * heads * width * 6,
            transcendentals=rows * SEGMENT_LENGTH * heads,
        ),
    )(
        skip_gain,
        c_part,
        b_part,
        xconv,
        columns_by_group(cum_heads, spans, heads),
        by_group(cum_heads, spans, heads),
        by_group(step_heads, spans, heads),
    )


def gate_terms(partial, c_part, state_enter, ecum, gate_in, spans, heads, width, offset):
    rows = partial.shape[0]
    size = c_part.shape[1]
    group = HEAD_GROUP
    return pl.pallas_call(
        gate_kernel,
        grid=(spans, heads // group),
        in_specs=[
            pl.BlockSpec((SEGMENT_LENGTH, group * width), lambda c, g: (c, g)),
            pl.BlockSpec((SEGMENT_LENGTH, size), lambda c, g: (c, 0)),
            pl.BlockSpec((1, group, size, width), lambda c, g: (c, g, 0, 0)),
            pl.BlockSpec((1, 1, SEGMENT_LENGTH, group), lambda c, g: (c, g, 0, 0)),
            pl.BlockSpec((SEGMENT_LENGTH, group * width), lambda c, g: (c, g + offset)),
        ],
        out_specs=[
            pl.BlockSpec((SEGMENT_LENGTH, group * width), lambda c, g: (c, g)),
            pl.BlockSpec((SEGMENT_LENGTH, 1), lambda c, g: (c, 0)),
        ],
        out_shape=[
            jax.ShapeDtypeStruct((rows, heads * width), jnp.float32),
            jax.ShapeDtypeStruct((rows, 1), jnp.float32),
        ],
        cost_estimate=pl.CostEstimate(
            flops=6 * rows * size * heads * width,
            bytes_accessed=rows * heads * width * 10,
            transcendentals=rows * heads * width,
        ),
    )(partial, c_part, state_enter, columns_by_group(ecum, spans, heads), gate_in)


def local(
    xin,
    gate_in,
    bc_proj,
    dt_raw,
    dt_bias,
    rate,
    skip_gain,
    conv_x,
    conv_bc,
    norm_gain,
    valid_blocks,
):
    row_count, channels = xin.shape
    head_count = dt_raw.shape[1]
    head_size = channels // head_count
    span_count = row_count // SEGMENT_LENGTH
    kernel_taps = conv_x.shape[0]
    live_rows = valid_blocks[0] * BLOCK
    tail_x = lax.dynamic_slice_in_dim(xin, live_rows - (kernel_taps - 1), kernel_taps - 1, 0)
    tail_bc = lax.dynamic_slice_in_dim(bc_proj, live_rows - (kernel_taps - 1), kernel_taps - 1, 0)
    prev_x, prev_bc = passed_along((tail_x, tail_bc), "seq", 1)
    lead = 8
    edges = jnp.concatenate(
        [prev_x[None], xin.reshape(span_count, SEGMENT_LENGTH, channels)[:-1, -(kernel_taps - 1) :]],
        axis=0,
    )
    halo = jnp.pad(edges, ((0, 0), (lead - (kernel_taps - 1), 0), (0, 0)))
    bc_local = conv_silu(bc_proj, prev_bc, conv_bc)
    bc_full = lax.all_gather(bc_local, "ch", axis=1, tiled=True)
    state_size = bc_full.shape[1] // 2
    b_part = bc_full[:, :state_size]
    c_part = bc_full[:, state_size:]
    b_t = b_part.reshape(span_count, SEGMENT_LENGTH, state_size).transpose(0, 2, 1)
    row_valid = (jnp.arange(row_count) < live_rows).astype(jnp.float32)
    step_size = jax.nn.softplus(dt_raw + dt_bias[None, :]) * row_valid[:, None]
    step_three = step_size.reshape(span_count, SEGMENT_LENGTH, head_count)
    cumul = jnp.cumsum(-rate[None, None, :] * step_three, axis=1)
    cum_heads = jnp.transpose(cumul, (0, 2, 1))
    step_heads = jnp.transpose(step_three, (0, 2, 1))
    last_cum = cum_heads[:, :, -1]
    to_end = jnp.exp(last_cum[:, :, None] - cum_heads) * step_heads
    block_decay = jnp.exp(last_cum)
    halves = 2 if head_count % (2 * HEAD_GROUP) == 0 else 1
    part_heads = head_count // halves
    gated_parts = []
    square_part = None
    for part in range(halves):
        heads = slice(part * part_heads, (part + 1) * part_heads)
        offset = part * part_heads // HEAD_GROUP
        block_state, xconv = block_states(
            xin, halo, conv_x, b_t, to_end[:, heads], span_count, part_heads, head_size, offset
        )
        current = jnp.zeros((part_heads, state_size, head_size), jnp.float32)
        factor = jnp.ones((part_heads,), jnp.float32)
        local_enter = []
        factor_list = []
        for index in range(span_count):
            local_enter.append(current)
            factor_list.append(factor)
            current = block_decay[index, heads][:, None, None] * current + block_state[index]
            factor = factor * block_decay[index, heads]
        group_state = scan_states(factor, current, "seq")
        partial = intra_terms(
            skip_gain[heads],
            c_part,
            b_part,
            xconv,
            cum_heads[:, heads],
            step_heads[:, heads],
            span_count,
            part_heads,
            head_size,
        )
        state_enter = jnp.stack(
            [
                local_enter[index] + factor_list[index][:, None, None] * group_state
                for index in range(span_count)
            ],
            axis=0,
        )
        gated, squares = gate_terms(
            partial,
            c_part,
            state_enter,
            jnp.exp(cum_heads[:, heads]),
            gate_in,
            span_count,
            part_heads,
            head_size,
            offset,
        )
        gated_parts.append(gated)
        square_part = squares if square_part is None else square_part + squares
    gated = jnp.concatenate(gated_parts, axis=1)
    square_sum = lax.psum(square_part[:, 0], "ch")
    mean_sq = square_sum / INNER
    normed = gated * lax.rsqrt(mean_sq + 1e-05)[:, None] * norm_gain[None, :] * row_valid[:, None]
    return normed.astype(jnp.bfloat16)


def solution(mesh):
    placed = (
        P("seq", "ch"),
        P("seq", "ch"),
        P("seq", "ch"),
        P("seq", "ch"),
        P("ch"),
        P("ch"),
        P("ch"),
        P(None, "ch"),
        P(None, "ch"),
        P("ch"),
        P("seq"),
    )
    return jax.shard_map(
        local, mesh=mesh, in_specs=placed, out_specs=P("seq", "ch"), check_vma=False
    )
```

```python
import functools

import jax
import jax.numpy as jnp
from jax import lax
from jax.experimental import pallas as pl
from jax.experimental.pallas import tpu as pltpu
from jax.sharding import PartitionSpec as P

SEGMENT_LENGTH = 256
BLOCK = 128
INNER = 16384


def passed_along(block, axis, distance):
    devices = range(lax.axis_size(axis))
    route = [(i - distance, i) for i in devices if i - distance in devices]
    return lax.ppermute(block, axis, route)


def scan_states(factor, state, axis, tied):
    count = lax.axis_size(axis)
    split = count % 2 == 0 and count >= 4
    members = count // 2 if split else count
    groups = [list(range(0, members)), list(range(members, count))] if split else None
    heads, size, width = state.shape
    piece = size // members
    parts = state.reshape(heads, members, piece, width).transpose(1, 0, 2, 3)
    slot = jnp.zeros((piece, width), jnp.float32).at[0, :heads].set(factor)
    payload = jnp.concatenate(
        [parts, jnp.broadcast_to(slot, (members, 1, piece, width))], axis=1
    )
    got = lax.all_to_all(payload, axis, 0, 0, tiled=True, axis_index_groups=groups)
    decays = got[:, heads, 0, :heads]
    tied = lax.optimization_barrier((tied, got))[0]
    running = jnp.zeros((heads, piece, width), jnp.float32)
    entries = []
    for index in range(members):
        entries.append(running)
        running = decays[index][:, None, None] * running + got[index, :heads]
    if split:
        route = [(i, i + members) for i in range(members)]
        earlier = lax.ppermute(running, axis, route)
        carry = jnp.ones((heads,), jnp.float32)
        for index in range(members):
            entries[index] = entries[index] + carry[:, None, None] * earlier
            carry = carry * decays[index]
    back = lax.all_to_all(
        jnp.stack(entries, axis=0), axis, 0, 0, tiled=True, axis_index_groups=groups
    )
    return back.transpose(1, 0, 2, 3).reshape(heads, size, width), tied


def conv_silu(signal, tail_rows, weights):
    stacked = jnp.concatenate([tail_rows, signal], axis=0)
    kernel_taps = weights.shape[0]
    length = signal.shape[0]
    accum = jnp.zeros(signal.shape, jnp.float32)
    for offset in range(kernel_taps):
        accum = accum + weights[offset].astype(jnp.float32) * stacked[
            offset : offset + length
        ].astype(jnp.float32)
    return jax.nn.silu(accum).astype(jnp.bfloat16)


HEAD_GROUP = 8


def state_kernel(x_ref, halo_ref, taps_ref, bt_ref, toend_ref, out_ref, conv_ref):
    width = out_ref.shape[-1]
    taps = taps_ref[...].astype(jnp.float32)
    kernel_taps = taps.shape[0]
    signal = x_ref[...].astype(jnp.float32)
    edge = halo_ref[0].astype(jnp.float32)
    lead = edge.shape[0]
    stacked = jnp.concatenate([edge, signal[:lead]], axis=0)
    accum = jnp.zeros(signal.shape, jnp.float32)
    head = jnp.zeros((lead, signal.shape[1]), jnp.float32)
    for offset in range(kernel_taps):
        shift = kernel_taps - 1 - offset
        moved = signal if shift == 0 else pltpu.roll(signal, shift, 0)
        accum = accum + taps[offset : offset + 1] * moved
        head = head + taps[offset : offset + 1] * stacked[lead - shift : 2 * lead - shift]
    conv_ref[...] = (accum / (1.0 + jnp.exp(-accum))).astype(jnp.bfloat16)
    conv_ref[:lead, :] = (head / (1.0 + jnp.exp(-head))).astype(jnp.bfloat16)
    bt = bt_ref[0]
    for j in range(out_ref.shape[1]):
        x = conv_ref[:, j * width : (j + 1) * width].astype(jnp.float32)
        xw = (x * toend_ref[0, 0, :, j : j + 1]).astype(jnp.bfloat16)
        out_ref[0, j] = jnp.dot(bt, xw, preferred_element_type=jnp.float32)


def intra_kernel(skip_ref, c_ref, b_ref, x_ref, cumc_ref, cumr_ref, stepr_ref, out_ref):
    group = pl.program_id(1)
    heads = cumc_ref.shape[-1]
    width = out_ref.shape[-1] // heads
    scores = lax.dot_general(
        c_ref[...], b_ref[...], (((1,), (1,)), ((), ())), preferred_element_type=jnp.float32
    )
    length = scores.shape[0]
    rows = lax.broadcasted_iota(jnp.int32, (length, length), 0)
    cols = lax.broadcasted_iota(jnp.int32, (length, length), 1)
    causal = rows >= cols
    for j in range(heads):
        diff = cumc_ref[0, 0, :, j : j + 1] - cumr_ref[0, 0, j : j + 1, :]
        decay = jnp.where(causal, jnp.exp(jnp.where(causal, diff, 0.0)), 0.0)
        weights = (scores * decay * stepr_ref[0, 0, j : j + 1, :]).astype(jnp.bfloat16)
        x = x_ref[:, j * width : (j + 1) * width]
        intra = jnp.dot(weights, x, preferred_element_type=jnp.float32)
        out_ref[:, j * width : (j + 1) * width] = (
            intra + skip_ref[group * heads + j] * x.astype(jnp.float32)
        )


def gate_kernel(part_ref, c_ref, state_ref, ecum_ref, z_ref, out_ref, sq_ref):
    group = pl.program_id(1)
    heads = ecum_ref.shape[-1]
    width = out_ref.shape[-1] // heads
    c = c_ref[...]
    total = jnp.zeros((c.shape[0], 1), jnp.float32)
    for j in range(heads):
        state = state_ref[0, j]
        high = state.astype(jnp.bfloat16)
        rest = state - high.astype(jnp.float32)
        mid = rest.astype(jnp.bfloat16)
        low = (rest - mid.astype(jnp.float32)).astype(jnp.bfloat16)
        inter = (
            jnp.dot(c, high, preferred_element_type=jnp.float32)
            + jnp.dot(c, mid, preferred_element_type=jnp.float32)
            + jnp.dot(c, low, preferred_element_type=jnp.float32)
        )
        columns = slice(j * width, (j + 1) * width)
        y = part_ref[:, columns] + inter * ecum_ref[0, 0, :, j : j + 1]
        z = z_ref[:, columns].astype(jnp.float32)
        gated = y * (z / (1.0 + jnp.exp(-z)))
        out_ref[:, columns] = gated
        total = total + jnp.sum(gated * gated, axis=1, keepdims=True)

    @pl.when(group == 0)
    def _():
        sq_ref[...] = total

    @pl.when(group > 0)
    def _():
        sq_ref[...] = sq_ref[...] + total


def by_group(values, spans, heads):
    return values.reshape(spans, heads // HEAD_GROUP, HEAD_GROUP, -1)


def columns_by_group(values, spans, heads):
    return by_group(values, spans, heads).transpose(0, 1, 3, 2)


def block_states(xin, halo, conv_x, b_t, to_end, spans, heads, width, offset):
    rows = xin.shape[0]
    size = b_t.shape[1]
    group = HEAD_GROUP
    lead = halo.shape[1]
    kernel_taps = conv_x.shape[0]
    return pl.pallas_call(
        state_kernel,
        grid=(spans, heads // group),
        in_specs=[
            pl.BlockSpec((SEGMENT_LENGTH, group * width), lambda c, g: (c, g + offset)),
            pl.BlockSpec((1, lead, group * width), lambda c, g: (c, 0, g + offset)),
            pl.BlockSpec((kernel_taps, group * width), lambda c, g: (0, g + offset)),
            pl.BlockSpec((1, size, SEGMENT_LENGTH), lambda c, g: (c, 0, 0)),
            pl.BlockSpec((1, 1, SEGMENT_LENGTH, group), lambda c, g: (c, g, 0, 0)),
        ],
        out_specs=[
            pl.BlockSpec((1, group, size, width), lambda c, g: (c, g, 0, 0)),
            pl.BlockSpec((SEGMENT_LENGTH, group * width), lambda c, g: (c, g)),
        ],
        out_shape=[
            jax.ShapeDtypeStruct((spans, heads, size, width), jnp.float32),
            jax.ShapeDtypeStruct((rows, heads * width), jnp.bfloat16),
        ],
        cost_estimate=pl.CostEstimate(
            flops=2 * rows * heads * width * size,
            bytes_accessed=rows * heads * width * 4 + spans * heads * size * width * 4,
            transcendentals=rows * heads * width,
        ),
    )(xin, halo, conv_x, b_t, columns_by_group(to_end, spans, heads))


def intra_terms(skip_gain, c_part, b_part, xconv, cum_heads, step_heads, spans, heads, width):
    rows = xconv.shape[0]
    size = c_part.shape[1]
    group = HEAD_GROUP
    return pl.pallas_call(
        intra_kernel,
        grid=(spans, heads // group),
        in_specs=[
            pl.BlockSpec(memory_space=pltpu.SMEM),
            pl.BlockSpec((SEGMENT_LENGTH, size), lambda c, g: (c, 0)),
            pl.BlockSpec((SEGMENT_LENGTH, size), lambda c, g: (c, 0)),
            pl.BlockSpec((SEGMENT_LENGTH, group * width), lambda c, g: (c, g)),
            pl.BlockSpec((1, 1, SEGMENT_LENGTH, group), lambda c, g: (c, g, 0, 0)),
            pl.BlockSpec((1, 1, group, SEGMENT_LENGTH), lambda c, g: (c, g, 0, 0)),
            pl.BlockSpec((1, 1, group, SEGMENT_LENGTH), lambda c, g: (c, g, 0, 0)),
        ],
        out_specs=pl.BlockSpec((SEGMENT_LENGTH, group * width), lambda c, g: (c, g)),
        out_shape=jax.ShapeDtypeStruct((rows, heads * width), jnp.float32),
        cost_estimate=pl.CostEstimate(
            flops=2 * rows * SEGMENT_LENGTH * (heads * width + size),
            bytes_accessed=rows * heads * width * 6,
            transcendentals=rows * SEGMENT_LENGTH * heads,
        ),
    )(
        skip_gain,
        c_part,
        b_part,
        xconv,
        columns_by_group(cum_heads, spans, heads),
        by_group(cum_heads, spans, heads),
        by_group(step_heads, spans, heads),
    )


def gate_terms(partial, c_part, state_enter, ecum, gate_in, spans, heads, width, offset):
    rows = partial.shape[0]
    size = c_part.shape[1]
    group = HEAD_GROUP
    return pl.pallas_call(
        gate_kernel,
        grid=(spans, heads // group),
        in_specs=[
            pl.BlockSpec((SEGMENT_LENGTH, group * width), lambda c, g: (c, g)),
            pl.BlockSpec((SEGMENT_LENGTH, size), lambda c, g: (c, 0)),
            pl.BlockSpec((1, group, size, width), lambda c, g: (c, g, 0, 0)),
            pl.BlockSpec((1, 1, SEGMENT_LENGTH, group), lambda c, g: (c, g, 0, 0)),
            pl.BlockSpec((SEGMENT_LENGTH, group * width), lambda c, g: (c, g + offset)),
        ],
        out_specs=[
            pl.BlockSpec((SEGMENT_LENGTH, group * width), lambda c, g: (c, g)),
            pl.BlockSpec((SEGMENT_LENGTH, 1), lambda c, g: (c, 0)),
        ],
        out_shape=[
            jax.ShapeDtypeStruct((rows, heads * width), jnp.float32),
            jax.ShapeDtypeStruct((rows, 1), jnp.float32),
        ],
        cost_estimate=pl.CostEstimate(
            flops=6 * rows * size * heads * width,
            bytes_accessed=rows * heads * width * 10,
            transcendentals=rows * heads * width,
        ),
    )(partial, c_part, state_enter, columns_by_group(ecum, spans, heads), gate_in)


def local(
    xin,
    gate_in,
    bc_proj,
    dt_raw,
    dt_bias,
    rate,
    skip_gain,
    conv_x,
    conv_bc,
    norm_gain,
    valid_blocks,
):
    row_count, channels = xin.shape
    head_count = dt_raw.shape[1]
    head_size = channels // head_count
    span_count = row_count // SEGMENT_LENGTH
    kernel_taps = conv_x.shape[0]
    live_rows = valid_blocks[0] * BLOCK
    tail_x = lax.dynamic_slice_in_dim(xin, live_rows - (kernel_taps - 1), kernel_taps - 1, 0)
    tail_bc = lax.dynamic_slice_in_dim(bc_proj, live_rows - (kernel_taps - 1), kernel_taps - 1, 0)
    prev_x, prev_bc = passed_along((tail_x, tail_bc), "seq", 1)
    lead = 8
    edges = jnp.concatenate(
        [prev_x[None], xin.reshape(span_count, SEGMENT_LENGTH, channels)[:-1, -(kernel_taps - 1) :]],
        axis=0,
    )
    halo = jnp.pad(edges, ((0, 0), (lead - (kernel_taps - 1), 0), (0, 0)))
    bc_local = conv_silu(bc_proj, prev_bc, conv_bc)
    bc_full = lax.all_gather(bc_local, "ch", axis=1, tiled=True)
    state_size = bc_full.shape[1] // 2
    b_part = bc_full[:, :state_size]
    c_part = bc_full[:, state_size:]
    b_t = b_part.reshape(span_count, SEGMENT_LENGTH, state_size).transpose(0, 2, 1)
    row_valid = (jnp.arange(row_count) < live_rows).astype(jnp.float32)
    step_size = jax.nn.softplus(dt_raw + dt_bias[None, :]) * row_valid[:, None]
    step_three = step_size.reshape(span_count, SEGMENT_LENGTH, head_count)
    cumul = jnp.cumsum(-rate[None, None, :] * step_three, axis=1)
    cum_heads = jnp.transpose(cumul, (0, 2, 1))
    step_heads = jnp.transpose(step_three, (0, 2, 1))
    last_cum = cum_heads[:, :, -1]
    to_end = jnp.exp(last_cum[:, :, None] - cum_heads) * step_heads
    block_decay = jnp.exp(last_cum)
    halves = 1
    part_heads = head_count // halves
    gated_parts = []
    square_part = None
    for part in range(halves):
        heads = slice(part * part_heads, (part + 1) * part_heads)
        offset = part * part_heads // HEAD_GROUP
        block_state, xconv = block_states(
            xin, halo, conv_x, b_t, to_end[:, heads], span_count, part_heads, head_size, offset
        )
        current = jnp.zeros((part_heads, state_size, head_size), jnp.float32)
        factor = jnp.ones((part_heads,), jnp.float32)
        local_enter = []
        factor_list = []
        for index in range(span_count):
            local_enter.append(current)
            factor_list.append(factor)
            current = block_decay[index, heads][:, None, None] * current + block_state[index]
            factor = factor * block_decay[index, heads]
        group_state, xconv = scan_states(factor, current, "seq", xconv)
        partial = intra_terms(
            skip_gain[heads],
            c_part,
            b_part,
            xconv,
            cum_heads[:, heads],
            step_heads[:, heads],
            span_count,
            part_heads,
            head_size,
        )
        state_enter = jnp.stack(
            [
                local_enter[index] + factor_list[index][:, None, None] * group_state
                for index in range(span_count)
            ],
            axis=0,
        )
        gated, squares = gate_terms(
            partial,
            c_part,
            state_enter,
            jnp.exp(cum_heads[:, heads]),
            gate_in,
            span_count,
            part_heads,
            head_size,
            offset,
        )
        gated_parts.append(gated)
        square_part = squares if square_part is None else square_part + squares
    gated = jnp.concatenate(gated_parts, axis=1)
    square_sum = lax.psum(square_part[:, 0], "ch")
    mean_sq = square_sum / INNER
    normed = gated * lax.rsqrt(mean_sq + 1e-05)[:, None] * norm_gain[None, :] * row_valid[:, None]
    return normed.astype(jnp.bfloat16)


def solution(mesh):
    placed = (
        P("seq", "ch"),
        P("seq", "ch"),
        P("seq", "ch"),
        P("seq", "ch"),
        P("ch"),
        P("ch"),
        P("ch"),
        P(None, "ch"),
        P(None, "ch"),
        P("ch"),
        P("seq"),
    )
    return jax.shard_map(
        local, mesh=mesh, in_specs=placed, out_specs=P("seq", "ch"), check_vma=False
    )
```

```python
import functools

import jax
import jax.numpy as jnp
from jax import lax
from jax.experimental import pallas as pl
from jax.experimental.pallas import tpu as pltpu
from jax.sharding import PartitionSpec as P

SEGMENT_LENGTH = 256
BLOCK = 128
INNER = 16384


def passed_along(block, axis, distance):
    devices = range(lax.axis_size(axis))
    route = [(i - distance, i) for i in devices if i - distance in devices]
    return lax.ppermute(block, axis, route)


def scan_states(factor, state, axis, tied):
    count = lax.axis_size(axis)
    split = count % 2 == 0 and count >= 4
    members = count // 2 if split else count
    groups = [list(range(0, members)), list(range(members, count))] if split else None
    heads, size, width = state.shape
    piece = size // members
    parts = state.reshape(heads, members, piece, width).transpose(1, 0, 2, 3)
    slot = jnp.zeros((piece, width), jnp.float32).at[0, :heads].set(factor)
    payload = jnp.concatenate(
        [parts, jnp.broadcast_to(slot, (members, 1, piece, width))], axis=1
    )
    got = lax.all_to_all(payload, axis, 0, 0, tiled=True, axis_index_groups=groups)
    decays = got[:, heads, 0, :heads]
    tied = lax.optimization_barrier((tied, got))[0]
    running = jnp.zeros((heads, piece, width), jnp.float32)
    entries = []
    for index in range(members):
        entries.append(running)
        running = decays[index][:, None, None] * running + got[index, :heads]
    if split:
        route = [(i, i + members) for i in range(members)]
        earlier = lax.ppermute(running, axis, route)
        carry = jnp.ones((heads,), jnp.float32)
        for index in range(members):
            entries[index] = entries[index] + carry[:, None, None] * earlier
            carry = carry * decays[index]
    back = lax.all_to_all(
        jnp.stack(entries, axis=0), axis, 0, 0, tiled=True, axis_index_groups=groups
    )
    return back.transpose(1, 0, 2, 3).reshape(heads, size, width), tied


def conv_silu(signal, tail_rows, weights):
    stacked = jnp.concatenate([tail_rows, signal], axis=0)
    kernel_taps = weights.shape[0]
    length = signal.shape[0]
    accum = jnp.zeros(signal.shape, jnp.float32)
    for offset in range(kernel_taps):
        accum = accum + weights[offset].astype(jnp.float32) * stacked[
            offset : offset + length
        ].astype(jnp.float32)
    return jax.nn.silu(accum).astype(jnp.bfloat16)


HEAD_GROUP = 8


def state_kernel(x_ref, halo_ref, taps_ref, bt_ref, toend_ref, out_ref, conv_ref):
    width = out_ref.shape[-1]
    taps = taps_ref[...].astype(jnp.float32)
    kernel_taps = taps.shape[0]
    signal = x_ref[...].astype(jnp.float32)
    edge = halo_ref[0].astype(jnp.float32)
    lead = edge.shape[0]
    stacked = jnp.concatenate([edge, signal[:lead]], axis=0)
    accum = jnp.zeros(signal.shape, jnp.float32)
    head = jnp.zeros((lead, signal.shape[1]), jnp.float32)
    for offset in range(kernel_taps):
        shift = kernel_taps - 1 - offset
        moved = signal if shift == 0 else pltpu.roll(signal, shift, 0)
        accum = accum + taps[offset : offset + 1] * moved
        head = head + taps[offset : offset + 1] * stacked[lead - shift : 2 * lead - shift]
    conv_ref[...] = (accum / (1.0 + jnp.exp(-accum))).astype(jnp.bfloat16)
    conv_ref[:lead, :] = (head / (1.0 + jnp.exp(-head))).astype(jnp.bfloat16)
    bt = bt_ref[0]
    for j in range(out_ref.shape[1]):
        x = conv_ref[:, j * width : (j + 1) * width].astype(jnp.float32)
        xw = (x * toend_ref[0, 0, :, j : j + 1]).astype(jnp.bfloat16)
        out_ref[0, j] = jnp.dot(bt, xw, preferred_element_type=jnp.float32)


def intra_kernel(skip_ref, c_ref, b_ref, x_ref, cumc_ref, cumr_ref, stepr_ref, out_ref):
    group = pl.program_id(1)
    heads = cumc_ref.shape[-1]
    width = out_ref.shape[-1] // heads
    scores = lax.dot_general(
        c_ref[...], b_ref[...], (((1,), (1,)), ((), ())), preferred_element_type=jnp.float32
    )
    length = scores.shape[0]
    rows = lax.broadcasted_iota(jnp.int32, (length, length), 0)
    cols = lax.broadcasted_iota(jnp.int32, (length, length), 1)
    causal = rows >= cols
    for j in range(heads):
        diff = cumc_ref[0, 0, :, j : j + 1] - cumr_ref[0, 0, j : j + 1, :]
        decay = jnp.where(causal, jnp.exp(jnp.where(causal, diff, 0.0)), 0.0)
        weights = (scores * decay * stepr_ref[0, 0, j : j + 1, :]).astype(jnp.bfloat16)
        x = x_ref[:, j * width : (j + 1) * width]
        intra = jnp.dot(weights, x, preferred_element_type=jnp.float32)
        out_ref[:, j * width : (j + 1) * width] = (
            intra + skip_ref[group * heads + j] * x.astype(jnp.float32)
        )


def gate_kernel(decay_ref, part_ref, c_ref, block_ref, group_ref, ecum_ref, z_ref, out_ref, sq_ref):
    group = pl.program_id(0)
    span = pl.program_id(1)
    spans = block_ref.shape[0]
    heads = ecum_ref.shape[-1]
    head_count = decay_ref.shape[0] // spans
    width = out_ref.shape[-1] // heads
    c = c_ref[...]
    total = jnp.zeros((c.shape[0], width), jnp.float32)
    for j in range(heads):
        head = group * heads + j
        local_state = jnp.zeros(block_ref.shape[2:], jnp.float32)
        factor = jnp.float32(1.0)
        for earlier in range(spans - 1):
            decay = decay_ref[earlier * head_count + head]
            take = earlier < span
            local_state = jnp.where(
                take, decay * local_state + block_ref[earlier, j], local_state
            )
            factor = jnp.where(take, factor * decay, factor)
        state = local_state + factor * group_ref[j]
        high = state.astype(jnp.bfloat16)
        rest = state - high.astype(jnp.float32)
        mid = rest.astype(jnp.bfloat16)
        low = (rest - mid.astype(jnp.float32)).astype(jnp.bfloat16)
        inter = (
            jnp.dot(c, high, preferred_element_type=jnp.float32)
            + jnp.dot(c, mid, preferred_element_type=jnp.float32)
            + jnp.dot(c, low, preferred_element_type=jnp.float32)
        )
        columns = slice(j * width, (j + 1) * width)
        y = part_ref[:, columns] + inter * ecum_ref[0, 0, :, j : j + 1]
        z = z_ref[:, columns].astype(jnp.float32)
        gated = y * (z / (1.0 + jnp.exp(-z)))
        out_ref[:, columns] = gated
        total = total + gated * gated
    sq_ref[0] = jnp.sum(total, axis=1, keepdims=True)


def by_group(values, spans, heads):
    return values.reshape(spans, heads // HEAD_GROUP, HEAD_GROUP, -1)


def columns_by_group(values, spans, heads):
    return by_group(values, spans, heads).transpose(0, 1, 3, 2)


def block_states(xin, halo, conv_x, b_t, to_end, spans, heads, width, offset):
    rows = xin.shape[0]
    size = b_t.shape[1]
    group = HEAD_GROUP
    lead = halo.shape[1]
    kernel_taps = conv_x.shape[0]
    return pl.pallas_call(
        state_kernel,
        grid=(spans, heads // group),
        in_specs=[
            pl.BlockSpec((SEGMENT_LENGTH, group * width), lambda c, g: (c, g + offset)),
            pl.BlockSpec((1, lead, group * width), lambda c, g: (c, 0, g + offset)),
            pl.BlockSpec((kernel_taps, group * width), lambda c, g: (0, g + offset)),
            pl.BlockSpec((1, size, SEGMENT_LENGTH), lambda c, g: (c, 0, 0)),
            pl.BlockSpec((1, 1, SEGMENT_LENGTH, group), lambda c, g: (c, g, 0, 0)),
        ],
        out_specs=[
            pl.BlockSpec((1, group, size, width), lambda c, g: (c, g, 0, 0)),
            pl.BlockSpec((SEGMENT_LENGTH, group * width), lambda c, g: (c, g)),
        ],
        out_shape=[
            jax.ShapeDtypeStruct((spans, heads, size, width), jnp.float32),
            jax.ShapeDtypeStruct((rows, heads * width), jnp.bfloat16),
        ],
        cost_estimate=pl.CostEstimate(
            flops=2 * rows * heads * width * size,
            bytes_accessed=rows * heads * width * 4 + spans * heads * size * width * 4,
            transcendentals=rows * heads * width,
        ),
    )(xin, halo, conv_x, b_t, columns_by_group(to_end, spans, heads))


def intra_terms(skip_gain, c_part, b_part, xconv, cum_heads, step_heads, spans, heads, width):
    rows = xconv.shape[0]
    size = c_part.shape[1]
    group = HEAD_GROUP
    return pl.pallas_call(
        intra_kernel,
        grid=(spans, heads // group),
        in_specs=[
            pl.BlockSpec(memory_space=pltpu.SMEM),
            pl.BlockSpec((SEGMENT_LENGTH, size), lambda c, g: (c, 0)),
            pl.BlockSpec((SEGMENT_LENGTH, size), lambda c, g: (c, 0)),
            pl.BlockSpec((SEGMENT_LENGTH, group * width), lambda c, g: (c, g)),
            pl.BlockSpec((1, 1, SEGMENT_LENGTH, group), lambda c, g: (c, g, 0, 0)),
            pl.BlockSpec((1, 1, group, SEGMENT_LENGTH), lambda c, g: (c, g, 0, 0)),
            pl.BlockSpec((1, 1, group, SEGMENT_LENGTH), lambda c, g: (c, g, 0, 0)),
        ],
        out_specs=pl.BlockSpec((SEGMENT_LENGTH, group * width), lambda c, g: (c, g)),
        out_shape=jax.ShapeDtypeStruct((rows, heads * width), jnp.float32),
        cost_estimate=pl.CostEstimate(
            flops=2 * rows * SEGMENT_LENGTH * (heads * width + size),
            bytes_accessed=rows * heads * width * 6,
            transcendentals=rows * SEGMENT_LENGTH * heads,
        ),
    )(
        skip_gain,
        c_part,
        b_part,
        xconv,
        columns_by_group(cum_heads, spans, heads),
        by_group(cum_heads, spans, heads),
        by_group(step_heads, spans, heads),
    )


def gate_terms(
    block_decay, partial, c_part, block_state, group_state, ecum, gate_in, spans, heads, width, offset
):
    rows = partial.shape[0]
    size = c_part.shape[1]
    group = HEAD_GROUP
    groups = heads // group
    return pl.pallas_call(
        gate_kernel,
        grid=(groups, spans),
        in_specs=[
            pl.BlockSpec(memory_space=pltpu.SMEM),
            pl.BlockSpec((SEGMENT_LENGTH, group * width), lambda g, c: (c, g)),
            pl.BlockSpec((SEGMENT_LENGTH, size), lambda g, c: (c, 0)),
            pl.BlockSpec((spans, group, size, width), lambda g, c: (0, g, 0, 0)),
            pl.BlockSpec((group, size, width), lambda g, c: (g, 0, 0)),
            pl.BlockSpec((1, 1, SEGMENT_LENGTH, group), lambda g, c: (c, g, 0, 0)),
            pl.BlockSpec((SEGMENT_LENGTH, group * width), lambda g, c: (c, g + offset)),
        ],
        out_specs=[
            pl.BlockSpec((SEGMENT_LENGTH, group * width), lambda g, c: (c, g)),
            pl.BlockSpec((1, SEGMENT_LENGTH, 1), lambda g, c: (g, c, 0)),
        ],
        out_shape=[
            jax.ShapeDtypeStruct((rows, heads * width), jnp.float32),
            jax.ShapeDtypeStruct((groups, rows, 1), jnp.float32),
        ],
        compiler_params=pltpu.CompilerParams(vmem_limit_bytes=48 * 1024 * 1024),
        cost_estimate=pl.CostEstimate(
            flops=6 * rows * size * heads * width,
            bytes_accessed=rows * heads * width * 10,
            transcendentals=rows * heads * width,
        ),
    )(
        block_decay.reshape(-1),
        partial,
        c_part,
        block_state,
        group_state,
        columns_by_group(ecum, spans, heads),
        gate_in,
    )


def local(
    xin,
    gate_in,
    bc_proj,
    dt_raw,
    dt_bias,
    rate,
    skip_gain,
    conv_x,
    conv_bc,
    norm_gain,
    valid_blocks,
):
    row_count, channels = xin.shape
    head_count = dt_raw.shape[1]
    head_size = channels // head_count
    span_count = row_count // SEGMENT_LENGTH
    kernel_taps = conv_x.shape[0]
    live_rows = valid_blocks[0] * BLOCK
    tail_x = lax.dynamic_slice_in_dim(xin, live_rows - (kernel_taps - 1), kernel_taps - 1, 0)
    tail_bc = lax.dynamic_slice_in_dim(bc_proj, live_rows - (kernel_taps - 1), kernel_taps - 1, 0)
    prev = passed_along(jnp.concatenate([tail_x, tail_bc], axis=1), "seq", 1)
    prev_x, prev_bc = prev[:, :channels], prev[:, channels:]
    lead = 8
    edges = jnp.concatenate(
        [prev_x[None], xin.reshape(span_count, SEGMENT_LENGTH, channels)[:-1, -(kernel_taps - 1) :]],
        axis=0,
    )
    halo = jnp.pad(edges, ((0, 0), (lead - (kernel_taps - 1), 0), (0, 0)))
    bc_local = conv_silu(bc_proj, prev_bc, conv_bc)
    bc_full = lax.all_gather(bc_local, "ch", axis=1, tiled=True)
    state_size = bc_full.shape[1] // 2
    b_part = bc_full[:, :state_size]
    c_part = bc_full[:, state_size:]
    b_t = b_part.reshape(span_count, SEGMENT_LENGTH, state_size).transpose(0, 2, 1)
    row_valid = (jnp.arange(row_count) < live_rows).astype(jnp.float32)
    step_size = jax.nn.softplus(dt_raw + dt_bias[None, :]) * row_valid[:, None]
    step_three = step_size.reshape(span_count, SEGMENT_LENGTH, head_count)
    cumul = jnp.cumsum(-rate[None, None, :] * step_three, axis=1)
    cum_heads = jnp.transpose(cumul, (0, 2, 1))
    step_heads = jnp.transpose(step_three, (0, 2, 1))
    last_cum = cum_heads[:, :, -1]
    to_end = jnp.exp(last_cum[:, :, None] - cum_heads) * step_heads
    block_decay = jnp.exp(last_cum)
    halves = 1
    part_heads = head_count // halves
    gated_parts = []
    square_part = None
    for part in range(halves):
        heads = slice(part * part_heads, (part + 1) * part_heads)
        offset = part * part_heads // HEAD_GROUP
        block_state, xconv = block_states(
            xin, halo, conv_x, b_t, to_end[:, heads], span_count, part_heads, head_size, offset
        )
        current = jnp.zeros((part_heads, state_size, head_size), jnp.float32)
        factor = jnp.ones((part_heads,), jnp.float32)
        local_enter = []
        factor_list = []
        for index in range(span_count):
            local_enter.append(current)
            factor_list.append(factor)
            current = block_decay[index, heads][:, None, None] * current + block_state[index]
            factor = factor * block_decay[index, heads]
        group_state, xconv = scan_states(factor, current, "seq", xconv)
        partial = intra_terms(
            skip_gain[heads],
            c_part,
            b_part,
            xconv,
            cum_heads[:, heads],
            step_heads[:, heads],
            span_count,
            part_heads,
            head_size,
        )
        gated, squares = gate_terms(
            block_decay[:, heads],
            partial,
            c_part,
            block_state,
            group_state,
            jnp.exp(cum_heads[:, heads]),
            gate_in,
            span_count,
            part_heads,
            head_size,
            offset,
        )
        squares = jnp.sum(squares, axis=0)
        gated_parts.append(gated)
        square_part = squares if square_part is None else square_part + squares
    gated = jnp.concatenate(gated_parts, axis=1)
    square_sum = lax.psum(square_part[:, 0], "ch")
    mean_sq = square_sum / INNER
    normed = gated * lax.rsqrt(mean_sq + 1e-05)[:, None] * norm_gain[None, :] * row_valid[:, None]
    return normed.astype(jnp.bfloat16)


def solution(mesh):
    placed = (
        P("seq", "ch"),
        P("seq", "ch"),
        P("seq", "ch"),
        P("seq", "ch"),
        P("ch"),
        P("ch"),
        P("ch"),
        P(None, "ch"),
        P(None, "ch"),
        P("ch"),
        P("seq"),
    )
    return jax.shard_map(
        local, mesh=mesh, in_specs=placed, out_specs=P("seq", "ch"), check_vma=False
    )
```

```python
import functools

import jax
import jax.numpy as jnp
from jax import lax
from jax.experimental import pallas as pl
from jax.experimental.pallas import tpu as pltpu
from jax.sharding import PartitionSpec as P

SEGMENT_LENGTH = 256
BLOCK = 128
INNER = 16384


def passed_along(block, axis, distance):
    devices = range(lax.axis_size(axis))
    route = [(i - distance, i) for i in devices if i - distance in devices]
    return lax.ppermute(block, axis, route)


def scan_states(factor, state, axis, tied):
    count = lax.axis_size(axis)
    split = count % 2 == 0 and count >= 4
    members = count // 2 if split else count
    groups = [list(range(0, members)), list(range(members, count))] if split else None
    heads, size, width = state.shape
    piece = size // members
    parts = state.reshape(heads, members, piece, width).transpose(1, 0, 2, 3)
    slot = jnp.zeros((piece, width), jnp.float32).at[0, :heads].set(factor)
    payload = jnp.concatenate(
        [parts, jnp.broadcast_to(slot, (members, 1, piece, width))], axis=1
    )
    got = lax.all_to_all(payload, axis, 0, 0, tiled=True, axis_index_groups=groups)
    decays = got[:, heads, 0, :heads]
    tied = lax.optimization_barrier((tied, got))[0]
    running = jnp.zeros((heads, piece, width), jnp.float32)
    entries = []
    for index in range(members):
        entries.append(running)
        running = decays[index][:, None, None] * running + got[index, :heads]
    if split:
        route = [(i, i + members) for i in range(members)]
        earlier = lax.ppermute(running, axis, route)
        carry = jnp.ones((heads,), jnp.float32)
        for index in range(members):
            entries[index] = entries[index] + carry[:, None, None] * earlier
            carry = carry * decays[index]
    back = lax.all_to_all(
        jnp.stack(entries, axis=0), axis, 0, 0, tiled=True, axis_index_groups=groups
    )
    return back.transpose(1, 0, 2, 3).reshape(heads, size, width), tied


def conv_silu(signal, tail_rows, weights):
    stacked = jnp.concatenate([tail_rows, signal], axis=0)
    kernel_taps = weights.shape[0]
    length = signal.shape[0]
    accum = jnp.zeros(signal.shape, jnp.float32)
    for offset in range(kernel_taps):
        accum = accum + weights[offset].astype(jnp.float32) * stacked[
            offset : offset + length
        ].astype(jnp.float32)
    return jax.nn.silu(accum).astype(jnp.bfloat16)


HEAD_GROUP = 8


def silu(value):
    half = 0.5 * value
    return half + half * jnp.tanh(half)


def state_kernel(x_ref, halo_ref, taps_ref, bt_ref, toend_ref, out_ref, conv_ref):
    width = out_ref.shape[-1]
    taps = taps_ref[...].astype(jnp.float32)
    kernel_taps = taps.shape[0]
    signal = x_ref[...].astype(jnp.float32)
    edge = halo_ref[0].astype(jnp.float32)
    lead = edge.shape[0]
    stacked = jnp.concatenate([edge, signal[:lead]], axis=0)
    accum = jnp.zeros(signal.shape, jnp.float32)
    head = jnp.zeros((lead, signal.shape[1]), jnp.float32)
    for offset in range(kernel_taps):
        shift = kernel_taps - 1 - offset
        moved = signal if shift == 0 else pltpu.roll(signal, shift, 0)
        accum = accum + taps[offset : offset + 1] * moved
        head = head + taps[offset : offset + 1] * stacked[lead - shift : 2 * lead - shift]
    conv_ref[...] = silu(accum).astype(jnp.bfloat16)
    conv_ref[:lead, :] = silu(head).astype(jnp.bfloat16)
    bt = bt_ref[0]
    for j in range(out_ref.shape[1]):
        x = conv_ref[:, j * width : (j + 1) * width].astype(jnp.float32)
        xw = (x * toend_ref[0, 0, :, j : j + 1]).astype(jnp.bfloat16)
        out_ref[0, j] = jnp.dot(bt, xw, preferred_element_type=jnp.float32)


def intra_kernel(skip_ref, c_ref, b_ref, x_ref, cumc_ref, cumr_ref, stepr_ref, out_ref):
    group = pl.program_id(1)
    heads = cumc_ref.shape[-1]
    width = out_ref.shape[-1] // heads
    scores = lax.dot_general(
        c_ref[...], b_ref[...], (((1,), (1,)), ((), ())), preferred_element_type=jnp.float32
    )
    length = scores.shape[0]
    rows = lax.broadcasted_iota(jnp.int32, (length, length), 0)
    cols = lax.broadcasted_iota(jnp.int32, (length, length), 1)
    causal = rows >= cols
    for j in range(heads):
        diff = cumc_ref[0, 0, :, j : j + 1] - cumr_ref[0, 0, j : j + 1, :]
        decay = jnp.where(causal, jnp.exp(jnp.where(causal, diff, 0.0)), 0.0)
        weights = (scores * decay * stepr_ref[0, 0, j : j + 1, :]).astype(jnp.bfloat16)
        x = x_ref[:, j * width : (j + 1) * width]
        intra = jnp.dot(weights, x, preferred_element_type=jnp.float32)
        out_ref[:, j * width : (j + 1) * width] = (
            intra + skip_ref[group * heads + j] * x.astype(jnp.float32)
        )


def gate_kernel(decay_ref, part_ref, c_ref, block_ref, group_ref, ecum_ref, z_ref, out_ref, sq_ref):
    group = pl.program_id(0)
    span = pl.program_id(1)
    spans = block_ref.shape[0]
    heads = ecum_ref.shape[-1]
    head_count = decay_ref.shape[0] // spans
    width = out_ref.shape[-1] // heads
    c = c_ref[...]
    total = jnp.zeros((c.shape[0], width), jnp.float32)
    for j in range(heads):
        head = group * heads + j
        local_state = jnp.zeros(block_ref.shape[2:], jnp.float32)
        factor = jnp.float32(1.0)
        for earlier in range(spans - 1):
            decay = decay_ref[earlier * head_count + head]
            take = earlier < span
            local_state = jnp.where(
                take, decay * local_state + block_ref[earlier, j], local_state
            )
            factor = jnp.where(take, factor * decay, factor)
        state = local_state + factor * group_ref[j]
        high = state.astype(jnp.bfloat16)
        rest = state - high.astype(jnp.float32)
        mid = rest.astype(jnp.bfloat16)
        low = (rest - mid.astype(jnp.float32)).astype(jnp.bfloat16)
        inter = (
            jnp.dot(c, high, preferred_element_type=jnp.float32)
            + jnp.dot(c, mid, preferred_element_type=jnp.float32)
            + jnp.dot(c, low, preferred_element_type=jnp.float32)
        )
        columns = slice(j * width, (j + 1) * width)
        y = part_ref[:, columns] + inter * ecum_ref[0, 0, :, j : j + 1]
        z = z_ref[:, columns].astype(jnp.float32)
        gated = y * silu(z)
        out_ref[:, columns] = gated
        total = total + gated * gated
    sq_ref[0] = jnp.sum(total, axis=1, keepdims=True)


def by_group(values, spans, heads):
    return values.reshape(spans, heads // HEAD_GROUP, HEAD_GROUP, -1)


def columns_by_group(values, spans, heads):
    return by_group(values, spans, heads).transpose(0, 1, 3, 2)


def block_states(xin, halo, conv_x, b_t, to_end, spans, heads, width, offset):
    rows = xin.shape[0]
    size = b_t.shape[1]
    group = HEAD_GROUP
    lead = halo.shape[1]
    kernel_taps = conv_x.shape[0]
    return pl.pallas_call(
        state_kernel,
        grid=(spans, heads // group),
        in_specs=[
            pl.BlockSpec((SEGMENT_LENGTH, group * width), lambda c, g: (c, g + offset)),
            pl.BlockSpec((1, lead, group * width), lambda c, g: (c, 0, g + offset)),
            pl.BlockSpec((kernel_taps, group * width), lambda c, g: (0, g + offset)),
            pl.BlockSpec((1, size, SEGMENT_LENGTH), lambda c, g: (c, 0, 0)),
            pl.BlockSpec((1, 1, SEGMENT_LENGTH, group), lambda c, g: (c, g, 0, 0)),
        ],
        out_specs=[
            pl.BlockSpec((1, group, size, width), lambda c, g: (c, g, 0, 0)),
            pl.BlockSpec((SEGMENT_LENGTH, group * width), lambda c, g: (c, g)),
        ],
        out_shape=[
            jax.ShapeDtypeStruct((spans, heads, size, width), jnp.float32),
            jax.ShapeDtypeStruct((rows, heads * width), jnp.bfloat16),
        ],
        cost_estimate=pl.CostEstimate(
            flops=2 * rows * heads * width * size,
            bytes_accessed=rows * heads * width * 4 + spans * heads * size * width * 4,
            transcendentals=rows * heads * width,
        ),
    )(xin, halo, conv_x, b_t, columns_by_group(to_end, spans, heads))


def intra_terms(skip_gain, c_part, b_part, xconv, cum_heads, step_heads, spans, heads, width):
    rows = xconv.shape[0]
    size = c_part.shape[1]
    group = HEAD_GROUP
    return pl.pallas_call(
        intra_kernel,
        grid=(spans, heads // group),
        in_specs=[
            pl.BlockSpec(memory_space=pltpu.SMEM),
            pl.BlockSpec((SEGMENT_LENGTH, size), lambda c, g: (c, 0)),
            pl.BlockSpec((SEGMENT_LENGTH, size), lambda c, g: (c, 0)),
            pl.BlockSpec((SEGMENT_LENGTH, group * width), lambda c, g: (c, g)),
            pl.BlockSpec((1, 1, SEGMENT_LENGTH, group), lambda c, g: (c, g, 0, 0)),
            pl.BlockSpec((1, 1, group, SEGMENT_LENGTH), lambda c, g: (c, g, 0, 0)),
            pl.BlockSpec((1, 1, group, SEGMENT_LENGTH), lambda c, g: (c, g, 0, 0)),
        ],
        out_specs=pl.BlockSpec((SEGMENT_LENGTH, group * width), lambda c, g: (c, g)),
        out_shape=jax.ShapeDtypeStruct((rows, heads * width), jnp.float32),
        cost_estimate=pl.CostEstimate(
            flops=2 * rows * SEGMENT_LENGTH * (heads * width + size),
            bytes_accessed=rows * heads * width * 6,
            transcendentals=rows * SEGMENT_LENGTH * heads,
        ),
    )(
        skip_gain,
        c_part,
        b_part,
        xconv,
        columns_by_group(cum_heads, spans, heads),
        by_group(cum_heads, spans, heads),
        by_group(step_heads, spans, heads),
    )


def gate_terms(
    block_decay, partial, c_part, block_state, group_state, ecum, gate_in, spans, heads, width, offset
):
    rows = partial.shape[0]
    size = c_part.shape[1]
    group = HEAD_GROUP
    groups = heads // group
    return pl.pallas_call(
        gate_kernel,
        grid=(groups, spans),
        in_specs=[
            pl.BlockSpec(memory_space=pltpu.SMEM),
            pl.BlockSpec((SEGMENT_LENGTH, group * width), lambda g, c: (c, g)),
            pl.BlockSpec((SEGMENT_LENGTH, size), lambda g, c: (c, 0)),
            pl.BlockSpec((spans, group, size, width), lambda g, c: (0, g, 0, 0)),
            pl.BlockSpec((group, size, width), lambda g, c: (g, 0, 0)),
            pl.BlockSpec((1, 1, SEGMENT_LENGTH, group), lambda g, c: (c, g, 0, 0)),
            pl.BlockSpec((SEGMENT_LENGTH, group * width), lambda g, c: (c, g + offset)),
        ],
        out_specs=[
            pl.BlockSpec((SEGMENT_LENGTH, group * width), lambda g, c: (c, g)),
            pl.BlockSpec((1, SEGMENT_LENGTH, 1), lambda g, c: (g, c, 0)),
        ],
        out_shape=[
            jax.ShapeDtypeStruct((rows, heads * width), jnp.float32),
            jax.ShapeDtypeStruct((groups, rows, 1), jnp.float32),
        ],
        compiler_params=pltpu.CompilerParams(vmem_limit_bytes=48 * 1024 * 1024),
        cost_estimate=pl.CostEstimate(
            flops=6 * rows * size * heads * width,
            bytes_accessed=rows * heads * width * 10,
            transcendentals=rows * heads * width,
        ),
    )(
        block_decay.reshape(-1),
        partial,
        c_part,
        block_state,
        group_state,
        columns_by_group(ecum, spans, heads),
        gate_in,
    )


def local(
    xin,
    gate_in,
    bc_proj,
    dt_raw,
    dt_bias,
    rate,
    skip_gain,
    conv_x,
    conv_bc,
    norm_gain,
    valid_blocks,
):
    row_count, channels = xin.shape
    head_count = dt_raw.shape[1]
    head_size = channels // head_count
    span_count = row_count // SEGMENT_LENGTH
    kernel_taps = conv_x.shape[0]
    live_rows = valid_blocks[0] * BLOCK
    tail_x = lax.dynamic_slice_in_dim(xin, live_rows - (kernel_taps - 1), kernel_taps - 1, 0)
    tail_bc = lax.dynamic_slice_in_dim(bc_proj, live_rows - (kernel_taps - 1), kernel_taps - 1, 0)
    prev = passed_along(jnp.concatenate([tail_x, tail_bc], axis=1), "seq", 1)
    prev_x, prev_bc = prev[:, :channels], prev[:, channels:]
    lead = 8
    edges = jnp.concatenate(
        [prev_x[None], xin.reshape(span_count, SEGMENT_LENGTH, channels)[:-1, -(kernel_taps - 1) :]],
        axis=0,
    )
    halo = jnp.pad(edges, ((0, 0), (lead - (kernel_taps - 1), 0), (0, 0)))
    bc_local = conv_silu(bc_proj, prev_bc, conv_bc)
    bc_full = lax.all_gather(bc_local, "ch", axis=1, tiled=True)
    state_size = bc_full.shape[1] // 2
    b_part = bc_full[:, :state_size]
    c_part = bc_full[:, state_size:]
    b_t = b_part.reshape(span_count, SEGMENT_LENGTH, state_size).transpose(0, 2, 1)
    row_valid = (jnp.arange(row_count) < live_rows).astype(jnp.float32)
    step_size = jax.nn.softplus(dt_raw + dt_bias[None, :]) * row_valid[:, None]
    step_three = step_size.reshape(span_count, SEGMENT_LENGTH, head_count)
    cumul = jnp.cumsum(-rate[None, None, :] * step_three, axis=1)
    cum_heads = jnp.transpose(cumul, (0, 2, 1))
    step_heads = jnp.transpose(step_three, (0, 2, 1))
    last_cum = cum_heads[:, :, -1]
    to_end = jnp.exp(last_cum[:, :, None] - cum_heads) * step_heads
    block_decay = jnp.exp(last_cum)
    halves = 1
    part_heads = head_count // halves
    gated_parts = []
    square_part = None
    for part in range(halves):
        heads = slice(part * part_heads, (part + 1) * part_heads)
        offset = part * part_heads // HEAD_GROUP
        block_state, xconv = block_states(
            xin, halo, conv_x, b_t, to_end[:, heads], span_count, part_heads, head_size, offset
        )
        current = jnp.zeros((part_heads, state_size, head_size), jnp.float32)
        factor = jnp.ones((part_heads,), jnp.float32)
        local_enter = []
        factor_list = []
        for index in range(span_count):
            local_enter.append(current)
            factor_list.append(factor)
            current = block_decay[index, heads][:, None, None] * current + block_state[index]
            factor = factor * block_decay[index, heads]
        group_state, xconv = scan_states(factor, current, "seq", xconv)
        partial = intra_terms(
            skip_gain[heads],
            c_part,
            b_part,
            xconv,
            cum_heads[:, heads],
            step_heads[:, heads],
            span_count,
            part_heads,
            head_size,
        )
        gated, squares = gate_terms(
            block_decay[:, heads],
            partial,
            c_part,
            block_state,
            group_state,
            jnp.exp(cum_heads[:, heads]),
            gate_in,
            span_count,
            part_heads,
            head_size,
            offset,
        )
        squares = jnp.sum(squares, axis=0)
        gated_parts.append(gated)
        square_part = squares if square_part is None else square_part + squares
    gated = jnp.concatenate(gated_parts, axis=1)
    square_sum = lax.psum(square_part[:, 0], "ch")
    mean_sq = square_sum / INNER
    normed = gated * lax.rsqrt(mean_sq + 1e-05)[:, None] * norm_gain[None, :] * row_valid[:, None]
    return normed.astype(jnp.bfloat16)


def solution(mesh):
    placed = (
        P("seq", "ch"),
        P("seq", "ch"),
        P("seq", "ch"),
        P("seq", "ch"),
        P("ch"),
        P("ch"),
        P("ch"),
        P(None, "ch"),
        P(None, "ch"),
        P("ch"),
        P("seq"),
    )
    return jax.shard_map(
        local, mesh=mesh, in_specs=placed, out_specs=P("seq", "ch"), check_vma=False
    )
```

```python
import functools

import jax
import jax.numpy as jnp
from jax import lax
from jax.experimental import pallas as pl
from jax.experimental.pallas import tpu as pltpu
from jax.sharding import PartitionSpec as P

SEGMENT_LENGTH = 256
BLOCK = 128
INNER = 16384


def passed_along(block, axis, distance):
    devices = range(lax.axis_size(axis))
    route = [(i - distance, i) for i in devices if i - distance in devices]
    return lax.ppermute(block, axis, route)


def scan_states(decays, state, axis, tied):
    count = lax.axis_size(axis)
    split = count % 2 == 0 and count >= 4
    members = count // 2 if split else count
    groups = [list(range(0, members)), list(range(members, count))] if split else None
    heads, size, width = state.shape
    piece = size // members
    parts = state.reshape(heads, members, piece, width).transpose(1, 0, 2, 3)
    got = lax.all_to_all(parts, axis, 0, 0, tiled=True, axis_index_groups=groups)
    running = jnp.zeros((heads, piece, width), jnp.float32)
    entries = []
    for index in range(members):
        entries.append(running)
        running = decays[index][:, None, None] * running + got[index]
    running, tied = lax.optimization_barrier((running, tied))
    if split:
        route = [(i, i + members) for i in range(members)]
        earlier = lax.ppermute(running, axis, route)
        carry = jnp.ones((heads,), jnp.float32)
        for index in range(members):
            entries[index] = entries[index] + carry[:, None, None] * earlier
            carry = carry * decays[index]
    back = lax.all_to_all(
        jnp.stack(entries, axis=0), axis, 0, 0, tiled=True, axis_index_groups=groups
    )
    return back.transpose(1, 0, 2, 3).reshape(heads, size, width), tied


def conv_silu(signal, tail_rows, weights):
    stacked = jnp.concatenate([tail_rows, signal], axis=0)
    kernel_taps = weights.shape[0]
    length = signal.shape[0]
    accum = jnp.zeros(signal.shape, jnp.float32)
    for offset in range(kernel_taps):
        accum = accum + weights[offset].astype(jnp.float32) * stacked[
            offset : offset + length
        ].astype(jnp.float32)
    return jax.nn.silu(accum).astype(jnp.bfloat16)


HEAD_GROUP = 8


def silu(value):
    half = 0.5 * value
    return half + half * jnp.tanh(half)


def state_kernel(x_ref, halo_ref, taps_ref, bt_ref, toend_ref, out_ref, conv_ref):
    width = out_ref.shape[-1]
    taps = taps_ref[...].astype(jnp.float32)
    kernel_taps = taps.shape[0]
    signal = x_ref[...].astype(jnp.float32)
    edge = halo_ref[0].astype(jnp.float32)
    lead = edge.shape[0]
    stacked = jnp.concatenate([edge, signal[:lead]], axis=0)
    accum = jnp.zeros(signal.shape, jnp.float32)
    head = jnp.zeros((lead, signal.shape[1]), jnp.float32)
    for offset in range(kernel_taps):
        shift = kernel_taps - 1 - offset
        moved = signal if shift == 0 else pltpu.roll(signal, shift, 0)
        accum = accum + taps[offset : offset + 1] * moved
        head = head + taps[offset : offset + 1] * stacked[lead - shift : 2 * lead - shift]
    conv_ref[...] = silu(accum).astype(jnp.bfloat16)
    conv_ref[:lead, :] = silu(head).astype(jnp.bfloat16)
    bt = bt_ref[0]
    for j in range(out_ref.shape[1]):
        x = conv_ref[:, j * width : (j + 1) * width].astype(jnp.float32)
        xw = (x * toend_ref[0, 0, :, j : j + 1]).astype(jnp.bfloat16)
        out_ref[0, j] = jnp.dot(bt, xw, preferred_element_type=jnp.float32)


def intra_kernel(offset, skip_ref, c_ref, b_ref, x_ref, cumc_ref, cumr_ref, stepr_ref, *rest):
    out_ref = rest[-1]
    group = pl.program_id(1) + offset
    heads = cumc_ref.shape[-1]
    width = out_ref.shape[-1] // heads
    scores = lax.dot_general(
        c_ref[...], b_ref[...], (((1,), (1,)), ((), ())), preferred_element_type=jnp.float32
    )
    length = scores.shape[0]
    rows = lax.broadcasted_iota(jnp.int32, (length, length), 0)
    cols = lax.broadcasted_iota(jnp.int32, (length, length), 1)
    causal = rows >= cols
    for j in range(heads):
        diff = cumc_ref[0, 0, :, j : j + 1] - cumr_ref[0, 0, j : j + 1, :]
        decay = jnp.where(causal, jnp.exp(jnp.where(causal, diff, 0.0)), 0.0)
        weights = (scores * decay * stepr_ref[0, 0, j : j + 1, :]).astype(jnp.bfloat16)
        x = x_ref[:, j * width : (j + 1) * width]
        intra = jnp.dot(weights, x, preferred_element_type=jnp.float32)
        out_ref[:, j * width : (j + 1) * width] = (
            intra + skip_ref[group * heads + j] * x.astype(jnp.float32)
        )


def gate_kernel(decay_ref, part_ref, c_ref, block_ref, group_ref, ecum_ref, z_ref, out_ref, sq_ref):
    group = pl.program_id(0)
    span = pl.program_id(1)
    spans = block_ref.shape[0]
    heads = ecum_ref.shape[-1]
    head_count = decay_ref.shape[0] // spans
    width = out_ref.shape[-1] // heads
    c = c_ref[...]
    total = jnp.zeros((c.shape[0], width), jnp.float32)
    for j in range(heads):
        head = group * heads + j
        local_state = jnp.zeros(block_ref.shape[2:], jnp.float32)
        factor = jnp.float32(1.0)
        for earlier in range(spans - 1):
            decay = decay_ref[earlier * head_count + head]
            take = earlier < span
            local_state = jnp.where(
                take, decay * local_state + block_ref[earlier, j], local_state
            )
            factor = jnp.where(take, factor * decay, factor)
        state = local_state + factor * group_ref[j]
        high = state.astype(jnp.bfloat16)
        rest = state - high.astype(jnp.float32)
        mid = rest.astype(jnp.bfloat16)
        low = (rest - mid.astype(jnp.float32)).astype(jnp.bfloat16)
        inter = (
            jnp.dot(c, high, preferred_element_type=jnp.float32)
            + jnp.dot(c, mid, preferred_element_type=jnp.float32)
            + jnp.dot(c, low, preferred_element_type=jnp.float32)
        )
        columns = slice(j * width, (j + 1) * width)
        y = part_ref[:, columns] + inter * ecum_ref[0, 0, :, j : j + 1]
        z = z_ref[:, columns].astype(jnp.float32)
        gated = y * silu(z)
        out_ref[:, columns] = gated
        total = total + gated * gated
    sq_ref[0] = jnp.sum(total, axis=1, keepdims=True)


def by_group(values, spans, heads):
    return values.reshape(spans, heads // HEAD_GROUP, HEAD_GROUP, -1)


def columns_by_group(values, spans, heads):
    return by_group(values, spans, heads).transpose(0, 1, 3, 2)


def block_states(xin, halo, conv_x, b_t, to_end, spans, heads, width, offset):
    rows = xin.shape[0]
    size = b_t.shape[1]
    group = HEAD_GROUP
    lead = halo.shape[1]
    kernel_taps = conv_x.shape[0]
    return pl.pallas_call(
        state_kernel,
        grid=(spans, heads // group),
        in_specs=[
            pl.BlockSpec((SEGMENT_LENGTH, group * width), lambda c, g: (c, g + offset)),
            pl.BlockSpec((1, lead, group * width), lambda c, g: (c, 0, g + offset)),
            pl.BlockSpec((kernel_taps, group * width), lambda c, g: (0, g + offset)),
            pl.BlockSpec((1, size, SEGMENT_LENGTH), lambda c, g: (c, 0, 0)),
            pl.BlockSpec((1, 1, SEGMENT_LENGTH, group), lambda c, g: (c, g, 0, 0)),
        ],
        out_specs=[
            pl.BlockSpec((1, group, size, width), lambda c, g: (c, g, 0, 0)),
            pl.BlockSpec((SEGMENT_LENGTH, group * width), lambda c, g: (c, g)),
        ],
        out_shape=[
            jax.ShapeDtypeStruct((spans, heads, size, width), jnp.float32),
            jax.ShapeDtypeStruct((rows, heads * width), jnp.bfloat16),
        ],
        cost_estimate=pl.CostEstimate(
            flops=2 * rows * heads * width * size,
            bytes_accessed=rows * heads * width * 4 + spans * heads * size * width * 4,
            transcendentals=rows * heads * width,
        ),
    )(xin, halo, conv_x, b_t, columns_by_group(to_end, spans, heads))


def intra_terms(
    skip_gain, c_part, b_part, xconv, cum_col, cum_row, step_row, spans, groups, width, offset, into
):
    rows = xconv.shape[0]
    size = c_part.shape[1]
    group = HEAD_GROUP
    heads = groups * group
    in_specs = [
        pl.BlockSpec(memory_space=pltpu.SMEM),
        pl.BlockSpec((SEGMENT_LENGTH, size), lambda c, g: (c, 0)),
        pl.BlockSpec((SEGMENT_LENGTH, size), lambda c, g: (c, 0)),
        pl.BlockSpec((SEGMENT_LENGTH, group * width), lambda c, g: (c, g + offset)),
        pl.BlockSpec((1, 1, SEGMENT_LENGTH, group), lambda c, g: (c, g + offset, 0, 0)),
        pl.BlockSpec((1, 1, group, SEGMENT_LENGTH), lambda c, g: (c, g + offset, 0, 0)),
        pl.BlockSpec((1, 1, group, SEGMENT_LENGTH), lambda c, g: (c, g + offset, 0, 0)),
    ]
    operands = [skip_gain, c_part, b_part, xconv, cum_col, cum_row, step_row]
    aliases = {}
    if into is not None:
        in_specs.append(pl.BlockSpec(memory_space=pl.ANY))
        operands.append(into)
        aliases = {len(operands) - 1: 0}
    return pl.pallas_call(
        functools.partial(intra_kernel, offset),
        grid=(spans, groups),
        in_specs=in_specs,
        out_specs=pl.BlockSpec((SEGMENT_LENGTH, group * width), lambda c, g: (c, g + offset)),
        out_shape=jax.ShapeDtypeStruct((rows, xconv.shape[1]), jnp.float32),
        input_output_aliases=aliases,
        cost_estimate=pl.CostEstimate(
            flops=2 * rows * SEGMENT_LENGTH * (heads * width + size),
            bytes_accessed=rows * heads * width * 6,
            transcendentals=rows * SEGMENT_LENGTH * heads,
        ),
    )(*operands)


def gate_terms(
    block_decay, partial, c_part, block_state, group_state, ecum, gate_in, spans, heads, width, offset
):
    rows = partial.shape[0]
    size = c_part.shape[1]
    group = HEAD_GROUP
    groups = heads // group
    return pl.pallas_call(
        gate_kernel,
        grid=(groups, spans),
        in_specs=[
            pl.BlockSpec(memory_space=pltpu.SMEM),
            pl.BlockSpec((SEGMENT_LENGTH, group * width), lambda g, c: (c, g)),
            pl.BlockSpec((SEGMENT_LENGTH, size), lambda g, c: (c, 0)),
            pl.BlockSpec((spans, group, size, width), lambda g, c: (0, g, 0, 0)),
            pl.BlockSpec((group, size, width), lambda g, c: (g, 0, 0)),
            pl.BlockSpec((1, 1, SEGMENT_LENGTH, group), lambda g, c: (c, g, 0, 0)),
            pl.BlockSpec((SEGMENT_LENGTH, group * width), lambda g, c: (c, g + offset)),
        ],
        out_specs=[
            pl.BlockSpec((SEGMENT_LENGTH, group * width), lambda g, c: (c, g)),
            pl.BlockSpec((1, SEGMENT_LENGTH, 1), lambda g, c: (g, c, 0)),
        ],
        out_shape=[
            jax.ShapeDtypeStruct((rows, heads * width), jnp.float32),
            jax.ShapeDtypeStruct((groups, rows, 1), jnp.float32),
        ],
        compiler_params=pltpu.CompilerParams(vmem_limit_bytes=48 * 1024 * 1024),
        cost_estimate=pl.CostEstimate(
            flops=6 * rows * size * heads * width,
            bytes_accessed=rows * heads * width * 10,
            transcendentals=rows * heads * width,
        ),
    )(
        block_decay.reshape(-1),
        partial,
        c_part,
        block_state,
        group_state,
        columns_by_group(ecum, spans, heads),
        gate_in,
    )


def local(
    xin,
    gate_in,
    bc_proj,
    dt_raw,
    dt_bias,
    rate,
    skip_gain,
    conv_x,
    conv_bc,
    norm_gain,
    valid_blocks,
):
    row_count, channels = xin.shape
    head_count = dt_raw.shape[1]
    head_size = channels // head_count
    span_count = row_count // SEGMENT_LENGTH
    kernel_taps = conv_x.shape[0]
    live_rows = valid_blocks[0] * BLOCK
    tail_x = lax.dynamic_slice_in_dim(xin, live_rows - (kernel_taps - 1), kernel_taps - 1, 0)
    tail_bc = lax.dynamic_slice_in_dim(bc_proj, live_rows - (kernel_taps - 1), kernel_taps - 1, 0)
    prev = passed_along(jnp.concatenate([tail_x, tail_bc], axis=1), "seq", 1)
    prev_x, prev_bc = prev[:, :channels], prev[:, channels:]
    lead = 8
    edges = jnp.concatenate(
        [prev_x[None], xin.reshape(span_count, SEGMENT_LENGTH, channels)[:-1, -(kernel_taps - 1) :]],
        axis=0,
    )
    halo = jnp.pad(edges, ((0, 0), (lead - (kernel_taps - 1), 0), (0, 0)))
    bc_local = conv_silu(bc_proj, prev_bc, conv_bc)
    bc_full = lax.all_gather(bc_local, "ch", axis=1, tiled=True)
    state_size = bc_full.shape[1] // 2
    b_part = bc_full[:, :state_size]
    c_part = bc_full[:, state_size:]
    b_t = b_part.reshape(span_count, SEGMENT_LENGTH, state_size).transpose(0, 2, 1)
    row_valid = (jnp.arange(row_count) < live_rows).astype(jnp.float32)
    step_size = jax.nn.softplus(dt_raw + dt_bias[None, :]) * row_valid[:, None]
    step_three = step_size.reshape(span_count, SEGMENT_LENGTH, head_count)
    cumul = jnp.cumsum(-rate[None, None, :] * step_three, axis=1)
    cum_heads = jnp.transpose(cumul, (0, 2, 1))
    step_heads = jnp.transpose(step_three, (0, 2, 1))
    last_cum = cum_heads[:, :, -1]
    to_end = jnp.exp(last_cum[:, :, None] - cum_heads) * step_heads
    block_decay = jnp.exp(last_cum)
    count = lax.axis_size("seq")
    members = count // 2 if count % 2 == 0 and count >= 4 else count
    groups = [list(range(0, members)), list(range(members, count))] if members < count else None
    group_decay = jnp.ones((head_count,), jnp.float32)
    for index in range(span_count):
        group_decay = group_decay * block_decay[index]
    decays = lax.all_gather(group_decay, "seq", axis_index_groups=groups)
    to_end, decays = lax.optimization_barrier((to_end, decays))
    halves = 1
    part_heads = head_count // halves
    gated_parts = []
    square_part = None
    for part in range(halves):
        heads = slice(part * part_heads, (part + 1) * part_heads)
        offset = part * part_heads // HEAD_GROUP
        block_state, xconv = block_states(
            xin, halo, conv_x, b_t, to_end[:, heads], span_count, part_heads, head_size, offset
        )
        current = jnp.zeros((part_heads, state_size, head_size), jnp.float32)
        factor = jnp.ones((part_heads,), jnp.float32)
        local_enter = []
        factor_list = []
        for index in range(span_count):
            local_enter.append(current)
            factor_list.append(factor)
            current = block_decay[index, heads][:, None, None] * current + block_state[index]
            factor = factor * block_decay[index, heads]
        cum_col = columns_by_group(cum_heads[:, heads], span_count, part_heads)
        cum_row = by_group(cum_heads[:, heads], span_count, part_heads)
        step_row = by_group(step_heads[:, heads], span_count, part_heads)
        groups = part_heads // HEAD_GROUP
        first = groups // 2 if groups >= 2 else groups
        partial = intra_terms(
            skip_gain[heads], c_part, b_part, xconv, cum_col, cum_row, step_row,
            span_count, first, head_size, 0, None,
        )
        group_state, partial = scan_states(decays, current, "seq", partial)
        if first < groups:
            partial = intra_terms(
                skip_gain[heads], c_part, b_part, xconv, cum_col, cum_row, step_row,
                span_count, groups - first, head_size, first, partial,
            )
        gated, squares = gate_terms(
            block_decay[:, heads],
            partial,
            c_part,
            block_state,
            group_state,
            jnp.exp(cum_heads[:, heads]),
            gate_in,
            span_count,
            part_heads,
            head_size,
            offset,
        )
        squares = jnp.sum(squares, axis=0)
        gated_parts.append(gated)
        square_part = squares if square_part is None else square_part + squares
    gated = jnp.concatenate(gated_parts, axis=1)
    square_sum = lax.psum(square_part[:, 0], "ch")
    mean_sq = square_sum / INNER
    normed = gated * lax.rsqrt(mean_sq + 1e-05)[:, None] * norm_gain[None, :] * row_valid[:, None]
    return normed.astype(jnp.bfloat16)


def solution(mesh):
    placed = (
        P("seq", "ch"),
        P("seq", "ch"),
        P("seq", "ch"),
        P("seq", "ch"),
        P("ch"),
        P("ch"),
        P("ch"),
        P(None, "ch"),
        P(None, "ch"),
        P("ch"),
        P("seq"),
    )
    return jax.shard_map(
        local, mesh=mesh, in_specs=placed, out_specs=P("seq", "ch"), check_vma=False
    )
```

```python
import functools

import jax
import jax.numpy as jnp
from jax import lax
from jax.experimental import pallas as pl
from jax.experimental.pallas import tpu as pltpu
from jax.sharding import PartitionSpec as P

SEGMENT_LENGTH = 256
BLOCK = 128
INNER = 16384


def passed_along(block, axis, distance):
    devices = range(lax.axis_size(axis))
    route = [(i - distance, i) for i in devices if i - distance in devices]
    return lax.ppermute(block, axis, route)


def scan_states(factor, state, axis, tied):
    count = lax.axis_size(axis)
    split = count % 2 == 0 and count >= 4
    members = count // 2 if split else count
    groups = [list(range(0, members)), list(range(members, count))] if split else None
    heads, size, width = state.shape
    piece = size // members
    parts = state.reshape(heads, members, piece, width).transpose(1, 0, 2, 3)
    slot = jnp.zeros((piece, width), jnp.float32).at[0, :heads].set(factor)
    payload = jnp.concatenate(
        [parts, jnp.broadcast_to(slot, (members, 1, piece, width))], axis=1
    )
    got = lax.all_to_all(payload, axis, 0, 0, tiled=True, axis_index_groups=groups)
    decays = got[:, heads, 0, :heads]
    tied = lax.optimization_barrier((tied, got))[0]
    running = jnp.zeros((heads, piece, width), jnp.float32)
    entries = []
    for index in range(members):
        entries.append(running)
        running = decays[index][:, None, None] * running + got[index, :heads]
    if split:
        route = [(i, i + members) for i in range(members)]
        earlier = lax.ppermute(running, axis, route)
        carry = jnp.ones((heads,), jnp.float32)
        for index in range(members):
            entries[index] = entries[index] + carry[:, None, None] * earlier
            carry = carry * decays[index]
    back = lax.all_to_all(
        jnp.stack(entries, axis=0), axis, 0, 0, tiled=True, axis_index_groups=groups
    )
    return back.transpose(1, 0, 2, 3).reshape(heads, size, width), tied


def conv_silu(signal, tail_rows, weights):
    stacked = jnp.concatenate([tail_rows, signal], axis=0)
    kernel_taps = weights.shape[0]
    length = signal.shape[0]
    accum = jnp.zeros(signal.shape, jnp.float32)
    for offset in range(kernel_taps):
        accum = accum + weights[offset].astype(jnp.float32) * stacked[
            offset : offset + length
        ].astype(jnp.float32)
    return jax.nn.silu(accum).astype(jnp.bfloat16)


HEAD_GROUP = 16


def silu(value):
    half = 0.5 * value
    return half + half * jnp.tanh(half)


def state_kernel(x_ref, halo_ref, taps_ref, bt_ref, toend_ref, out_ref, conv_ref):
    width = out_ref.shape[-1]
    taps = taps_ref[...].astype(jnp.float32)
    kernel_taps = taps.shape[0]
    signal = x_ref[...].astype(jnp.float32)
    edge = halo_ref[0].astype(jnp.float32)
    lead = edge.shape[0]
    stacked = jnp.concatenate([edge, signal[:lead]], axis=0)
    accum = jnp.zeros(signal.shape, jnp.float32)
    head = jnp.zeros((lead, signal.shape[1]), jnp.float32)
    for offset in range(kernel_taps):
        shift = kernel_taps - 1 - offset
        moved = signal if shift == 0 else pltpu.roll(signal, shift, 0)
        accum = accum + taps[offset : offset + 1] * moved
        head = head + taps[offset : offset + 1] * stacked[lead - shift : 2 * lead - shift]
    conv_ref[...] = silu(accum).astype(jnp.bfloat16)
    conv_ref[:lead, :] = silu(head).astype(jnp.bfloat16)
    bt = bt_ref[0]
    for j in range(out_ref.shape[1]):
        x = conv_ref[:, j * width : (j + 1) * width].astype(jnp.float32)
        xw = (x * toend_ref[0, 0, :, j : j + 1]).astype(jnp.bfloat16)
        out_ref[0, j] = jnp.dot(bt, xw, preferred_element_type=jnp.float32)


def intra_kernel(skip_ref, c_ref, b_ref, x_ref, cumc_ref, cumr_ref, stepr_ref, out_ref):
    group = pl.program_id(1)
    heads = cumc_ref.shape[-1]
    width = out_ref.shape[-1] // heads
    scores = lax.dot_general(
        c_ref[...], b_ref[...], (((1,), (1,)), ((), ())), preferred_element_type=jnp.float32
    )
    length = scores.shape[0]
    rows = lax.broadcasted_iota(jnp.int32, (length, length), 0)
    cols = lax.broadcasted_iota(jnp.int32, (length, length), 1)
    causal = rows >= cols
    for j in range(heads):
        diff = cumc_ref[0, 0, :, j : j + 1] - cumr_ref[0, 0, j : j + 1, :]
        decay = jnp.where(causal, jnp.exp(jnp.where(causal, diff, 0.0)), 0.0)
        weights = (scores * decay * stepr_ref[0, 0, j : j + 1, :]).astype(jnp.bfloat16)
        x = x_ref[:, j * width : (j + 1) * width]
        intra = jnp.dot(weights, x, preferred_element_type=jnp.float32)
        out_ref[:, j * width : (j + 1) * width] = (
            intra + skip_ref[group * heads + j] * x.astype(jnp.float32)
        )


def gate_kernel(decay_ref, part_ref, c_ref, block_ref, group_ref, ecum_ref, z_ref, out_ref, sq_ref):
    group = pl.program_id(0)
    span = pl.program_id(1)
    spans = block_ref.shape[0]
    heads = ecum_ref.shape[-1]
    head_count = decay_ref.shape[0] // spans
    width = out_ref.shape[-1] // heads
    c = c_ref[...]
    total = jnp.zeros((c.shape[0], width), jnp.float32)
    for j in range(heads):
        head = group * heads + j
        local_state = jnp.zeros(block_ref.shape[2:], jnp.float32)
        factor = jnp.float32(1.0)
        for earlier in range(spans - 1):
            decay = decay_ref[earlier * head_count + head]
            take = earlier < span
            local_state = jnp.where(
                take, decay * local_state + block_ref[earlier, j], local_state
            )
            factor = jnp.where(take, factor * decay, factor)
        state = local_state + factor * group_ref[j]
        high = state.astype(jnp.bfloat16)
        rest = state - high.astype(jnp.float32)
        mid = rest.astype(jnp.bfloat16)
        low = (rest - mid.astype(jnp.float32)).astype(jnp.bfloat16)
        inter = (
            jnp.dot(c, high, preferred_element_type=jnp.float32)
            + jnp.dot(c, mid, preferred_element_type=jnp.float32)
            + jnp.dot(c, low, preferred_element_type=jnp.float32)
        )
        columns = slice(j * width, (j + 1) * width)
        y = part_ref[:, columns] + inter * ecum_ref[0, 0, :, j : j + 1]
        z = z_ref[:, columns].astype(jnp.float32)
        gated = y * silu(z)
        out_ref[:, columns] = gated
        total = total + gated * gated
    sq_ref[0] = jnp.sum(total, axis=1, keepdims=True)


def by_group(values, spans, heads):
    return values.reshape(spans, heads // HEAD_GROUP, HEAD_GROUP, -1)


def columns_by_group(values, spans, heads):
    return by_group(values, spans, heads).transpose(0, 1, 3, 2)


def block_states(xin, halo, conv_x, b_t, to_end, spans, heads, width, offset):
    rows = xin.shape[0]
    size = b_t.shape[1]
    group = HEAD_GROUP
    lead = halo.shape[1]
    kernel_taps = conv_x.shape[0]
    return pl.pallas_call(
        state_kernel,
        grid=(spans, heads // group),
        in_specs=[
            pl.BlockSpec((SEGMENT_LENGTH, group * width), lambda c, g: (c, g + offset)),
            pl.BlockSpec((1, lead, group * width), lambda c, g: (c, 0, g + offset)),
            pl.BlockSpec((kernel_taps, group * width), lambda c, g: (0, g + offset)),
            pl.BlockSpec((1, size, SEGMENT_LENGTH), lambda c, g: (c, 0, 0)),
            pl.BlockSpec((1, 1, SEGMENT_LENGTH, group), lambda c, g: (c, g, 0, 0)),
        ],
        out_specs=[
            pl.BlockSpec((1, group, size, width), lambda c, g: (c, g, 0, 0)),
            pl.BlockSpec((SEGMENT_LENGTH, group * width), lambda c, g: (c, g)),
        ],
        out_shape=[
            jax.ShapeDtypeStruct((spans, heads, size, width), jnp.float32),
            jax.ShapeDtypeStruct((rows, heads * width), jnp.bfloat16),
        ],
        cost_estimate=pl.CostEstimate(
            flops=2 * rows * heads * width * size,
            bytes_accessed=rows * heads * width * 4 + spans * heads * size * width * 4,
            transcendentals=rows * heads * width,
        ),
    )(xin, halo, conv_x, b_t, columns_by_group(to_end, spans, heads))


def intra_terms(skip_gain, c_part, b_part, xconv, cum_heads, step_heads, spans, heads, width):
    rows = xconv.shape[0]
    size = c_part.shape[1]
    group = HEAD_GROUP
    return pl.pallas_call(
        intra_kernel,
        grid=(spans, heads // group),
        in_specs=[
            pl.BlockSpec(memory_space=pltpu.SMEM),
            pl.BlockSpec((SEGMENT_LENGTH, size), lambda c, g: (c, 0)),
            pl.BlockSpec((SEGMENT_LENGTH, size), lambda c, g: (c, 0)),
            pl.BlockSpec((SEGMENT_LENGTH, group * width), lambda c, g: (c, g)),
            pl.BlockSpec((1, 1, SEGMENT_LENGTH, group), lambda c, g: (c, g, 0, 0)),
            pl.BlockSpec((1, 1, group, SEGMENT_LENGTH), lambda c, g: (c, g, 0, 0)),
            pl.BlockSpec((1, 1, group, SEGMENT_LENGTH), lambda c, g: (c, g, 0, 0)),
        ],
        out_specs=pl.BlockSpec((SEGMENT_LENGTH, group * width), lambda c, g: (c, g)),
        out_shape=jax.ShapeDtypeStruct((rows, heads * width), jnp.float32),
        cost_estimate=pl.CostEstimate(
            flops=2 * rows * SEGMENT_LENGTH * (heads * width + size),
            bytes_accessed=rows * heads * width * 6,
            transcendentals=rows * SEGMENT_LENGTH * heads,
        ),
    )(
        skip_gain,
        c_part,
        b_part,
        xconv,
        columns_by_group(cum_heads, spans, heads),
        by_group(cum_heads, spans, heads),
        by_group(step_heads, spans, heads),
    )


def gate_terms(
    block_decay, partial, c_part, block_state, group_state, ecum, gate_in, spans, heads, width, offset
):
    rows = partial.shape[0]
    size = c_part.shape[1]
    group = HEAD_GROUP
    groups = heads // group
    return pl.pallas_call(
        gate_kernel,
        grid=(groups, spans),
        in_specs=[
            pl.BlockSpec(memory_space=pltpu.SMEM),
            pl.BlockSpec((SEGMENT_LENGTH, group * width), lambda g, c: (c, g)),
            pl.BlockSpec((SEGMENT_LENGTH, size), lambda g, c: (c, 0)),
            pl.BlockSpec((spans, group, size, width), lambda g, c: (0, g, 0, 0)),
            pl.BlockSpec((group, size, width), lambda g, c: (g, 0, 0)),
            pl.BlockSpec((1, 1, SEGMENT_LENGTH, group), lambda g, c: (c, g, 0, 0)),
            pl.BlockSpec((SEGMENT_LENGTH, group * width), lambda g, c: (c, g + offset)),
        ],
        out_specs=[
            pl.BlockSpec((SEGMENT_LENGTH, group * width), lambda g, c: (c, g)),
            pl.BlockSpec((1, SEGMENT_LENGTH, 1), lambda g, c: (g, c, 0)),
        ],
        out_shape=[
            jax.ShapeDtypeStruct((rows, heads * width), jnp.float32),
            jax.ShapeDtypeStruct((groups, rows, 1), jnp.float32),
        ],
        compiler_params=pltpu.CompilerParams(vmem_limit_bytes=48 * 1024 * 1024),
        cost_estimate=pl.CostEstimate(
            flops=6 * rows * size * heads * width,
            bytes_accessed=rows * heads * width * 10,
            transcendentals=rows * heads * width,
        ),
    )(
        block_decay.reshape(-1),
        partial,
        c_part,
        block_state,
        group_state,
        columns_by_group(ecum, spans, heads),
        gate_in,
    )


def local(
    xin,
    gate_in,
    bc_proj,
    dt_raw,
    dt_bias,
    rate,
    skip_gain,
    conv_x,
    conv_bc,
    norm_gain,
    valid_blocks,
):
    row_count, channels = xin.shape
    head_count = dt_raw.shape[1]
    head_size = channels // head_count
    span_count = row_count // SEGMENT_LENGTH
    kernel_taps = conv_x.shape[0]
    live_rows = valid_blocks[0] * BLOCK
    tail_x = lax.dynamic_slice_in_dim(xin, live_rows - (kernel_taps - 1), kernel_taps - 1, 0)
    tail_bc = lax.dynamic_slice_in_dim(bc_proj, live_rows - (kernel_taps - 1), kernel_taps - 1, 0)
    prev = passed_along(jnp.concatenate([tail_x, tail_bc], axis=1), "seq", 1)
    prev_x, prev_bc = prev[:, :channels], prev[:, channels:]
    lead = 8
    edges = jnp.concatenate(
        [prev_x[None], xin.reshape(span_count, SEGMENT_LENGTH, channels)[:-1, -(kernel_taps - 1) :]],
        axis=0,
    )
    halo = jnp.pad(edges, ((0, 0), (lead - (kernel_taps - 1), 0), (0, 0)))
    bc_local = conv_silu(bc_proj, prev_bc, conv_bc)
    bc_full = lax.all_gather(bc_local, "ch", axis=1, tiled=True)
    state_size = bc_full.shape[1] // 2
    b_part = bc_full[:, :state_size]
    c_part = bc_full[:, state_size:]
    b_t = b_part.reshape(span_count, SEGMENT_LENGTH, state_size).transpose(0, 2, 1)
    row_valid = (jnp.arange(row_count) < live_rows).astype(jnp.float32)
    step_size = jax.nn.softplus(dt_raw + dt_bias[None, :]) * row_valid[:, None]
    step_three = step_size.reshape(span_count, SEGMENT_LENGTH, head_count)
    cumul = jnp.cumsum(-rate[None, None, :] * step_three, axis=1)
    cum_heads = jnp.transpose(cumul, (0, 2, 1))
    step_heads = jnp.transpose(step_three, (0, 2, 1))
    last_cum = cum_heads[:, :, -1]
    to_end = jnp.exp(last_cum[:, :, None] - cum_heads) * step_heads
    block_decay = jnp.exp(last_cum)
    halves = 1
    part_heads = head_count // halves
    gated_parts = []
    square_part = None
    for part in range(halves):
        heads = slice(part * part_heads, (part + 1) * part_heads)
        offset = part * part_heads // HEAD_GROUP
        block_state, xconv = block_states(
            xin, halo, conv_x, b_t, to_end[:, heads], span_count, part_heads, head_size, offset
        )
        current = jnp.zeros((part_heads, state_size, head_size), jnp.float32)
        factor = jnp.ones((part_heads,), jnp.float32)
        local_enter = []
        factor_list = []
        for index in range(span_count):
            local_enter.append(current)
            factor_list.append(factor)
            current = block_decay[index, heads][:, None, None] * current + block_state[index]
            factor = factor * block_decay[index, heads]
        group_state, xconv = scan_states(factor, current, "seq", xconv)
        partial = intra_terms(
            skip_gain[heads],
            c_part,
            b_part,
            xconv,
            cum_heads[:, heads],
            step_heads[:, heads],
            span_count,
            part_heads,
            head_size,
        )
        gated, squares = gate_terms(
            block_decay[:, heads],
            partial,
            c_part,
            block_state,
            group_state,
            jnp.exp(cum_heads[:, heads]),
            gate_in,
            span_count,
            part_heads,
            head_size,
            offset,
        )
        squares = jnp.sum(squares, axis=0)
        gated_parts.append(gated)
        square_part = squares if square_part is None else square_part + squares
    gated = jnp.concatenate(gated_parts, axis=1)
    square_sum = lax.psum(square_part[:, 0], "ch")
    mean_sq = square_sum / INNER
    normed = gated * lax.rsqrt(mean_sq + 1e-05)[:, None] * norm_gain[None, :] * row_valid[:, None]
    return normed.astype(jnp.bfloat16)


def solution(mesh):
    placed = (
        P("seq", "ch"),
        P("seq", "ch"),
        P("seq", "ch"),
        P("seq", "ch"),
        P("ch"),
        P("ch"),
        P("ch"),
        P(None, "ch"),
        P(None, "ch"),
        P("ch"),
        P("seq"),
    )
    return jax.shard_map(
        local, mesh=mesh, in_specs=placed, out_specs=P("seq", "ch"), check_vma=False
    )
```

```python
import functools

import jax
import jax.numpy as jnp
from jax import lax
from jax.experimental import pallas as pl
from jax.experimental.pallas import tpu as pltpu
from jax.sharding import PartitionSpec as P

SEGMENT_LENGTH = 256
BLOCK = 128
INNER = 16384


def passed_along(block, axis, distance):
    devices = range(lax.axis_size(axis))
    route = [(i - distance, i) for i in devices if i - distance in devices]
    return lax.ppermute(block, axis, route)


def scan_states(factor, state, axis, tied):
    count = lax.axis_size(axis)
    split = count % 2 == 0 and count >= 4
    members = count // 2 if split else count
    groups = [list(range(0, members)), list(range(members, count))] if split else None
    heads, size, width = state.shape
    piece = size // members
    parts = state.reshape(heads, members, piece, width).transpose(1, 0, 2, 3)
    slot = jnp.zeros((piece, width), jnp.float32).at[0, :heads].set(factor)
    payload = jnp.concatenate(
        [parts, jnp.broadcast_to(slot, (members, 1, piece, width))], axis=1
    )
    got = lax.all_to_all(payload, axis, 0, 0, tiled=True, axis_index_groups=groups)
    decays = got[:, heads, 0, :heads]
    tied = lax.optimization_barrier((tied, got))[0]
    running = jnp.zeros((heads, piece, width), jnp.float32)
    entries = []
    for index in range(members):
        entries.append(running)
        running = decays[index][:, None, None] * running + got[index, :heads]
    if split:
        route = [(i, i + members) for i in range(members)]
        earlier = lax.ppermute(running, axis, route)
        carry = jnp.ones((heads,), jnp.float32)
        for index in range(members):
            entries[index] = entries[index] + carry[:, None, None] * earlier
            carry = carry * decays[index]
    back = lax.all_to_all(
        jnp.stack(entries, axis=0), axis, 0, 0, tiled=True, axis_index_groups=groups
    )
    return back.transpose(1, 0, 2, 3).reshape(heads, size, width), tied


def conv_silu(signal, tail_rows, weights):
    stacked = jnp.concatenate([tail_rows, signal], axis=0)
    kernel_taps = weights.shape[0]
    length = signal.shape[0]
    accum = jnp.zeros(signal.shape, jnp.float32)
    for offset in range(kernel_taps):
        accum = accum + weights[offset].astype(jnp.float32) * stacked[
            offset : offset + length
        ].astype(jnp.float32)
    return jax.nn.silu(accum).astype(jnp.bfloat16)


HEAD_GROUP = 32


def silu(value):
    half = 0.5 * value
    return half + half * jnp.tanh(half)


def state_kernel(x_ref, halo_ref, taps_ref, bt_ref, toend_ref, out_ref, conv_ref):
    width = out_ref.shape[-1]
    taps = taps_ref[...].astype(jnp.float32)
    kernel_taps = taps.shape[0]
    signal = x_ref[...].astype(jnp.float32)
    edge = halo_ref[0].astype(jnp.float32)
    lead = edge.shape[0]
    stacked = jnp.concatenate([edge, signal[:lead]], axis=0)
    accum = jnp.zeros(signal.shape, jnp.float32)
    head = jnp.zeros((lead, signal.shape[1]), jnp.float32)
    for offset in range(kernel_taps):
        shift = kernel_taps - 1 - offset
        moved = signal if shift == 0 else pltpu.roll(signal, shift, 0)
        accum = accum + taps[offset : offset + 1] * moved
        head = head + taps[offset : offset + 1] * stacked[lead - shift : 2 * lead - shift]
    conv_ref[...] = silu(accum).astype(jnp.bfloat16)
    conv_ref[:lead, :] = silu(head).astype(jnp.bfloat16)
    bt = bt_ref[0]
    for j in range(out_ref.shape[1]):
        x = conv_ref[:, j * width : (j + 1) * width].astype(jnp.float32)
        xw = (x * toend_ref[0, 0, :, j : j + 1]).astype(jnp.bfloat16)
        out_ref[0, j] = jnp.dot(bt, xw, preferred_element_type=jnp.float32)


def intra_kernel(skip_ref, c_ref, b_ref, x_ref, cumc_ref, cumr_ref, stepr_ref, out_ref):
    group = pl.program_id(1)
    heads = cumc_ref.shape[-1]
    width = out_ref.shape[-1] // heads
    scores = lax.dot_general(
        c_ref[...], b_ref[...], (((1,), (1,)), ((), ())), preferred_element_type=jnp.float32
    )
    length = scores.shape[0]
    rows = lax.broadcasted_iota(jnp.int32, (length, length), 0)
    cols = lax.broadcasted_iota(jnp.int32, (length, length), 1)
    causal = rows >= cols
    for j in range(heads):
        diff = cumc_ref[0, 0, :, j : j + 1] - cumr_ref[0, 0, j : j + 1, :]
        decay = jnp.where(causal, jnp.exp(jnp.where(causal, diff, 0.0)), 0.0)
        weights = (scores * decay * stepr_ref[0, 0, j : j + 1, :]).astype(jnp.bfloat16)
        x = x_ref[:, j * width : (j + 1) * width]
        intra = jnp.dot(weights, x, preferred_element_type=jnp.float32)
        out_ref[:, j * width : (j + 1) * width] = (
            intra + skip_ref[group * heads + j] * x.astype(jnp.float32)
        )


def gate_kernel(decay_ref, part_ref, c_ref, block_ref, group_ref, ecum_ref, z_ref, out_ref, sq_ref):
    group = pl.program_id(0)
    span = pl.program_id(1)
    spans = block_ref.shape[0]
    heads = ecum_ref.shape[-1]
    head_count = decay_ref.shape[0] // spans
    width = out_ref.shape[-1] // heads
    c = c_ref[...]
    total = jnp.zeros((c.shape[0], width), jnp.float32)
    for j in range(heads):
        head = group * heads + j
        local_state = jnp.zeros(block_ref.shape[2:], jnp.float32)
        factor = jnp.float32(1.0)
        for earlier in range(spans - 1):
            decay = decay_ref[earlier * head_count + head]
            take = earlier < span
            local_state = jnp.where(
                take, decay * local_state + block_ref[earlier, j], local_state
            )
            factor = jnp.where(take, factor * decay, factor)
        state = local_state + factor * group_ref[j]
        high = state.astype(jnp.bfloat16)
        rest = state - high.astype(jnp.float32)
        mid = rest.astype(jnp.bfloat16)
        low = (rest - mid.astype(jnp.float32)).astype(jnp.bfloat16)
        inter = (
            jnp.dot(c, high, preferred_element_type=jnp.float32)
            + jnp.dot(c, mid, preferred_element_type=jnp.float32)
            + jnp.dot(c, low, preferred_element_type=jnp.float32)
        )
        columns = slice(j * width, (j + 1) * width)
        y = part_ref[:, columns] + inter * ecum_ref[0, 0, :, j : j + 1]
        z = z_ref[:, columns].astype(jnp.float32)
        gated = y * silu(z)
        out_ref[:, columns] = gated
        total = total + gated * gated
    sq_ref[0] = jnp.sum(total, axis=1, keepdims=True)


def by_group(values, spans, heads):
    return values.reshape(spans, heads // HEAD_GROUP, HEAD_GROUP, -1)


def columns_by_group(values, spans, heads):
    return by_group(values, spans, heads).transpose(0, 1, 3, 2)


def block_states(xin, halo, conv_x, b_t, to_end, spans, heads, width, offset):
    rows = xin.shape[0]
    size = b_t.shape[1]
    group = HEAD_GROUP
    lead = halo.shape[1]
    kernel_taps = conv_x.shape[0]
    return pl.pallas_call(
        state_kernel,
        grid=(spans, heads // group),
        in_specs=[
            pl.BlockSpec((SEGMENT_LENGTH, group * width), lambda c, g: (c, g + offset)),
            pl.BlockSpec((1, lead, group * width), lambda c, g: (c, 0, g + offset)),
            pl.BlockSpec((kernel_taps, group * width), lambda c, g: (0, g + offset)),
            pl.BlockSpec((1, size, SEGMENT_LENGTH), lambda c, g: (c, 0, 0)),
            pl.BlockSpec((1, 1, SEGMENT_LENGTH, group), lambda c, g: (c, g, 0, 0)),
        ],
        out_specs=[
            pl.BlockSpec((1, group, size, width), lambda c, g: (c, g, 0, 0)),
            pl.BlockSpec((SEGMENT_LENGTH, group * width), lambda c, g: (c, g)),
        ],
        out_shape=[
            jax.ShapeDtypeStruct((spans, heads, size, width), jnp.float32),
            jax.ShapeDtypeStruct((rows, heads * width), jnp.bfloat16),
        ],
        compiler_params=pltpu.CompilerParams(vmem_limit_bytes=60 * 1024 * 1024),
        cost_estimate=pl.CostEstimate(
            flops=2 * rows * heads * width * size,
            bytes_accessed=rows * heads * width * 4 + spans * heads * size * width * 4,
            transcendentals=rows * heads * width,
        ),
    )(xin, halo, conv_x, b_t, columns_by_group(to_end, spans, heads))


def intra_terms(skip_gain, c_part, b_part, xconv, cum_heads, step_heads, spans, heads, width):
    rows = xconv.shape[0]
    size = c_part.shape[1]
    group = HEAD_GROUP
    return pl.pallas_call(
        intra_kernel,
        grid=(spans, heads // group),
        in_specs=[
            pl.BlockSpec(memory_space=pltpu.SMEM),
            pl.BlockSpec((SEGMENT_LENGTH, size), lambda c, g: (c, 0)),
            pl.BlockSpec((SEGMENT_LENGTH, size), lambda c, g: (c, 0)),
            pl.BlockSpec((SEGMENT_LENGTH, group * width), lambda c, g: (c, g)),
            pl.BlockSpec((1, 1, SEGMENT_LENGTH, group), lambda c, g: (c, g, 0, 0)),
            pl.BlockSpec((1, 1, group, SEGMENT_LENGTH), lambda c, g: (c, g, 0, 0)),
            pl.BlockSpec((1, 1, group, SEGMENT_LENGTH), lambda c, g: (c, g, 0, 0)),
        ],
        out_specs=pl.BlockSpec((SEGMENT_LENGTH, group * width), lambda c, g: (c, g)),
        out_shape=jax.ShapeDtypeStruct((rows, heads * width), jnp.float32),
        compiler_params=pltpu.CompilerParams(vmem_limit_bytes=60 * 1024 * 1024),
        cost_estimate=pl.CostEstimate(
            flops=2 * rows * SEGMENT_LENGTH * (heads * width + size),
            bytes_accessed=rows * heads * width * 6,
            transcendentals=rows * SEGMENT_LENGTH * heads,
        ),
    )(
        skip_gain,
        c_part,
        b_part,
        xconv,
        columns_by_group(cum_heads, spans, heads),
        by_group(cum_heads, spans, heads),
        by_group(step_heads, spans, heads),
    )


def gate_terms(
    block_decay, partial, c_part, block_state, group_state, ecum, gate_in, spans, heads, width, offset
):
    rows = partial.shape[0]
    size = c_part.shape[1]
    group = HEAD_GROUP
    groups = heads // group
    return pl.pallas_call(
        gate_kernel,
        grid=(groups, spans),
        in_specs=[
            pl.BlockSpec(memory_space=pltpu.SMEM),
            pl.BlockSpec((SEGMENT_LENGTH, group * width), lambda g, c: (c, g)),
            pl.BlockSpec((SEGMENT_LENGTH, size), lambda g, c: (c, 0)),
            pl.BlockSpec((spans, group, size, width), lambda g, c: (0, g, 0, 0)),
            pl.BlockSpec((group, size, width), lambda g, c: (g, 0, 0)),
            pl.BlockSpec((1, 1, SEGMENT_LENGTH, group), lambda g, c: (c, g, 0, 0)),
            pl.BlockSpec((SEGMENT_LENGTH, group * width), lambda g, c: (c, g + offset)),
        ],
        out_specs=[
            pl.BlockSpec((SEGMENT_LENGTH, group * width), lambda g, c: (c, g)),
            pl.BlockSpec((1, SEGMENT_LENGTH, 1), lambda g, c: (g, c, 0)),
        ],
        out_shape=[
            jax.ShapeDtypeStruct((rows, heads * width), jnp.float32),
            jax.ShapeDtypeStruct((groups, rows, 1), jnp.float32),
        ],
        compiler_params=pltpu.CompilerParams(vmem_limit_bytes=60 * 1024 * 1024),
        cost_estimate=pl.CostEstimate(
            flops=6 * rows * size * heads * width,
            bytes_accessed=rows * heads * width * 10,
            transcendentals=rows * heads * width,
        ),
    )(
        block_decay.reshape(-1),
        partial,
        c_part,
        block_state,
        group_state,
        columns_by_group(ecum, spans, heads),
        gate_in,
    )


def local(
    xin,
    gate_in,
    bc_proj,
    dt_raw,
    dt_bias,
    rate,
    skip_gain,
    conv_x,
    conv_bc,
    norm_gain,
    valid_blocks,
):
    row_count, channels = xin.shape
    head_count = dt_raw.shape[1]
    head_size = channels // head_count
    span_count = row_count // SEGMENT_LENGTH
    kernel_taps = conv_x.shape[0]
    live_rows = valid_blocks[0] * BLOCK
    tail_x = lax.dynamic_slice_in_dim(xin, live_rows - (kernel_taps - 1), kernel_taps - 1, 0)
    tail_bc = lax.dynamic_slice_in_dim(bc_proj, live_rows - (kernel_taps - 1), kernel_taps - 1, 0)
    prev = passed_along(jnp.concatenate([tail_x, tail_bc], axis=1), "seq", 1)
    prev_x, prev_bc = prev[:, :channels], prev[:, channels:]
    lead = 8
    edges = jnp.concatenate(
        [prev_x[None], xin.reshape(span_count, SEGMENT_LENGTH, channels)[:-1, -(kernel_taps - 1) :]],
        axis=0,
    )
    halo = jnp.pad(edges, ((0, 0), (lead - (kernel_taps - 1), 0), (0, 0)))
    bc_local = conv_silu(bc_proj, prev_bc, conv_bc)
    bc_full = lax.all_gather(bc_local, "ch", axis=1, tiled=True)
    state_size = bc_full.shape[1] // 2
    b_part = bc_full[:, :state_size]
    c_part = bc_full[:, state_size:]
    b_t = b_part.reshape(span_count, SEGMENT_LENGTH, state_size).transpose(0, 2, 1)
    row_valid = (jnp.arange(row_count) < live_rows).astype(jnp.float32)
    step_size = jax.nn.softplus(dt_raw + dt_bias[None, :]) * row_valid[:, None]
    step_three = step_size.reshape(span_count, SEGMENT_LENGTH, head_count)
    cumul = jnp.cumsum(-rate[None, None, :] * step_three, axis=1)
    cum_heads = jnp.transpose(cumul, (0, 2, 1))
    step_heads = jnp.transpose(step_three, (0, 2, 1))
    last_cum = cum_heads[:, :, -1]
    to_end = jnp.exp(last_cum[:, :, None] - cum_heads) * step_heads
    block_decay = jnp.exp(last_cum)
    halves = 1
    part_heads = head_count // halves
    gated_parts = []
    square_part = None
    for part in range(halves):
        heads = slice(part * part_heads, (part + 1) * part_heads)
        offset = part * part_heads // HEAD_GROUP
        block_state, xconv = block_states(
            xin, halo, conv_x, b_t, to_end[:, heads], span_count, part_heads, head_size, offset
        )
        current = jnp.zeros((part_heads, state_size, head_size), jnp.float32)
        factor = jnp.ones((part_heads,), jnp.float32)
        local_enter = []
        factor_list = []
        for index in range(span_count):
            local_enter.append(current)
            factor_list.append(factor)
            current = block_decay[index, heads][:, None, None] * current + block_state[index]
            factor = factor * block_decay[index, heads]
        group_state, xconv = scan_states(factor, current, "seq", xconv)
        partial = intra_terms(
            skip_gain[heads],
            c_part,
            b_part,
            xconv,
            cum_heads[:, heads],
            step_heads[:, heads],
            span_count,
            part_heads,
            head_size,
        )
        gated, squares = gate_terms(
            block_decay[:, heads],
            partial,
            c_part,
            block_state,
            group_state,
            jnp.exp(cum_heads[:, heads]),
            gate_in,
            span_count,
            part_heads,
            head_size,
            offset,
        )
        squares = jnp.sum(squares, axis=0)
        gated_parts.append(gated)
        square_part = squares if square_part is None else square_part + squares
    gated = jnp.concatenate(gated_parts, axis=1)
    square_sum = lax.psum(square_part[:, 0], "ch")
    mean_sq = square_sum / INNER
    normed = gated * lax.rsqrt(mean_sq + 1e-05)[:, None] * norm_gain[None, :] * row_valid[:, None]
    return normed.astype(jnp.bfloat16)


def solution(mesh):
    placed = (
        P("seq", "ch"),
        P("seq", "ch"),
        P("seq", "ch"),
        P("seq", "ch"),
        P("ch"),
        P("ch"),
        P("ch"),
        P(None, "ch"),
        P(None, "ch"),
        P("ch"),
        P("seq"),
    )
    return jax.shard_map(
        local, mesh=mesh, in_specs=placed, out_specs=P("seq", "ch"), check_vma=False
    )
```

```python
import functools

import jax
import jax.numpy as jnp
from jax import lax
from jax.experimental import pallas as pl
from jax.experimental.pallas import tpu as pltpu
from jax.sharding import PartitionSpec as P

SEGMENT_LENGTH = 256
BLOCK = 128
INNER = 16384


def passed_along(block, axis, distance):
    devices = range(lax.axis_size(axis))
    route = [(i - distance, i) for i in devices if i - distance in devices]
    return lax.ppermute(block, axis, route)


def scan_states(factor, state, axis, tied):
    count = lax.axis_size(axis)
    split = count % 2 == 0 and count >= 4
    members = count // 2 if split else count
    groups = [list(range(0, members)), list(range(members, count))] if split else None
    heads, size, width = state.shape
    piece = size // members
    parts = state.reshape(heads, members, piece, width).transpose(1, 0, 2, 3)
    slot = jnp.zeros((piece, width), jnp.float32).at[0, :heads].set(factor)
    payload = jnp.concatenate(
        [parts, jnp.broadcast_to(slot, (members, 1, piece, width))], axis=1
    )
    got = lax.all_to_all(payload, axis, 0, 0, tiled=True, axis_index_groups=groups)
    decays = got[:, heads, 0, :heads]
    tied = lax.optimization_barrier((tied, got))[0]
    running = jnp.zeros((heads, piece, width), jnp.float32)
    entries = []
    for index in range(members):
        entries.append(running)
        running = decays[index][:, None, None] * running + got[index, :heads]
    if split:
        route = [(i, i + members) for i in range(members)]
        earlier = lax.ppermute(running, axis, route)
        carry = jnp.ones((heads,), jnp.float32)
        for index in range(members):
            entries[index] = entries[index] + carry[:, None, None] * earlier
            carry = carry * decays[index]
    back = lax.all_to_all(
        jnp.stack(entries, axis=0), axis, 0, 0, tiled=True, axis_index_groups=groups
    )
    return back.transpose(1, 0, 2, 3).reshape(heads, size, width), tied


def conv_silu(signal, tail_rows, weights):
    stacked = jnp.concatenate([tail_rows, signal], axis=0)
    kernel_taps = weights.shape[0]
    length = signal.shape[0]
    accum = jnp.zeros(signal.shape, jnp.float32)
    for offset in range(kernel_taps):
        accum = accum + weights[offset].astype(jnp.float32) * stacked[
            offset : offset + length
        ].astype(jnp.float32)
    return jax.nn.silu(accum).astype(jnp.bfloat16)


HEAD_GROUP = 16


def silu(value):
    half = 0.5 * value
    return half + half * jnp.tanh(half)


def state_kernel(x_ref, halo_ref, taps_ref, bt_ref, toend_ref, out_ref, conv_ref):
    width = out_ref.shape[-1]
    taps = taps_ref[...].astype(jnp.float32)
    kernel_taps = taps.shape[0]
    signal = x_ref[...].astype(jnp.float32)
    edge = halo_ref[0].astype(jnp.float32)
    lead = edge.shape[0]
    stacked = jnp.concatenate([edge, signal[:lead]], axis=0)
    accum = jnp.zeros(signal.shape, jnp.float32)
    head = jnp.zeros((lead, signal.shape[1]), jnp.float32)
    for offset in range(kernel_taps):
        shift = kernel_taps - 1 - offset
        moved = signal if shift == 0 else pltpu.roll(signal, shift, 0)
        accum = accum + taps[offset : offset + 1] * moved
        head = head + taps[offset : offset + 1] * stacked[lead - shift : 2 * lead - shift]
    conv_ref[...] = silu(accum).astype(jnp.bfloat16)
    conv_ref[:lead, :] = silu(head).astype(jnp.bfloat16)
    bt = bt_ref[0]
    for j in range(out_ref.shape[1]):
        x = conv_ref[:, j * width : (j + 1) * width].astype(jnp.float32)
        xw = (x * toend_ref[0, 0, :, j : j + 1]).astype(jnp.bfloat16)
        out_ref[0, j] = jnp.dot(bt, xw, preferred_element_type=jnp.float32)


def intra_kernel(skip_ref, c_ref, b_ref, x_ref, cumc_ref, cumr_ref, stepr_ref, out_ref):
    group = pl.program_id(1)
    heads = cumc_ref.shape[-1]
    width = out_ref.shape[-1] // heads
    scores = lax.dot_general(
        c_ref[...], b_ref[...], (((1,), (1,)), ((), ())), preferred_element_type=jnp.float32
    )
    length = scores.shape[0]
    rows = lax.broadcasted_iota(jnp.int32, (length, length), 0)
    cols = lax.broadcasted_iota(jnp.int32, (length, length), 1)
    causal = rows >= cols
    for j in range(heads):
        diff = cumc_ref[0, 0, :, j : j + 1] - cumr_ref[0, 0, j : j + 1, :]
        decay = jnp.where(causal, jnp.exp(jnp.where(causal, diff, 0.0)), 0.0)
        weights = (scores * decay * stepr_ref[0, 0, j : j + 1, :]).astype(jnp.bfloat16)
        x = x_ref[:, j * width : (j + 1) * width]
        intra = jnp.dot(weights, x, preferred_element_type=jnp.float32)
        out_ref[:, j * width : (j + 1) * width] = (
            intra + skip_ref[group * heads + j] * x.astype(jnp.float32)
        )


def gate_kernel(decay_ref, part_ref, c_ref, block_ref, group_ref, ecum_ref, z_ref, out_ref, sq_ref):
    group = pl.program_id(0)
    span = pl.program_id(1)
    spans = block_ref.shape[0]
    heads = ecum_ref.shape[-1]
    head_count = decay_ref.shape[0] // spans
    width = out_ref.shape[-1] // heads
    c = c_ref[...]
    total = jnp.zeros((c.shape[0], width), jnp.float32)
    for j in range(heads):
        head = group * heads + j
        local_state = jnp.zeros(block_ref.shape[2:], jnp.float32)
        factor = jnp.float32(1.0)
        for earlier in range(spans - 1):
            decay = decay_ref[earlier * head_count + head]
            take = earlier < span
            local_state = jnp.where(
                take, decay * local_state + block_ref[earlier, j], local_state
            )
            factor = jnp.where(take, factor * decay, factor)
        state = local_state + factor * group_ref[j]
        high = state.astype(jnp.bfloat16)
        rest = state - high.astype(jnp.float32)
        mid = rest.astype(jnp.bfloat16)
        low = (rest - mid.astype(jnp.float32)).astype(jnp.bfloat16)
        inter = (
            jnp.dot(c, high, preferred_element_type=jnp.float32)
            + jnp.dot(c, mid, preferred_element_type=jnp.float32)
            + jnp.dot(c, low, preferred_element_type=jnp.float32)
        )
        columns = slice(j * width, (j + 1) * width)
        y = part_ref[:, columns] + inter * ecum_ref[0, 0, :, j : j + 1]
        z = z_ref[:, columns].astype(jnp.float32)
        gated = y * silu(z)
        out_ref[:, columns] = gated
        total = total + gated * gated
    sq_ref[0] = jnp.sum(total, axis=1, keepdims=True)


def scale_kernel(gated_ref, scale_ref, gain_ref, live_ref, out_ref):
    out_ref[...] = (
        gated_ref[...] * scale_ref[...] * gain_ref[...] * live_ref[...]
    ).astype(jnp.bfloat16)


def scaled_output(gated, scale, gain, live):
    rows, channels = gated.shape
    tile = 128
    return pl.pallas_call(
        scale_kernel,
        grid=(rows // tile,),
        in_specs=[
            pl.BlockSpec((tile, channels), lambda r: (r, 0)),
            pl.BlockSpec((tile, 1), lambda r: (r, 0)),
            pl.BlockSpec((1, channels), lambda r: (0, 0)),
            pl.BlockSpec((tile, 1), lambda r: (r, 0)),
        ],
        out_specs=pl.BlockSpec((tile, channels), lambda r: (r, 0)),
        out_shape=jax.ShapeDtypeStruct((rows, channels), jnp.bfloat16),
        compiler_params=pltpu.CompilerParams(vmem_limit_bytes=48 * 1024 * 1024),
        cost_estimate=pl.CostEstimate(
            flops=3 * rows * channels, bytes_accessed=6 * rows * channels, transcendentals=0
        ),
    )(gated, scale[:, None], gain[None, :], live[:, None])


def by_group(values, spans, heads):
    return values.reshape(spans, heads // HEAD_GROUP, HEAD_GROUP, -1)


def columns_by_group(values, spans, heads):
    return by_group(values, spans, heads).transpose(0, 1, 3, 2)


def block_states(xin, halo, conv_x, b_t, to_end, spans, heads, width, offset):
    rows = xin.shape[0]
    size = b_t.shape[1]
    group = HEAD_GROUP
    lead = halo.shape[1]
    kernel_taps = conv_x.shape[0]
    return pl.pallas_call(
        state_kernel,
        grid=(spans, heads // group),
        in_specs=[
            pl.BlockSpec((SEGMENT_LENGTH, group * width), lambda c, g: (c, g + offset)),
            pl.BlockSpec((1, lead, group * width), lambda c, g: (c, 0, g + offset)),
            pl.BlockSpec((kernel_taps, group * width), lambda c, g: (0, g + offset)),
            pl.BlockSpec((1, size, SEGMENT_LENGTH), lambda c, g: (c, 0, 0)),
            pl.BlockSpec((1, 1, SEGMENT_LENGTH, group), lambda c, g: (c, g, 0, 0)),
        ],
        out_specs=[
            pl.BlockSpec((1, group, size, width), lambda c, g: (c, g, 0, 0)),
            pl.BlockSpec((SEGMENT_LENGTH, group * width), lambda c, g: (c, g)),
        ],
        out_shape=[
            jax.ShapeDtypeStruct((spans, heads, size, width), jnp.float32),
            jax.ShapeDtypeStruct((rows, heads * width), jnp.bfloat16),
        ],
        cost_estimate=pl.CostEstimate(
            flops=2 * rows * heads * width * size,
            bytes_accessed=rows * heads * width * 4 + spans * heads * size * width * 4,
            transcendentals=rows * heads * width,
        ),
    )(xin, halo, conv_x, b_t, columns_by_group(to_end, spans, heads))


def intra_terms(skip_gain, c_part, b_part, xconv, cum_heads, step_heads, spans, heads, width):
    rows = xconv.shape[0]
    size = c_part.shape[1]
    group = HEAD_GROUP
    return pl.pallas_call(
        intra_kernel,
        grid=(spans, heads // group),
        in_specs=[
            pl.BlockSpec(memory_space=pltpu.SMEM),
            pl.BlockSpec((SEGMENT_LENGTH, size), lambda c, g: (c, 0)),
            pl.BlockSpec((SEGMENT_LENGTH, size), lambda c, g: (c, 0)),
            pl.BlockSpec((SEGMENT_LENGTH, group * width), lambda c, g: (c, g)),
            pl.BlockSpec((1, 1, SEGMENT_LENGTH, group), lambda c, g: (c, g, 0, 0)),
            pl.BlockSpec((1, 1, group, SEGMENT_LENGTH), lambda c, g: (c, g, 0, 0)),
            pl.BlockSpec((1, 1, group, SEGMENT_LENGTH), lambda c, g: (c, g, 0, 0)),
        ],
        out_specs=pl.BlockSpec((SEGMENT_LENGTH, group * width), lambda c, g: (c, g)),
        out_shape=jax.ShapeDtypeStruct((rows, heads * width), jnp.float32),
        cost_estimate=pl.CostEstimate(
            flops=2 * rows * SEGMENT_LENGTH * (heads * width + size),
            bytes_accessed=rows * heads * width * 6,
            transcendentals=rows * SEGMENT_LENGTH * heads,
        ),
    )(
        skip_gain,
        c_part,
        b_part,
        xconv,
        columns_by_group(cum_heads, spans, heads),
        by_group(cum_heads, spans, heads),
        by_group(step_heads, spans, heads),
    )


def gate_terms(
    block_decay, partial, c_part, block_state, group_state, ecum, gate_in, spans, heads, width, offset
):
    rows = partial.shape[0]
    size = c_part.shape[1]
    group = HEAD_GROUP
    groups = heads // group
    return pl.pallas_call(
        gate_kernel,
        grid=(groups, spans),
        in_specs=[
            pl.BlockSpec(memory_space=pltpu.SMEM),
            pl.BlockSpec((SEGMENT_LENGTH, group * width), lambda g, c: (c, g)),
            pl.BlockSpec((SEGMENT_LENGTH, size), lambda g, c: (c, 0)),
            pl.BlockSpec((spans, group, size, width), lambda g, c: (0, g, 0, 0)),
            pl.BlockSpec((group, size, width), lambda g, c: (g, 0, 0)),
            pl.BlockSpec((1, 1, SEGMENT_LENGTH, group), lambda g, c: (c, g, 0, 0)),
            pl.BlockSpec((SEGMENT_LENGTH, group * width), lambda g, c: (c, g + offset)),
        ],
        out_specs=[
            pl.BlockSpec((SEGMENT_LENGTH, group * width), lambda g, c: (c, g)),
            pl.BlockSpec((1, SEGMENT_LENGTH, 1), lambda g, c: (g, c, 0)),
        ],
        out_shape=[
            jax.ShapeDtypeStruct((rows, heads * width), jnp.float32),
            jax.ShapeDtypeStruct((groups, rows, 1), jnp.float32),
        ],
        compiler_params=pltpu.CompilerParams(vmem_limit_bytes=48 * 1024 * 1024),
        cost_estimate=pl.CostEstimate(
            flops=6 * rows * size * heads * width,
            bytes_accessed=rows * heads * width * 10,
            transcendentals=rows * heads * width,
        ),
    )(
        block_decay.reshape(-1),
        partial,
        c_part,
        block_state,
        group_state,
        columns_by_group(ecum, spans, heads),
        gate_in,
    )


def local(
    xin,
    gate_in,
    bc_proj,
    dt_raw,
    dt_bias,
    rate,
    skip_gain,
    conv_x,
    conv_bc,
    norm_gain,
    valid_blocks,
):
    row_count, channels = xin.shape
    head_count = dt_raw.shape[1]
    head_size = channels // head_count
    span_count = row_count // SEGMENT_LENGTH
    kernel_taps = conv_x.shape[0]
    live_rows = valid_blocks[0] * BLOCK
    tail_x = lax.dynamic_slice_in_dim(xin, live_rows - (kernel_taps - 1), kernel_taps - 1, 0)
    tail_bc = lax.dynamic_slice_in_dim(bc_proj, live_rows - (kernel_taps - 1), kernel_taps - 1, 0)
    prev = passed_along(jnp.concatenate([tail_x, tail_bc], axis=1), "seq", 1)
    prev_x, prev_bc = prev[:, :channels], prev[:, channels:]
    lead = 8
    edges = jnp.concatenate(
        [prev_x[None], xin.reshape(span_count, SEGMENT_LENGTH, channels)[:-1, -(kernel_taps - 1) :]],
        axis=0,
    )
    halo = jnp.pad(edges, ((0, 0), (lead - (kernel_taps - 1), 0), (0, 0)))
    bc_local = conv_silu(bc_proj, prev_bc, conv_bc)
    bc_full = lax.all_gather(bc_local, "ch", axis=1, tiled=True)
    state_size = bc_full.shape[1] // 2
    b_part = bc_full[:, :state_size]
    c_part = bc_full[:, state_size:]
    b_t = b_part.reshape(span_count, SEGMENT_LENGTH, state_size).transpose(0, 2, 1)
    row_valid = (jnp.arange(row_count) < live_rows).astype(jnp.float32)
    step_size = jax.nn.softplus(dt_raw + dt_bias[None, :]) * row_valid[:, None]
    step_three = step_size.reshape(span_count, SEGMENT_LENGTH, head_count)
    cumul = jnp.cumsum(-rate[None, None, :] * step_three, axis=1)
    cum_heads = jnp.transpose(cumul, (0, 2, 1))
    step_heads = jnp.transpose(step_three, (0, 2, 1))
    last_cum = cum_heads[:, :, -1]
    to_end = jnp.exp(last_cum[:, :, None] - cum_heads) * step_heads
    block_decay = jnp.exp(last_cum)
    halves = 1
    part_heads = head_count // halves
    gated_parts = []
    square_part = None
    for part in range(halves):
        heads = slice(part * part_heads, (part + 1) * part_heads)
        offset = part * part_heads // HEAD_GROUP
        block_state, xconv = block_states(
            xin, halo, conv_x, b_t, to_end[:, heads], span_count, part_heads, head_size, offset
        )
        current = jnp.zeros((part_heads, state_size, head_size), jnp.float32)
        factor = jnp.ones((part_heads,), jnp.float32)
        local_enter = []
        factor_list = []
        for index in range(span_count):
            local_enter.append(current)
            factor_list.append(factor)
            current = block_decay[index, heads][:, None, None] * current + block_state[index]
            factor = factor * block_decay[index, heads]
        group_state, xconv = scan_states(factor, current, "seq", xconv)
        partial = intra_terms(
            skip_gain[heads],
            c_part,
            b_part,
            xconv,
            cum_heads[:, heads],
            step_heads[:, heads],
            span_count,
            part_heads,
            head_size,
        )
        gated, squares = gate_terms(
            block_decay[:, heads],
            partial,
            c_part,
            block_state,
            group_state,
            jnp.exp(cum_heads[:, heads]),
            gate_in,
            span_count,
            part_heads,
            head_size,
            offset,
        )
        squares = jnp.sum(squares, axis=0)
        gated_parts.append(gated)
        square_part = squares if square_part is None else square_part + squares
    gated = jnp.concatenate(gated_parts, axis=1)
    square_sum = lax.psum(square_part[:, 0], "ch")
    mean_sq = square_sum / INNER
    return scaled_output(gated, lax.rsqrt(mean_sq + 1e-05), norm_gain, row_valid)


def solution(mesh):
    placed = (
        P("seq", "ch"),
        P("seq", "ch"),
        P("seq", "ch"),
        P("seq", "ch"),
        P("ch"),
        P("ch"),
        P("ch"),
        P(None, "ch"),
        P(None, "ch"),
        P("ch"),
        P("seq"),
    )
    return jax.shard_map(
        local, mesh=mesh, in_specs=placed, out_specs=P("seq", "ch"), check_vma=False
    )
```

```python
import functools

import jax
import jax.numpy as jnp
from jax import lax
from jax.experimental import pallas as pl
from jax.experimental.pallas import tpu as pltpu
from jax.sharding import PartitionSpec as P

SEGMENT_LENGTH = 256
BLOCK = 128
INNER = 16384


def passed_along(block, axis, distance):
    devices = range(lax.axis_size(axis))
    route = [(i - distance, i) for i in devices if i - distance in devices]
    return lax.ppermute(block, axis, route)


def scan_states(factor, state, axis, tied):
    count = lax.axis_size(axis)
    split = count % 2 == 0 and count >= 4
    members = count // 2 if split else count
    groups = [list(range(0, members)), list(range(members, count))] if split else None
    heads, size, width = state.shape
    piece = size // members
    parts = state.reshape(heads, members, piece, width).transpose(1, 0, 2, 3)
    slot = jnp.zeros((piece, width), jnp.float32).at[0, :heads].set(factor)
    payload = jnp.concatenate(
        [parts, jnp.broadcast_to(slot, (members, 1, piece, width))], axis=1
    )
    got = lax.all_to_all(payload, axis, 0, 0, tiled=True, axis_index_groups=groups)
    decays = got[:, heads, 0, :heads]
    tied = lax.optimization_barrier((tied, got))[0]
    running = jnp.zeros((heads, piece, width), jnp.float32)
    entries = []
    for index in range(members):
        entries.append(running)
        running = decays[index][:, None, None] * running + got[index, :heads]
    if split:
        route = [(i, i + members) for i in range(members)]
        earlier = lax.ppermute(running, axis, route)
        carry = jnp.ones((heads,), jnp.float32)
        for index in range(members):
            entries[index] = entries[index] + carry[:, None, None] * earlier
            carry = carry * decays[index]
    back = lax.all_to_all(
        jnp.stack(entries, axis=0), axis, 0, 0, tiled=True, axis_index_groups=groups
    )
    return back.transpose(1, 0, 2, 3).reshape(heads, size, width), tied


def conv_silu(signal, tail_rows, weights):
    stacked = jnp.concatenate([tail_rows, signal], axis=0)
    kernel_taps = weights.shape[0]
    length = signal.shape[0]
    accum = jnp.zeros(signal.shape, jnp.float32)
    for offset in range(kernel_taps):
        accum = accum + weights[offset].astype(jnp.float32) * stacked[
            offset : offset + length
        ].astype(jnp.float32)
    return jax.nn.silu(accum).astype(jnp.bfloat16)


HEAD_GROUP = 16


def silu(value):
    half = 0.5 * value
    return half + half * jnp.tanh(half)


def state_kernel(x_ref, halo_ref, taps_ref, bt_ref, toend_ref, out_ref, conv_ref):
    width = out_ref.shape[-1]
    taps = taps_ref[...].astype(jnp.float32)
    kernel_taps = taps.shape[0]
    signal = x_ref[...].astype(jnp.float32)
    edge = halo_ref[0].astype(jnp.float32)
    lead = edge.shape[0]
    stacked = jnp.concatenate([edge, signal[:lead]], axis=0)
    accum = jnp.zeros(signal.shape, jnp.float32)
    head = jnp.zeros((lead, signal.shape[1]), jnp.float32)
    for offset in range(kernel_taps):
        shift = kernel_taps - 1 - offset
        moved = signal if shift == 0 else pltpu.roll(signal, shift, 0)
        accum = accum + taps[offset : offset + 1] * moved
        head = head + taps[offset : offset + 1] * stacked[lead - shift : 2 * lead - shift]
    conv_ref[...] = silu(accum).astype(jnp.bfloat16)
    conv_ref[:lead, :] = silu(head).astype(jnp.bfloat16)
    bt = bt_ref[0]
    for j in range(out_ref.shape[1]):
        x = conv_ref[:, j * width : (j + 1) * width].astype(jnp.float32)
        xw = (x * toend_ref[0, 0, :, j : j + 1]).astype(jnp.bfloat16)
        out_ref[0, j] = jnp.dot(bt, xw, preferred_element_type=jnp.float32)


def intra_kernel(skip_ref, c_ref, b_ref, x_ref, cumc_ref, cumr_ref, stepr_ref, out_ref):
    group = pl.program_id(1)
    heads = cumc_ref.shape[-1]
    width = out_ref.shape[-1] // heads
    scores = lax.dot_general(
        c_ref[...], b_ref[...], (((1,), (1,)), ((), ())), preferred_element_type=jnp.float32
    )
    length = scores.shape[0]
    rows = lax.broadcasted_iota(jnp.int32, (length, length), 0)
    cols = lax.broadcasted_iota(jnp.int32, (length, length), 1)
    causal = rows >= cols
    for j in range(heads):
        diff = cumc_ref[0, 0, :, j : j + 1] - cumr_ref[0, 0, j : j + 1, :]
        decay = jnp.where(causal, jnp.exp(jnp.where(causal, diff, 0.0)), 0.0)
        weights = (scores * decay * stepr_ref[0, 0, j : j + 1, :]).astype(jnp.bfloat16)
        x = x_ref[:, j * width : (j + 1) * width]
        intra = jnp.dot(weights, x, preferred_element_type=jnp.float32)
        out_ref[:, j * width : (j + 1) * width] = (
            intra + skip_ref[group * heads + j] * x.astype(jnp.float32)
        )


def gate_kernel(decay_ref, part_ref, c_ref, block_ref, group_ref, ecum_ref, z_ref, out_ref, sq_ref):
    group = pl.program_id(0)
    span = pl.program_id(1)
    spans = block_ref.shape[0]
    heads = ecum_ref.shape[-1]
    head_count = decay_ref.shape[0] // spans
    width = out_ref.shape[-1] // heads
    c = c_ref[...]
    total = jnp.zeros((c.shape[0], width), jnp.float32)
    for j in range(heads):
        head = group * heads + j
        local_state = jnp.zeros(block_ref.shape[2:], jnp.float32)
        factor = jnp.float32(1.0)
        for earlier in range(spans - 1):
            decay = decay_ref[earlier * head_count + head]
            take = earlier < span
            local_state = jnp.where(
                take, decay * local_state + block_ref[earlier, j], local_state
            )
            factor = jnp.where(take, factor * decay, factor)
        state = local_state + factor * group_ref[j]
        high = state.astype(jnp.bfloat16)
        low = (state - high.astype(jnp.float32)).astype(jnp.bfloat16)
        inter = jnp.dot(c, high, preferred_element_type=jnp.float32) + jnp.dot(
            c, low, preferred_element_type=jnp.float32
        )
        columns = slice(j * width, (j + 1) * width)
        y = part_ref[:, columns] + inter * ecum_ref[0, 0, :, j : j + 1]
        z = z_ref[:, columns].astype(jnp.float32)
        gated = y * silu(z)
        out_ref[:, columns] = gated
        total = total + gated * gated
    sq_ref[0] = jnp.sum(total, axis=1, keepdims=True)


def by_group(values, spans, heads):
    return values.reshape(spans, heads // HEAD_GROUP, HEAD_GROUP, -1)


def columns_by_group(values, spans, heads):
    return by_group(values, spans, heads).transpose(0, 1, 3, 2)


def block_states(xin, halo, conv_x, b_t, to_end, spans, heads, width, offset):
    rows = xin.shape[0]
    size = b_t.shape[1]
    group = HEAD_GROUP
    lead = halo.shape[1]
    kernel_taps = conv_x.shape[0]
    return pl.pallas_call(
        state_kernel,
        grid=(spans, heads // group),
        in_specs=[
            pl.BlockSpec((SEGMENT_LENGTH, group * width), lambda c, g: (c, g + offset)),
            pl.BlockSpec((1, lead, group * width), lambda c, g: (c, 0, g + offset)),
            pl.BlockSpec((kernel_taps, group * width), lambda c, g: (0, g + offset)),
            pl.BlockSpec((1, size, SEGMENT_LENGTH), lambda c, g: (c, 0, 0)),
            pl.BlockSpec((1, 1, SEGMENT_LENGTH, group), lambda c, g: (c, g, 0, 0)),
        ],
        out_specs=[
            pl.BlockSpec((1, group, size, width), lambda c, g: (c, g, 0, 0)),
            pl.BlockSpec((SEGMENT_LENGTH, group * width), lambda c, g: (c, g)),
        ],
        out_shape=[
            jax.ShapeDtypeStruct((spans, heads, size, width), jnp.float32),
            jax.ShapeDtypeStruct((rows, heads * width), jnp.bfloat16),
        ],
        cost_estimate=pl.CostEstimate(
            flops=2 * rows * heads * width * size,
            bytes_accessed=rows * heads * width * 4 + spans * heads * size * width * 4,
            transcendentals=rows * heads * width,
        ),
    )(xin, halo, conv_x, b_t, columns_by_group(to_end, spans, heads))


def intra_terms(skip_gain, c_part, b_part, xconv, cum_heads, step_heads, spans, heads, width):
    rows = xconv.shape[0]
    size = c_part.shape[1]
    group = HEAD_GROUP
    return pl.pallas_call(
        intra_kernel,
        grid=(spans, heads // group),
        in_specs=[
            pl.BlockSpec(memory_space=pltpu.SMEM),
            pl.BlockSpec((SEGMENT_LENGTH, size), lambda c, g: (c, 0)),
            pl.BlockSpec((SEGMENT_LENGTH, size), lambda c, g: (c, 0)),
            pl.BlockSpec((SEGMENT_LENGTH, group * width), lambda c, g: (c, g)),
            pl.BlockSpec((1, 1, SEGMENT_LENGTH, group), lambda c, g: (c, g, 0, 0)),
            pl.BlockSpec((1, 1, group, SEGMENT_LENGTH), lambda c, g: (c, g, 0, 0)),
            pl.BlockSpec((1, 1, group, SEGMENT_LENGTH), lambda c, g: (c, g, 0, 0)),
        ],
        out_specs=pl.BlockSpec((SEGMENT_LENGTH, group * width), lambda c, g: (c, g)),
        out_shape=jax.ShapeDtypeStruct((rows, heads * width), jnp.float32),
        cost_estimate=pl.CostEstimate(
            flops=2 * rows * SEGMENT_LENGTH * (heads * width + size),
            bytes_accessed=rows * heads * width * 6,
            transcendentals=rows * SEGMENT_LENGTH * heads,
        ),
    )(
        skip_gain,
        c_part,
        b_part,
        xconv,
        columns_by_group(cum_heads, spans, heads),
        by_group(cum_heads, spans, heads),
        by_group(step_heads, spans, heads),
    )


def gate_terms(
    block_decay, partial, c_part, block_state, group_state, ecum, gate_in, spans, heads, width, offset
):
    rows = partial.shape[0]
    size = c_part.shape[1]
    group = HEAD_GROUP
    groups = heads // group
    return pl.pallas_call(
        gate_kernel,
        grid=(groups, spans),
        in_specs=[
            pl.BlockSpec(memory_space=pltpu.SMEM),
            pl.BlockSpec((SEGMENT_LENGTH, group * width), lambda g, c: (c, g)),
            pl.BlockSpec((SEGMENT_LENGTH, size), lambda g, c: (c, 0)),
            pl.BlockSpec((spans, group, size, width), lambda g, c: (0, g, 0, 0)),
            pl.BlockSpec((group, size, width), lambda g, c: (g, 0, 0)),
            pl.BlockSpec((1, 1, SEGMENT_LENGTH, group), lambda g, c: (c, g, 0, 0)),
            pl.BlockSpec((SEGMENT_LENGTH, group * width), lambda g, c: (c, g + offset)),
        ],
        out_specs=[
            pl.BlockSpec((SEGMENT_LENGTH, group * width), lambda g, c: (c, g)),
            pl.BlockSpec((1, SEGMENT_LENGTH, 1), lambda g, c: (g, c, 0)),
        ],
        out_shape=[
            jax.ShapeDtypeStruct((rows, heads * width), jnp.float32),
            jax.ShapeDtypeStruct((groups, rows, 1), jnp.float32),
        ],
        compiler_params=pltpu.CompilerParams(vmem_limit_bytes=48 * 1024 * 1024),
        cost_estimate=pl.CostEstimate(
            flops=6 * rows * size * heads * width,
            bytes_accessed=rows * heads * width * 10,
            transcendentals=rows * heads * width,
        ),
    )(
        block_decay.reshape(-1),
        partial,
        c_part,
        block_state,
        group_state,
        columns_by_group(ecum, spans, heads),
        gate_in,
    )


def local(
    xin,
    gate_in,
    bc_proj,
    dt_raw,
    dt_bias,
    rate,
    skip_gain,
    conv_x,
    conv_bc,
    norm_gain,
    valid_blocks,
):
    row_count, channels = xin.shape
    head_count = dt_raw.shape[1]
    head_size = channels // head_count
    span_count = row_count // SEGMENT_LENGTH
    kernel_taps = conv_x.shape[0]
    live_rows = valid_blocks[0] * BLOCK
    tail_x = lax.dynamic_slice_in_dim(xin, live_rows - (kernel_taps - 1), kernel_taps - 1, 0)
    tail_bc = lax.dynamic_slice_in_dim(bc_proj, live_rows - (kernel_taps - 1), kernel_taps - 1, 0)
    prev = passed_along(jnp.concatenate([tail_x, tail_bc], axis=1), "seq", 1)
    prev_x, prev_bc = prev[:, :channels], prev[:, channels:]
    lead = 8
    edges = jnp.concatenate(
        [prev_x[None], xin.reshape(span_count, SEGMENT_LENGTH, channels)[:-1, -(kernel_taps - 1) :]],
        axis=0,
    )
    halo = jnp.pad(edges, ((0, 0), (lead - (kernel_taps - 1), 0), (0, 0)))
    bc_local = conv_silu(bc_proj, prev_bc, conv_bc)
    bc_full = lax.all_gather(bc_local, "ch", axis=1, tiled=True)
    state_size = bc_full.shape[1] // 2
    b_part = bc_full[:, :state_size]
    c_part = bc_full[:, state_size:]
    b_t = b_part.reshape(span_count, SEGMENT_LENGTH, state_size).transpose(0, 2, 1)
    row_valid = (jnp.arange(row_count) < live_rows).astype(jnp.float32)
    step_size = jax.nn.softplus(dt_raw + dt_bias[None, :]) * row_valid[:, None]
    step_three = step_size.reshape(span_count, SEGMENT_LENGTH, head_count)
    cumul = jnp.cumsum(-rate[None, None, :] * step_three, axis=1)
    cum_heads = jnp.transpose(cumul, (0, 2, 1))
    step_heads = jnp.transpose(step_three, (0, 2, 1))
    last_cum = cum_heads[:, :, -1]
    to_end = jnp.exp(last_cum[:, :, None] - cum_heads) * step_heads
    block_decay = jnp.exp(last_cum)
    halves = 1
    part_heads = head_count // halves
    gated_parts = []
    square_part = None
    for part in range(halves):
        heads = slice(part * part_heads, (part + 1) * part_heads)
        offset = part * part_heads // HEAD_GROUP
        block_state, xconv = block_states(
            xin, halo, conv_x, b_t, to_end[:, heads], span_count, part_heads, head_size, offset
        )
        current = jnp.zeros((part_heads, state_size, head_size), jnp.float32)
        factor = jnp.ones((part_heads,), jnp.float32)
        local_enter = []
        factor_list = []
        for index in range(span_count):
            local_enter.append(current)
            factor_list.append(factor)
            current = block_decay[index, heads][:, None, None] * current + block_state[index]
            factor = factor * block_decay[index, heads]
        group_state, xconv = scan_states(factor, current, "seq", xconv)
        partial = intra_terms(
            skip_gain[heads],
            c_part,
            b_part,
            xconv,
            cum_heads[:, heads],
            step_heads[:, heads],
            span_count,
            part_heads,
            head_size,
        )
        gated, squares = gate_terms(
            block_decay[:, heads],
            partial,
            c_part,
            block_state,
            group_state,
            jnp.exp(cum_heads[:, heads]),
            gate_in,
            span_count,
            part_heads,
            head_size,
            offset,
        )
        squares = jnp.sum(squares, axis=0)
        gated_parts.append(gated)
        square_part = squares if square_part is None else square_part + squares
    gated = jnp.concatenate(gated_parts, axis=1)
    square_sum = lax.psum(square_part[:, 0], "ch")
    mean_sq = square_sum / INNER
    normed = gated * lax.rsqrt(mean_sq + 1e-05)[:, None] * norm_gain[None, :] * row_valid[:, None]
    return normed.astype(jnp.bfloat16)


def solution(mesh):
    placed = (
        P("seq", "ch"),
        P("seq", "ch"),
        P("seq", "ch"),
        P("seq", "ch"),
        P("ch"),
        P("ch"),
        P("ch"),
        P(None, "ch"),
        P(None, "ch"),
        P("ch"),
        P("seq"),
    )
    return jax.shard_map(
        local, mesh=mesh, in_specs=placed, out_specs=P("seq", "ch"), check_vma=False
    )
```
